32 devices in a mesh: rep: 8 (over z, x), shard: 4 (over y, core).
Axes of the slice: x: 2, y: 2, z: 4, core: 2. Of those that a mesh axis runs over, the one named last changes fastest.
Arguments:
- tokens: bfloat16 [32, 384, 1024], P(('rep', 'shard')), may hold values from -6 to 6
- cont_segment: int32 [32, 2, 64], P(('rep', 'shard')), may hold values from 0 to 1, as said below
- cotangent: bfloat16 [32, 384, 1024], P(('rep', 'shard')), may hold values from -6 to 6
- ln1_gain: bfloat16 [1024], P('shard'), may hold values from 0.099609375 to 1.8984375
- ln1_bias: bfloat16 [1024], P('shard'), may hold values from -3 to 3
- w_qkv: bfloat16 [1024, 3072], P(None, 'shard'), may hold values from -0.1875 to 0.1875
- q_bias: bfloat16 [1024], P('shard'), may hold values from -3 to 3
- v_bias: bfloat16 [1024], P('shard'), may hold values from -3 to 3
- w_out: bfloat16 [1024, 1024], P('shard'), may hold values from -0.75 to 0.75
- b_out: bfloat16 [1024], P('shard'), may hold values from -3 to 3
- ln2_gain: bfloat16 [1024], P('shard'), may hold values from 0.099609375 to 1.8984375
- ln2_bias: bfloat16 [1024], P('shard'), may hold values from -3 to 3
- w_up: bfloat16 [1024, 4096], P(None, 'shard'), may hold values from -0.1875 to 0.1875
- b_up: bfloat16 [4096], P('shard'), may hold values from -3 to 3
- w_down: bfloat16 [4096, 1024], P('shard'), may hold values from -0.125 to 0.125
- b_down: bfloat16 [1024], P('shard'), may hold values from -3 to 3
Outputs:
- layer_out: bfloat16 [32, 384, 1024], P(('rep', 'shard'))
- grad_tokens: bfloat16 [32, 384, 1024], P(('rep', 'shard'))
- grad_ln1_gain: float32 [1024], P('shard')
- grad_ln1_bias: float32 [1024], P('shard')
- grad_w_qkv: float32 [1024, 3072], P(None, 'shard')
- grad_q_bias: float32 [1024], P('shard')
- grad_v_bias: float32 [1024], P('shard')
- grad_w_out: float32 [1024, 1024], P('shard')
- grad_b_out: float32 [1024], P('shard')
- grad_ln2_gain: float32 [1024], P('shard')
- grad_ln2_bias: float32 [1024], P('shard')
- grad_w_up: float32 [1024, 4096], P(None, 'shard')
- grad_b_up: float32 [4096], P('shard')
- grad_w_down: float32 [4096, 1024], P('shard')
- grad_b_down: float32 [1024], P('shard')
The draws below stay inside these ranges and needn't reach their ends.
Inputs may be any that keep to these rules, and one draw needn't show every extreme that they name: `cont_segment`: each micro-batch holds 2 continuations, numbers never falling, each of 16 to 48 rows; in the first micro-batch of every prompt one continuation has exactly 48 rows.
All inputs are finite; a program needn't handle non-finite values.
Results may differ from the reference program's by a relative error of at most 0.015.
Values may be sent and summed in bfloat16 or wider, within the bound.
No kernel may reach another device: no remote copies, remote signals or barrier semaphores. Data moves between devices by JAX's collectives and lax.ppermute only.
A program may use at most 256 MiB of HBM per device.

```python
import jax
import jax.numpy as jnp
from jax import lax

D = 1024
HEADS = 16
HDIM = 64
FF = 4096
PROMPT = 256
ROWS = 64
MICRO = 2
MOSTLEN = 48
SEQ = 384
PROMPTS = 32


def draw_cont_segment(key, part):
    key_cut = jax.random.fold_in(key, 11)
    key_flip = jax.random.fold_in(key, 23)
    cuts = jax.random.randint(key_cut, (PROMPTS, MICRO), ROWS - MOSTLEN, MOSTLEN + 1).astype(jnp.int32)
    flips = jax.random.randint(key_flip, (PROMPTS,), 0, 2).astype(jnp.int32)
    first_cut = jnp.where(flips == 1, MOSTLEN, ROWS - MOSTLEN).astype(jnp.int32)
    cuts = cuts.at[:, 0].set(first_cut)
    places = jnp.arange(ROWS, dtype=jnp.int32)
    return (places[None, None, :] >= cuts[:, :, None]).astype(jnp.int32)


def strengthened(values, key, source, target, parts, factor):
    def block_of(position):
        return (jnp.arange(values.shape[position]) // (values.shape[position] // parts)).reshape((-1,) + (1,) * (values.ndim - 1 - position))

    near = jax.random.permutation(key, parts)[block_of(target)]
    other_side = (block_of(target) + parts // 2) % parts
    return jnp.where((block_of(source) == near) | (block_of(source) == other_side), factor * values, values)


def block_scale(rng, extent, cuts, least, high):
    loudness = 1.0
    for position, shards_of in cuts:
        steps = jax.random.uniform(jax.random.fold_in(jax.random.fold_in(rng, 6), position), (shards_of,), jnp.float32, least / len(cuts), high / len(cuts))
        loudness = loudness * jnp.repeat(jnp.exp(steps), extent[position] // shards_of).reshape((-1,) + (1,) * (len(extent) - 1 - position))
    return loudness


def noise(key, dims, scale, limit, pieces=(), kind=jnp.bfloat16):
    loudness = block_scale(key, dims, pieces, -0.22, 0.18) if pieces else 1.0
    values = jax.random.normal(key, dims, jnp.float32) * scale * loudness
    return jnp.minimum(jnp.maximum(values, -limit), limit).astype(kind)


def gaussian_with(key, dims, width, reach, cuts, heavy, kind=jnp.bfloat16):
    values = width * jax.random.normal(key, dims, jnp.float32)
    if cuts:
        values = values * block_scale(key, dims, cuts, -0.22, 0.18)
    return jnp.clip(strengthened(values, jax.random.fold_in(key, 3), *heavy), -reach, reach).astype(kind)


def setup_inputs(seed: int = 0) -> dict:
    key_list = jax.random.split(jax.random.key(seed), 17)
    tokens = noise(key_list[0], (PROMPTS, SEQ, D), 1.0, 6.0, ((0, 32),))
    cont_segment = draw_cont_segment(jax.random.fold_in(key_list[16], 71), 0)
    cotangent = gaussian_with(key_list[2], (PROMPTS, SEQ, D), 1.0, 6.0, ((0, 32),), (0, 2, 32, 2.75))
    ln1_gain = jnp.clip(1.0 + 0.18 * jax.random.normal(key_list[3], (D,), jnp.float32), 0.099609375, 1.8984375).astype(jnp.bfloat16)
    ln1_bias = noise(key_list[4], (D,), 0.5, 3.0, ((0, 4),))
    w_qkv = noise(key_list[5], (D, 3 * D), D ** -0.5, 0.1875, ((1, 4),))
    q_bias = noise(key_list[6], (D,), 0.5, 3.0, ((0, 4),))
    v_bias = noise(key_list[7], (D,), 0.5, 3.0, ((0, 4),))
    w_out = noise(key_list[8], (D, D), (D // 16) ** -0.5, 0.75, ((0, 4),))
    b_out = noise(key_list[9], (D,), 0.5, 3.0, ((0, 4),))
    ln2_gain = jnp.clip(1.0 + 0.18 * jax.random.normal(key_list[10], (D,), jnp.float32), 0.099609375, 1.8984375).astype(jnp.bfloat16)
    ln2_bias = noise(key_list[11], (D,), 0.5, 3.0, ((0, 4),))
    w_up = noise(key_list[12], (D, FF), D ** -0.5, 0.1875, ((1, 4),))
    b_up = noise(key_list[13], (FF,), 0.5, 3.0, ((0, 4),))
    w_down = noise(key_list[14], (FF, D), (FF // 2) ** -0.5, 0.125, ((0, 4),))
    b_down = noise(key_list[15], (D,), 0.5, 3.0, ((0, 4),))
    return dict(tokens=tokens, cont_segment=cont_segment, cotangent=cotangent, ln1_gain=ln1_gain, ln1_bias=ln1_bias, w_qkv=w_qkv, q_bias=q_bias, v_bias=v_bias, w_out=w_out, b_out=b_out, ln2_gain=ln2_gain, ln2_bias=ln2_bias, w_up=w_up, b_up=b_up, w_down=w_down, b_down=b_down)


@jax.custom_vjp
def low(v):
    return lax.optimization_barrier(v.astype(jnp.bfloat16)).astype(jnp.float32)

@jax.custom_vjp
def low_back(v):
    return v

def low_keep(v):
    return (low(v), None)

def low_pass(kept, grad):
    return (grad,)

def back_keep(v):
    return (v, None)

def back_low(kept, grad):
    return (low(grad),)
low.defvjp(low_keep, low_pass)
low_back.defvjp(back_keep, back_low)
precise = lax.Precision.HIGHEST

def both_round(value_in):
    return low(low_back(value_in))

def normalize(values, gain, shift):
    center = values - lax.optimization_barrier(jnp.mean(values, -1, keepdims=True))
    spread = lax.optimization_barrier(jnp.mean(center * center, -1, keepdims=True))
    return center * lax.rsqrt(spread + 1e-05) * gain + shift

def layout(segments):
    micros, row_count = segments.shape
    same_seg = segments[:, :, None] == segments[:, None, :]
    earlier = jnp.arange(row_count)[None, :] < jnp.arange(row_count)[:, None]
    offsets = lax.optimization_barrier(jnp.sum(jnp.where(same_seg & earlier[None], 1, 0), -1)).astype(jnp.int32)
    cont_pos = (PROMPT + offsets).astype(jnp.int32)
    owners = (jnp.arange(micros, dtype=jnp.int32)[:, None] * row_count + segments).astype(jnp.int32)
    positions = jnp.concatenate([jnp.arange(PROMPT, dtype=jnp.int32), cont_pos.reshape(-1)])
    groups = jnp.concatenate([jnp.full((PROMPT,), -1, jnp.int32), owners.reshape(-1)])
    places = jnp.arange(positions.shape[0], dtype=jnp.int32)
    allowed = (places[None, :] <= places[:, None]) & ((places[None, :] < PROMPT) | (groups[None, :] == groups[:, None]))
    distance = (positions[:, None] - positions[None, :]).astype(jnp.float32)
    return (distance, allowed)

def attention(queries, key_rows, values, distance, allowed):
    length = queries.shape[0]
    block_width = 4 * HDIM

    def head_block(block):
        q_part = lax.dynamic_slice_in_dim(queries, block * block_width, block_width, 1).reshape(length, 4, HDIM)
        k_part = lax.dynamic_slice_in_dim(key_rows, block * block_width, block_width, 1).reshape(length, 4, HDIM)
        v_part = lax.dynamic_slice_in_dim(values, block * block_width, block_width, 1).reshape(length, 4, HDIM)
        heads = (block * 4 + jnp.arange(4, dtype=jnp.int32)).astype(jnp.float32)
        slopes = jnp.exp2(-8.0 * (heads + 1.0) / HEADS)
        scores = jnp.einsum('qhd,khd->hqk', q_part, k_part, precision=precise) * HDIM ** (-0.5) - slopes[:, None, None] * distance[None]
        scores = jnp.where(allowed[None], low_back(scores), -jnp.inf)
        attn_probs = low(jax.nn.softmax(scores, axis=-1))
        return jnp.einsum('hqk,khd->qhd', attn_probs, v_part, precision=precise).reshape(length, block_width)
    blocks = lax.map(jax.checkpoint(head_block), jnp.arange(HEADS // 4, dtype=jnp.int32))
    return jnp.transpose(blocks, (1, 0, 2)).reshape(length, HEADS * HDIM)

def forward(params, inputs, distance, allowed):
    gain_one, shift_one, w_proj, bias_q, bias_v, w_mix, bias_mix, gain_two, shift_two, w_raise, bias_raise, w_lower, bias_lower = params
    model_width = inputs.shape[-1]
    normed = low(normalize(inputs, gain_one, shift_one))
    projected = jnp.dot(normed, w_proj, precision=precise)
    queries = both_round(projected[:, :model_width] + bias_q)
    key_rows = both_round(projected[:, model_width:2 * model_width])
    values = both_round(projected[:, 2 * model_width:] + bias_v)
    mixed = both_round(attention(queries, key_rows, values, distance, allowed))
    branch = low_back(jnp.dot(mixed, w_mix, precision=precise) + bias_mix)
    middle = inputs + branch
    normed_two = low(normalize(middle, gain_two, shift_two))
    pre_act = low_back(jnp.dot(normed_two, w_raise, precision=precise) + bias_raise)
    activated = low(jax.nn.gelu(pre_act, approximate=True))
    return middle + low_back(jnp.dot(activated, w_lower, precision=precise) + bias_lower)

def reference(tokens, cont_segment, cotangent, ln1_gain, ln1_bias, w_qkv, q_bias, v_bias, w_out, b_out, ln2_gain, ln2_bias, w_up, b_up, w_down, b_down):
    params = tuple((weight.astype(jnp.float32) for weight in (ln1_gain, ln1_bias, w_qkv, q_bias, v_bias, w_out, b_out, ln2_gain, ln2_bias, w_up, b_up, w_down, b_down)))
    prompt_count, length, model_width = tokens.shape
    per_step = 4
    steps_total = prompt_count // per_step
    shaped_in = tokens.astype(jnp.float32).reshape(steps_total, per_step, length, model_width)
    shaped_seg = cont_segment.reshape(steps_total, per_step, cont_segment.shape[1], cont_segment.shape[2])
    shaped_cot = cotangent.astype(jnp.float32).reshape(steps_total, per_step, length, model_width)

    def scan_step(totals, scan_item):
        inputs, segments, cotangents = scan_item
        distance, allowed = jax.vmap(layout)(segments)

        def run(weights, values):
            return jax.vmap(forward, in_axes=(None, 0, 0, 0))(weights, values, distance, allowed)
        outputs, pullback = jax.vjp(run, params, inputs)
        grad_params, grad_inputs = pullback(cotangents)
        totals = jax.tree.map(lambda earlier_sum, addend: earlier_sum + addend, totals, grad_params)
        return (totals, (outputs.astype(jnp.bfloat16), grad_inputs.astype(jnp.bfloat16)))
    zeros_init = tuple((jnp.zeros_like(weight) for weight in params))
    totals, (outputs, grad_inputs) = lax.scan(scan_step, zeros_init, (shaped_in, shaped_seg, shaped_cot))
    return (outputs.reshape(prompt_count, length, model_width), grad_inputs.reshape(prompt_count, length, model_width), totals[0], totals[1], totals[2], totals[3], totals[4], totals[5], totals[6], totals[7], totals[8], totals[9], totals[10], totals[11], totals[12])
```

```python
from functools import partial

import jax
import jax.numpy as jnp
from jax import lax
from jax.sharding import PartitionSpec as P

HEADS = 16
HDIM = 64
PROMPT = 256


def normalize(values, gain, shift):
    center = values - jnp.mean(values, -1, keepdims=True)
    spread = jnp.mean(center * center, -1, keepdims=True)
    return center * lax.rsqrt(spread + 1e-05) * gain + shift


def layout(segments):
    micros, row_count = segments.shape
    same_seg = segments[:, :, None] == segments[:, None, :]
    earlier = jnp.arange(row_count)[None, :] < jnp.arange(row_count)[:, None]
    offsets = jnp.sum(jnp.where(same_seg & earlier[None], 1, 0), -1).astype(jnp.int32)
    cont_pos = PROMPT + offsets
    owners = jnp.arange(micros, dtype=jnp.int32)[:, None] * row_count + segments
    positions = jnp.concatenate([jnp.arange(PROMPT, dtype=jnp.int32), cont_pos.reshape(-1)])
    groups = jnp.concatenate([jnp.full((PROMPT,), -1, jnp.int32), owners.reshape(-1)])
    places = jnp.arange(positions.shape[0], dtype=jnp.int32)
    allowed = (places[None, :] <= places[:, None]) & (
        (places[None, :] < PROMPT) | (groups[None, :] == groups[:, None])
    )
    distance = (positions[:, None] - positions[None, :]).astype(jnp.float32)
    return (distance, allowed)


def head_slice(matrix, block):
    block_width = 4 * HDIM
    part = lax.dynamic_slice_in_dim(matrix, block * block_width, block_width, 1)
    return part.reshape(matrix.shape[0], 4, HDIM)


def block_scores(q_part, k_part, block, distance, allowed):
    heads = (block * 4 + jnp.arange(4, dtype=jnp.int32)).astype(jnp.float32)
    slopes = jnp.exp2(-8.0 * (heads + 1.0) / HEADS)
    scores = jnp.einsum(
        "qhd,khd->hqk", q_part, k_part, preferred_element_type=jnp.float32
    ) * HDIM ** (-0.5)
    scores = scores - slopes[:, None, None] * distance[None]
    return jnp.where(allowed[None], scores, -jnp.inf)


def side_by_side(blocks):
    return jnp.transpose(blocks, (1, 0, 2)).reshape(
        blocks.shape[1], blocks.shape[0] * blocks.shape[2]
    )


def attend_forward(queries, key_rows, values, distance, allowed):
    length = queries.shape[0]

    def head_block(block):
        q_part = head_slice(queries, block)
        k_part = head_slice(key_rows, block)
        v_part = head_slice(values, block)
        scores = block_scores(q_part, k_part, block, distance, allowed)
        peak = jnp.max(scores, -1, keepdims=True)
        exps_rel = jnp.exp(scores - peak)
        row_totals = jnp.sum(exps_rel, -1, keepdims=True)
        attn_probs = (exps_rel / row_totals).astype(jnp.bfloat16)
        mixed = jnp.einsum("hqk,khd->qhd", attn_probs, v_part, preferred_element_type=jnp.float32)
        return (mixed.reshape(length, 4 * HDIM), (peak + jnp.log(row_totals))[:, :, 0])

    mixed, log_norms = lax.map(head_block, jnp.arange(HEADS // 4, dtype=jnp.int32))
    return (side_by_side(mixed).astype(jnp.bfloat16), log_norms)


def attend_backward(queries, key_rows, values, grad_mixed, log_norms, distance, allowed):
    length = queries.shape[0]
    scale = HDIM ** (-0.5)

    def head_block(block):
        q_part = head_slice(queries, block)
        k_part = head_slice(key_rows, block)
        v_part = head_slice(values, block)
        g_part = head_slice(grad_mixed, block)
        scores = block_scores(q_part, k_part, block, distance, allowed)
        attn_probs = jnp.exp(scores - log_norms[block][:, :, None])
        grad_probs = jnp.einsum("qhd,khd->hqk", g_part, v_part, preferred_element_type=jnp.float32)
        inner = jnp.sum(attn_probs * grad_probs, -1, keepdims=True)
        grad_scores = (attn_probs * (grad_probs - inner)).astype(jnp.bfloat16)
        grad_q = (
            jnp.einsum("hqk,khd->qhd", grad_scores, k_part, preferred_element_type=jnp.float32)
            * scale
        )
        grad_k = (
            jnp.einsum("hqk,qhd->khd", grad_scores, q_part, preferred_element_type=jnp.float32)
            * scale
        )
        grad_v = jnp.einsum(
            "hqk,qhd->khd",
            attn_probs.astype(jnp.bfloat16),
            g_part,
            preferred_element_type=jnp.float32,
        )
        block_width = 4 * HDIM
        return (
            grad_q.reshape(length, block_width),
            grad_k.reshape(length, block_width),
            grad_v.reshape(length, block_width),
        )

    grad_q, grad_k, grad_v = lax.map(head_block, jnp.arange(HEADS // 4, dtype=jnp.int32))
    return (
        side_by_side(grad_q).astype(jnp.bfloat16),
        side_by_side(grad_k).astype(jnp.bfloat16),
        side_by_side(grad_v).astype(jnp.bfloat16),
    )


SMALL = ("ln1_gain", "ln1_bias", "q_bias", "v_bias", "b_out", "ln2_gain", "ln2_bias", "b_up", "b_down")


def gather_small(pieces):
    packed = jnp.concatenate(pieces)
    shards = lax.all_gather(packed, "shard", axis=0, tiled=False)
    fulls, offset = [], 0
    for piece in pieces:
        width = piece.shape[0]
        fulls.append(shards[:, offset : offset + width].reshape(-1))
        offset += width
    return fulls


def body(
    tokens,
    cont_segment,
    cotangent,
    ln1_gain,
    ln1_bias,
    w_qkv,
    q_bias,
    v_bias,
    w_out,
    b_out,
    ln2_gain,
    ln2_bias,
    w_up,
    b_up,
    w_down,
    b_down,
):
    shard_count = lax.psum(1, "shard")
    full_g1, full_s1, full_qb, full_vb, full_bo, full_g2, full_s2, full_bu, full_bd = gather_small(
        [ln1_gain, ln1_bias, q_bias, v_bias, b_out, ln2_gain, ln2_bias, b_up, b_down]
    )
    full_qkv = lax.all_gather(w_qkv, "shard", axis=1, tiled=True)
    full_out = lax.all_gather(w_out, "shard", axis=0, tiled=True)
    full_up = lax.all_gather(w_up, "shard", axis=1, tiled=True)
    full_down = lax.all_gather(w_down, "shard", axis=0, tiled=True)
    inputs = tokens[0].astype(jnp.float32)
    length, model_width = inputs.shape
    distance, allowed = layout(cont_segment[0])
    normed = normalize(inputs, full_g1.astype(jnp.float32), full_s1.astype(jnp.float32)).astype(
        jnp.bfloat16
    )
    projected = jnp.dot(normed, full_qkv, preferred_element_type=jnp.float32)
    queries = (projected[:, :model_width] + full_qb.astype(jnp.float32)).astype(jnp.bfloat16)
    key_rows = projected[:, model_width : 2 * model_width].astype(jnp.bfloat16)
    values = (projected[:, 2 * model_width :] + full_vb.astype(jnp.float32)).astype(jnp.bfloat16)
    mixed, log_norms = attend_forward(queries, key_rows, values, distance, allowed)
    branch = jnp.dot(mixed, full_out, preferred_element_type=jnp.float32) + full_bo.astype(
        jnp.float32
    )
    middle = inputs + branch
    normed_two = normalize(middle, full_g2.astype(jnp.float32), full_s2.astype(jnp.float32)).astype(
        jnp.bfloat16
    )
    pre_act = jnp.dot(normed_two, full_up, preferred_element_type=jnp.float32) + full_bu.astype(
        jnp.float32
    )
    activated = jax.nn.gelu(pre_act, approximate=True).astype(jnp.bfloat16)
    outputs = middle + (
        jnp.dot(activated, full_down, preferred_element_type=jnp.float32)
        + full_bd.astype(jnp.float32)
    )
    back_g1, back_qkv, back_out, back_g2, back_up, back_down = (
        full_g1, full_qkv, full_out, full_g2, full_up, full_down
    )
    cot_low = cotangent[0]
    cot_full = cot_low.astype(jnp.float32)
    zero_shift = jnp.zeros((model_width,), jnp.float32)
    grad_bd = jnp.sum(cot_full, 0)
    grad_act = jnp.einsum("to,fo->tf", cot_low, back_down, preferred_element_type=jnp.float32)
    gelu_value, gelu_pull = jax.vjp(partial(jax.nn.gelu, approximate=True), pre_act)
    grad_pre = gelu_pull(grad_act)[0].astype(jnp.bfloat16)
    grad_bu = jnp.sum(grad_pre.astype(jnp.float32), 0)
    grad_normed_two = jnp.einsum("tf,if->ti", grad_pre, back_up, preferred_element_type=jnp.float32)
    norm_value_two, norm_pull_two = jax.vjp(
        normalize, middle, back_g2.astype(jnp.float32), zero_shift
    )
    grad_mid_part, grad_g2, grad_s2 = norm_pull_two(grad_normed_two)
    grad_middle = cot_full + grad_mid_part
    grad_branch = grad_middle.astype(jnp.bfloat16)
    grad_bo = jnp.sum(grad_branch.astype(jnp.float32), 0)
    grad_mixed = jnp.einsum(
        "to,io->ti", grad_branch, back_out, preferred_element_type=jnp.float32
    ).astype(jnp.bfloat16)
    grad_q, grad_k, grad_v = attend_backward(
        queries, key_rows, values, grad_mixed, log_norms, distance, allowed
    )
    grad_proj = jnp.concatenate([grad_q, grad_k, grad_v], 1)
    grad_qb = jnp.sum(grad_q.astype(jnp.float32), 0)
    grad_vb = jnp.sum(grad_v.astype(jnp.float32), 0)
    grad_normed = jnp.einsum("tc,ic->ti", grad_proj, back_qkv, preferred_element_type=jnp.float32)
    norm_value_one, norm_pull_one = jax.vjp(
        normalize, inputs, back_g1.astype(jnp.float32), zero_shift
    )
    grad_in_part, grad_g1, grad_s1 = norm_pull_one(grad_normed)
    grad_inputs = grad_middle + grad_in_part
    grad_down = jnp.einsum("tf,to->fo", activated, cot_low, preferred_element_type=jnp.float32)
    grad_up = jnp.einsum("ti,tf->if", normed_two, grad_pre, preferred_element_type=jnp.float32)
    grad_out = jnp.einsum("ti,to->io", mixed, grad_branch, preferred_element_type=jnp.float32)
    grad_qkv = jnp.einsum("ti,tc->ic", normed, grad_proj, preferred_element_type=jnp.float32)
    smalls = [grad_g1, grad_s1, grad_qb, grad_vb, grad_bo, grad_g2, grad_s2, grad_bu, grad_bd]
    small_rows = jnp.concatenate([g.reshape(shard_count, -1) for g in smalls], 1)
    small_rows = small_rows.reshape(shard_count, -1, model_width)
    small_rows = jnp.pad(small_rows, ((0, 0), (0, 16 - small_rows.shape[1]), (0, 0)))
    down_rows = grad_down.reshape(shard_count, -1, model_width)
    down_width = down_rows.shape[1] * model_width
    joined = jnp.concatenate([down_rows, small_rows], 1).reshape(-1, model_width)
    joined_own = lax.psum_scatter(
        joined.astype(jnp.bfloat16), "shard", scatter_dimension=0, tiled=True
    ).reshape(-1)
    qkv_own = lax.psum_scatter(grad_qkv.astype(jnp.bfloat16), "shard", scatter_dimension=1, tiled=True)
    out_own = lax.psum_scatter(grad_out.astype(jnp.bfloat16), "shard", scatter_dimension=0, tiled=True)
    up_own = lax.psum_scatter(grad_up.astype(jnp.bfloat16), "shard", scatter_dimension=1, tiled=True)
    owned = [qkv_own, out_own, up_own, joined_own]
    flat = jnp.concatenate([o.reshape(-1).astype(jnp.float32) for o in owned])
    total = lax.psum(flat, "rep")
    pieces, offset = [], 0
    for o in owned:
        pieces.append(total[offset : offset + o.size].reshape(o.shape))
        offset += o.size
    qkv_fin, out_fin, up_fin, joined_fin = pieces
    down_fin = joined_fin[:down_width].reshape(grad_down.shape[0] // shard_count, -1)
    small_fin, offset = [], down_width
    for g in smalls:
        width = g.shape[0] // shard_count
        small_fin.append(joined_fin[offset : offset + width])
        offset += width
    g1_fin, s1_fin, qb_fin, vb_fin, bo_fin, g2_fin, s2_fin, bu_fin, bd_fin = small_fin
    return (
        outputs.astype(jnp.bfloat16)[None],
        grad_inputs.astype(jnp.bfloat16)[None],
        g1_fin,
        s1_fin,
        qkv_fin,
        qb_fin,
        vb_fin,
        out_fin,
        bo_fin,
        g2_fin,
        s2_fin,
        up_fin,
        bu_fin,
        down_fin,
        bd_fin,
    )


def solution(mesh):
    return jax.shard_map(
        body,
        mesh=mesh,
        in_specs=(
            P(("rep", "shard"), None, None),
            P(("rep", "shard"), None, None),
            P(("rep", "shard"), None, None),
            P("shard"),
            P("shard"),
            P(None, "shard"),
            P("shard"),
            P("shard"),
            P("shard", None),
            P("shard"),
            P("shard"),
            P("shard"),
            P(None, "shard"),
            P("shard"),
            P("shard", None),
            P("shard"),
        ),
        out_specs=(
            P(("rep", "shard"), None, None),
            P(("rep", "shard"), None, None),
            P("shard"),
            P("shard"),
            P(None, "shard"),
            P("shard"),
            P("shard"),
            P("shard", None),
            P("shard"),
            P("shard"),
            P("shard"),
            P(None, "shard"),
            P("shard"),
            P("shard", None),
            P("shard"),
        ),
        check_vma=False,
    )
```

```python
from functools import partial

import jax
import jax.numpy as jnp
from jax import lax
from jax.sharding import PartitionSpec as P

HEADS = 16
HDIM = 64
PROMPT = 256


def normalize(values, gain, shift):
    center = values - jnp.mean(values, -1, keepdims=True)
    spread = jnp.mean(center * center, -1, keepdims=True)
    return center * lax.rsqrt(spread + 1e-05) * gain + shift


def layout(segments):
    micros, row_count = segments.shape
    same_seg = segments[:, :, None] == segments[:, None, :]
    earlier = jnp.arange(row_count)[None, :] < jnp.arange(row_count)[:, None]
    offsets = jnp.sum(jnp.where(same_seg & earlier[None], 1, 0), -1).astype(jnp.int32)
    cont_pos = PROMPT + offsets
    owners = jnp.arange(micros, dtype=jnp.int32)[:, None] * row_count + segments
    positions = jnp.concatenate([jnp.arange(PROMPT, dtype=jnp.int32), cont_pos.reshape(-1)])
    groups = jnp.concatenate([jnp.full((PROMPT,), -1, jnp.int32), owners.reshape(-1)])
    places = jnp.arange(positions.shape[0], dtype=jnp.int32)
    allowed = (places[None, :] <= places[:, None]) & (
        (places[None, :] < PROMPT) | (groups[None, :] == groups[:, None])
    )
    distance = (positions[:, None] - positions[None, :]).astype(jnp.float32)
    return (distance, allowed)


def head_slice(matrix, block):
    block_width = 4 * HDIM
    part = lax.dynamic_slice_in_dim(matrix, block * block_width, block_width, 1)
    return part.reshape(matrix.shape[0], 4, HDIM)


def block_scores(q_part, k_part, block, distance, allowed):
    heads = (block * 4 + jnp.arange(4, dtype=jnp.int32)).astype(jnp.float32)
    slopes = jnp.exp2(-8.0 * (heads + 1.0) / HEADS)
    scores = jnp.einsum(
        "qhd,khd->hqk", q_part, k_part, preferred_element_type=jnp.float32
    ) * HDIM ** (-0.5)
    scores = scores - slopes[:, None, None] * distance[None]
    return jnp.where(allowed[None], scores, -jnp.inf)


def side_by_side(blocks):
    return jnp.transpose(blocks, (1, 0, 2)).reshape(
        blocks.shape[1], blocks.shape[0] * blocks.shape[2]
    )


def attend_forward(queries, key_rows, values, distance, allowed):
    length = queries.shape[0]

    def head_block(block):
        q_part = head_slice(queries, block)
        k_part = head_slice(key_rows, block)
        v_part = head_slice(values, block)
        scores = block_scores(q_part, k_part, block, distance, allowed)
        peak = jnp.max(scores, -1, keepdims=True)
        exps_rel = jnp.exp(scores - peak)
        row_totals = jnp.sum(exps_rel, -1, keepdims=True)
        attn_probs = (exps_rel / row_totals).astype(jnp.bfloat16)
        mixed = jnp.einsum("hqk,khd->qhd", attn_probs, v_part, preferred_element_type=jnp.float32)
        return (mixed.reshape(length, 4 * HDIM), (peak + jnp.log(row_totals))[:, :, 0])

    mixed, log_norms = lax.map(head_block, jnp.arange(HEADS // 4, dtype=jnp.int32))
    return (side_by_side(mixed).astype(jnp.bfloat16), log_norms)


def attend_backward(queries, key_rows, values, grad_mixed, log_norms, distance, allowed):
    length = queries.shape[0]
    scale = HDIM ** (-0.5)

    def head_block(block):
        q_part = head_slice(queries, block)
        k_part = head_slice(key_rows, block)
        v_part = head_slice(values, block)
        g_part = head_slice(grad_mixed, block)
        scores = block_scores(q_part, k_part, block, distance, allowed)
        attn_probs = jnp.exp(scores - log_norms[block][:, :, None])
        grad_probs = jnp.einsum("qhd,khd->hqk", g_part, v_part, preferred_element_type=jnp.float32)
        inner = jnp.sum(attn_probs * grad_probs, -1, keepdims=True)
        grad_scores = (attn_probs * (grad_probs - inner)).astype(jnp.bfloat16)
        grad_q = (
            jnp.einsum("hqk,khd->qhd", grad_scores, k_part, preferred_element_type=jnp.float32)
            * scale
        )
        grad_k = (
            jnp.einsum("hqk,qhd->khd", grad_scores, q_part, preferred_element_type=jnp.float32)
            * scale
        )
        grad_v = jnp.einsum(
            "hqk,qhd->khd",
            attn_probs.astype(jnp.bfloat16),
            g_part,
            preferred_element_type=jnp.float32,
        )
        block_width = 4 * HDIM
        return (
            grad_q.reshape(length, block_width),
            grad_k.reshape(length, block_width),
            grad_v.reshape(length, block_width),
        )

    grad_q, grad_k, grad_v = lax.map(head_block, jnp.arange(HEADS // 4, dtype=jnp.int32))
    return (
        side_by_side(grad_q).astype(jnp.bfloat16),
        side_by_side(grad_k).astype(jnp.bfloat16),
        side_by_side(grad_v).astype(jnp.bfloat16),
    )


SMALL = ("ln1_gain", "ln1_bias", "q_bias", "v_bias", "b_out", "ln2_gain", "ln2_bias", "b_up", "b_down")


def gather_small(pieces):
    packed = jnp.concatenate(pieces)
    shards = lax.all_gather(packed, "shard", axis=0, tiled=False)
    fulls, offset = [], 0
    for piece in pieces:
        width = piece.shape[0]
        fulls.append(shards[:, offset : offset + width].reshape(-1))
        offset += width
    return fulls


def body(
    tokens,
    cont_segment,
    cotangent,
    ln1_gain,
    ln1_bias,
    w_qkv,
    q_bias,
    v_bias,
    w_out,
    b_out,
    ln2_gain,
    ln2_bias,
    w_up,
    b_up,
    w_down,
    b_down,
):
    shard_count = lax.psum(1, "shard")
    full_g1, full_s1, full_qb, full_vb, full_bo, full_g2, full_s2, full_bu, full_bd = gather_small(
        [ln1_gain, ln1_bias, q_bias, v_bias, b_out, ln2_gain, ln2_bias, b_up, b_down]
    )
    full_qkv = lax.all_gather(w_qkv, "shard", axis=1, tiled=True)
    full_out = lax.all_gather(w_out, "shard", axis=0, tiled=True)
    full_up = lax.all_gather(w_up, "shard", axis=1, tiled=True)
    full_down = lax.all_gather(w_down, "shard", axis=0, tiled=True)
    inputs = tokens[0].astype(jnp.float32)
    length, model_width = inputs.shape
    distance, allowed = layout(cont_segment[0])
    normed = normalize(inputs, full_g1.astype(jnp.float32), full_s1.astype(jnp.float32)).astype(
        jnp.bfloat16
    )
    projected = jnp.dot(normed, full_qkv, preferred_element_type=jnp.float32)
    queries = (projected[:, :model_width] + full_qb.astype(jnp.float32)).astype(jnp.bfloat16)
    key_rows = projected[:, model_width : 2 * model_width].astype(jnp.bfloat16)
    values = (projected[:, 2 * model_width :] + full_vb.astype(jnp.float32)).astype(jnp.bfloat16)
    mixed, log_norms = attend_forward(queries, key_rows, values, distance, allowed)
    branch = jnp.dot(mixed, full_out, preferred_element_type=jnp.float32) + full_bo.astype(
        jnp.float32
    )
    middle = inputs + branch
    normed_two = normalize(middle, full_g2.astype(jnp.float32), full_s2.astype(jnp.float32)).astype(
        jnp.bfloat16
    )
    pre_act = jnp.dot(normed_two, full_up, preferred_element_type=jnp.float32) + full_bu.astype(
        jnp.float32
    )
    activated = jax.nn.gelu(pre_act, approximate=True).astype(jnp.bfloat16)
    outputs = middle + (
        jnp.dot(activated, full_down, preferred_element_type=jnp.float32)
        + full_bd.astype(jnp.float32)
    )
    back_g1, back_qkv, back_out, back_g2, back_up, back_down = (
        full_g1, full_qkv, full_out, full_g2, full_up, full_down
    )
    cot_low = cotangent[0]
    cot_full = cot_low.astype(jnp.float32)
    zero_shift = jnp.zeros((model_width,), jnp.float32)
    grad_bd = jnp.sum(cot_full, 0)
    grad_act = jnp.einsum("to,fo->tf", cot_low, back_down, preferred_element_type=jnp.float32)
    gelu_value, gelu_pull = jax.vjp(partial(jax.nn.gelu, approximate=True), pre_act)
    grad_pre = gelu_pull(grad_act)[0].astype(jnp.bfloat16)
    grad_bu = jnp.sum(grad_pre.astype(jnp.float32), 0)
    grad_normed_two = jnp.einsum("tf,if->ti", grad_pre, back_up, preferred_element_type=jnp.float32)
    norm_value_two, norm_pull_two = jax.vjp(
        normalize, middle, back_g2.astype(jnp.float32), zero_shift
    )
    grad_mid_part, grad_g2, grad_s2 = norm_pull_two(grad_normed_two)
    grad_middle = cot_full + grad_mid_part
    grad_branch = grad_middle.astype(jnp.bfloat16)
    grad_bo = jnp.sum(grad_branch.astype(jnp.float32), 0)
    grad_mixed = jnp.einsum(
        "to,io->ti", grad_branch, back_out, preferred_element_type=jnp.float32
    ).astype(jnp.bfloat16)
    grad_q, grad_k, grad_v = attend_backward(
        queries, key_rows, values, grad_mixed, log_norms, distance, allowed
    )
    grad_proj = jnp.concatenate([grad_q, grad_k, grad_v], 1)
    grad_qb = jnp.sum(grad_q.astype(jnp.float32), 0)
    grad_vb = jnp.sum(grad_v.astype(jnp.float32), 0)
    grad_normed = jnp.einsum("tc,ic->ti", grad_proj, back_qkv, preferred_element_type=jnp.float32)
    norm_value_one, norm_pull_one = jax.vjp(
        normalize, inputs, back_g1.astype(jnp.float32), zero_shift
    )
    grad_in_part, grad_g1, grad_s1 = norm_pull_one(grad_normed)
    grad_inputs = grad_middle + grad_in_part
    grad_down = jnp.einsum("tf,to->fo", activated, cot_low, preferred_element_type=jnp.float32)
    grad_up = jnp.einsum("ti,tf->if", normed_two, grad_pre, preferred_element_type=jnp.float32)
    grad_out = jnp.einsum("ti,to->io", mixed, grad_branch, preferred_element_type=jnp.float32)
    grad_qkv_t = jnp.einsum("tc,ti->ci", grad_proj, normed, preferred_element_type=jnp.float32)
    smalls = [grad_g1, grad_s1, grad_qb, grad_vb, grad_bo, grad_g2, grad_s2, grad_bu, grad_bd]
    small_rows = jnp.concatenate([g.reshape(shard_count, -1) for g in smalls], 1)
    small_rows = small_rows.reshape(shard_count, -1, model_width)
    small_rows = jnp.pad(small_rows, ((0, 0), (0, 16 - small_rows.shape[1]), (0, 0)))
    down_rows = grad_down.reshape(shard_count, -1, model_width)
    down_height = down_rows.shape[1]
    joined = jnp.concatenate([down_rows, small_rows], 1).reshape(-1, model_width)
    joined_own = lax.psum_scatter(
        joined.astype(jnp.bfloat16), "shard", scatter_dimension=0, tiled=True
    )
    qkv_own = lax.psum_scatter(
        grad_qkv_t.astype(jnp.bfloat16), "shard", scatter_dimension=0, tiled=True
    )
    out_own = lax.psum_scatter(grad_out.astype(jnp.bfloat16), "shard", scatter_dimension=0, tiled=True)
    up_own = lax.psum_scatter(grad_up.astype(jnp.bfloat16), "shard", scatter_dimension=1, tiled=True)
    owned = [qkv_own, out_own, up_own, joined_own]
    total = lax.psum(jnp.concatenate(owned, 0), "rep")
    pieces, offset = [], 0
    for o in owned:
        pieces.append(total[offset : offset + o.shape[0]])
        offset += o.shape[0]
    qkv_fin, out_fin, up_fin, joined_fin = pieces
    qkv_fin = qkv_fin.astype(jnp.float32).T
    out_fin = out_fin.astype(jnp.float32)
    up_fin = up_fin.astype(jnp.float32)
    down_fin = joined_fin[:down_height].astype(jnp.float32)
    small_flat = joined_fin[down_height:].reshape(-1).astype(jnp.float32)
    small_fin, offset = [], 0
    for g in smalls:
        width = g.shape[0] // shard_count
        small_fin.append(small_flat[offset : offset + width])
        offset += width
    g1_fin, s1_fin, qb_fin, vb_fin, bo_fin, g2_fin, s2_fin, bu_fin, bd_fin = small_fin
    return (
        outputs.astype(jnp.bfloat16)[None],
        grad_inputs.astype(jnp.bfloat16)[None],
        g1_fin,
        s1_fin,
        qkv_fin,
        qb_fin,
        vb_fin,
        out_fin,
        bo_fin,
        g2_fin,
        s2_fin,
        up_fin,
        bu_fin,
        down_fin,
        bd_fin,
    )


def solution(mesh):
    return jax.shard_map(
        body,
        mesh=mesh,
        in_specs=(
            P(("rep", "shard"), None, None),
            P(("rep", "shard"), None, None),
            P(("rep", "shard"), None, None),
            P("shard"),
            P("shard"),
            P(None, "shard"),
            P("shard"),
            P("shard"),
            P("shard", None),
            P("shard"),
            P("shard"),
            P("shard"),
            P(None, "shard"),
            P("shard"),
            P("shard", None),
            P("shard"),
        ),
        out_specs=(
            P(("rep", "shard"), None, None),
            P(("rep", "shard"), None, None),
            P("shard"),
            P("shard"),
            P(None, "shard"),
            P("shard"),
            P("shard"),
            P("shard", None),
            P("shard"),
            P("shard"),
            P("shard"),
            P(None, "shard"),
            P("shard"),
            P("shard", None),
            P("shard"),
        ),
        check_vma=False,
    )
```

```python
from functools import partial

import jax
import jax.numpy as jnp
from jax import lax
from jax.sharding import PartitionSpec as P


HEADS = 16
HDIM = 64
PROMPT = 256


def normalize(values, gain, shift):
    center = values - jnp.mean(values, -1, keepdims=True)
    spread = jnp.mean(center * center, -1, keepdims=True)
    return center * lax.rsqrt(spread + 1e-05) * gain + shift


def layout(segments):
    micros, row_count = segments.shape
    same_seg = segments[:, :, None] == segments[:, None, :]
    earlier = jnp.arange(row_count)[None, :] < jnp.arange(row_count)[:, None]
    offsets = jnp.sum(jnp.where(same_seg & earlier[None], 1, 0), -1).astype(jnp.int32)
    cont_pos = PROMPT + offsets
    owners = jnp.arange(micros, dtype=jnp.int32)[:, None] * row_count + segments
    positions = jnp.concatenate([jnp.arange(PROMPT, dtype=jnp.int32), cont_pos.reshape(-1)])
    groups = jnp.concatenate([jnp.full((PROMPT,), -1, jnp.int32), owners.reshape(-1)])
    places = jnp.arange(positions.shape[0], dtype=jnp.int32)
    allowed = (places[None, :] <= places[:, None]) & (
        (places[None, :] < PROMPT) | (groups[None, :] == groups[:, None])
    )
    distance = (positions[:, None] - positions[None, :]).astype(jnp.float32)
    return (distance, allowed)


def head_slice(matrix, block):
    block_width = 4 * HDIM
    part = lax.dynamic_slice_in_dim(matrix, block * block_width, block_width, 1)
    return part.reshape(matrix.shape[0], 4, HDIM)


def block_scores(q_part, k_part, block, distance, allowed):
    heads = (block * 4 + jnp.arange(4, dtype=jnp.int32)).astype(jnp.float32)
    slopes = jnp.exp2(-8.0 * (heads + 1.0) / HEADS)
    scores = jnp.einsum(
        "qhd,khd->hqk", q_part, k_part, preferred_element_type=jnp.float32
    ) * HDIM ** (-0.5)
    scores = scores - slopes[:, None, None] * distance[None]
    return jnp.where(allowed[None], scores, -jnp.inf)


def side_by_side(blocks):
    return jnp.transpose(blocks, (1, 0, 2)).reshape(
        blocks.shape[1], blocks.shape[0] * blocks.shape[2]
    )


def attend_forward(queries, key_rows, values, distance, allowed):
    length = queries.shape[0]

    def head_block(block):
        q_part = head_slice(queries, block)
        k_part = head_slice(key_rows, block)
        v_part = head_slice(values, block)
        scores = block_scores(q_part, k_part, block, distance, allowed)
        peak = jnp.max(scores, -1, keepdims=True)
        exps_rel = jnp.exp(scores - peak)
        row_totals = jnp.sum(exps_rel, -1, keepdims=True)
        attn_probs = (exps_rel / row_totals).astype(jnp.bfloat16)
        mixed = jnp.einsum("hqk,khd->qhd", attn_probs, v_part, preferred_element_type=jnp.float32)
        return (mixed.reshape(length, 4 * HDIM), (peak + jnp.log(row_totals))[:, :, 0])

    mixed, log_norms = lax.map(head_block, jnp.arange(HEADS // 4, dtype=jnp.int32))
    return (side_by_side(mixed).astype(jnp.bfloat16), log_norms)


def attend_backward(queries, key_rows, values, grad_mixed, log_norms, distance, allowed):
    length = queries.shape[0]
    scale = HDIM ** (-0.5)

    def head_block(block):
        q_part = head_slice(queries, block)
        k_part = head_slice(key_rows, block)
        v_part = head_slice(values, block)
        g_part = head_slice(grad_mixed, block)
        scores = block_scores(q_part, k_part, block, distance, allowed)
        attn_probs = jnp.exp(scores - log_norms[block][:, :, None])
        grad_probs = jnp.einsum("qhd,khd->hqk", g_part, v_part, preferred_element_type=jnp.float32)
        inner = jnp.sum(attn_probs * grad_probs, -1, keepdims=True)
        grad_scores = (attn_probs * (grad_probs - inner)).astype(jnp.bfloat16)
        grad_q = (
            jnp.einsum("hqk,khd->qhd", grad_scores, k_part, preferred_element_type=jnp.float32)
            * scale
        )
        grad_k = (
            jnp.einsum("hqk,qhd->khd", grad_scores, q_part, preferred_element_type=jnp.float32)
            * scale
        )
        grad_v = jnp.einsum(
            "hqk,qhd->khd",
            attn_probs.astype(jnp.bfloat16),
            g_part,
            preferred_element_type=jnp.float32,
        )
        block_width = 4 * HDIM
        return (
            grad_q.reshape(length, block_width),
            grad_k.reshape(length, block_width),
            grad_v.reshape(length, block_width),
        )

    grad_q, grad_k, grad_v = lax.map(head_block, jnp.arange(HEADS // 4, dtype=jnp.int32))
    return (
        side_by_side(grad_q).astype(jnp.bfloat16),
        side_by_side(grad_k).astype(jnp.bfloat16),
        side_by_side(grad_v).astype(jnp.bfloat16),
    )


def bit_steps(size):
    assert size & (size - 1) == 0
    return [1 << b for b in range(size.bit_length() - 1)]


def chunk_order(size, steps):
    places = []
    for member in range(size):
        place = 0
        for step in steps:
            place = place * 2 + (member // step) % 2
        places.append(place)
    order = [0] * size
    for member, place in enumerate(places):
        order[place] = member
    return order


def reorder_cols(matrix, order):
    pieces = jnp.split(matrix, len(order), 1)
    return jnp.concatenate([pieces[k] for k in order], 1)


def halving(arrays, axis, size, steps):
    index = lax.axis_index(axis)
    for step in steps:
        bit = (index // step) % 2
        keeps, sends = [], []
        for array in arrays:
            pair = array.reshape(2, array.shape[0] // 2, *array.shape[1:])
            keeps.append(lax.dynamic_index_in_dim(pair, bit, 0, keepdims=False))
            sends.append(
                lax.dynamic_index_in_dim(pair, 1 - bit, 0, keepdims=False).astype(jnp.bfloat16)
            )
        got = lax.ppermute(jnp.concatenate(sends, 0), axis, [(a, a ^ step) for a in range(size)])
        arrays, offset = [], 0
        for keep in keeps:
            arrays.append(keep + got[offset : offset + keep.shape[0]].astype(jnp.float32))
            offset += keep.shape[0]
    return arrays


def gather_small(pieces):
    packed = jnp.concatenate(pieces)
    shards = lax.all_gather(packed, "shard", axis=0, tiled=False)
    fulls, offset = [], 0
    for piece in pieces:
        width = piece.shape[0]
        fulls.append(shards[:, offset : offset + width].reshape(-1))
        offset += width
    return fulls


def body_inner(
    tokens,
    cont_segment,
    cotangent,
    ln1_gain,
    ln1_bias,
    w_qkv,
    q_bias,
    v_bias,
    w_out,
    b_out,
    ln2_gain,
    ln2_bias,
    w_up,
    b_up,
    w_down,
    b_down,
):
    shard_count = lax.psum(1, "shard")
    full_g1, full_s1, full_qb, full_vb, full_bo, full_g2, full_s2, full_bu, full_bd = gather_small(
        [ln1_gain, ln1_bias, q_bias, v_bias, b_out, ln2_gain, ln2_bias, b_up, b_down]
    )
    full_qkv = lax.all_gather(w_qkv, "shard", axis=1, tiled=True)
    full_out = lax.all_gather(w_out, "shard", axis=0, tiled=True)
    full_up = lax.all_gather(w_up, "shard", axis=1, tiled=True)
    full_down = lax.all_gather(w_down, "shard", axis=0, tiled=True)
    inputs = tokens[0].astype(jnp.float32)
    _, model_width = inputs.shape
    distance, allowed = layout(cont_segment[0])
    normed = normalize(inputs, full_g1.astype(jnp.float32), full_s1.astype(jnp.float32)).astype(
        jnp.bfloat16
    )
    projected = jnp.dot(normed, full_qkv, preferred_element_type=jnp.float32)
    queries = (projected[:, :model_width] + full_qb.astype(jnp.float32)).astype(jnp.bfloat16)
    key_rows = projected[:, model_width : 2 * model_width].astype(jnp.bfloat16)
    values = (projected[:, 2 * model_width :] + full_vb.astype(jnp.float32)).astype(jnp.bfloat16)
    mixed, log_norms = attend_forward(queries, key_rows, values, distance, allowed)
    branch = jnp.dot(mixed, full_out, preferred_element_type=jnp.float32) + full_bo.astype(
        jnp.float32
    )
    middle = inputs + branch
    normed_two = normalize(middle, full_g2.astype(jnp.float32), full_s2.astype(jnp.float32)).astype(
        jnp.bfloat16
    )
    pre_act = jnp.dot(normed_two, full_up, preferred_element_type=jnp.float32) + full_bu.astype(
        jnp.float32
    )
    activated = jax.nn.gelu(pre_act, approximate=True).astype(jnp.bfloat16)
    outputs = middle + (
        jnp.dot(activated, full_down, preferred_element_type=jnp.float32)
        + full_bd.astype(jnp.float32)
    )
    back_g1, back_qkv, back_out, back_g2, back_up, back_down = (
        full_g1, full_qkv, full_out, full_g2, full_up, full_down
    )
    shard_steps = bit_steps(shard_count)
    order = chunk_order(shard_count, shard_steps)
    cot_low = cotangent[0]
    cot_full = cot_low.astype(jnp.float32)
    zero_shift = jnp.zeros((model_width,), jnp.float32)
    grad_bd = jnp.sum(cot_full, 0)
    grad_act = jnp.einsum("to,fo->tf", cot_low, back_down, preferred_element_type=jnp.float32)
    _, gelu_pull = jax.vjp(partial(jax.nn.gelu, approximate=True), pre_act)
    grad_pre = gelu_pull(grad_act)[0].astype(jnp.bfloat16)
    grad_bu = jnp.sum(grad_pre.astype(jnp.float32), 0)
    grad_down = jnp.einsum(
        "tf,to->fo", reorder_cols(activated, order), cot_low, preferred_element_type=jnp.float32
    )
    grad_up_t = jnp.einsum(
        "tf,ti->fi", reorder_cols(grad_pre, order), normed_two, preferred_element_type=jnp.float32
    )
    down_own, up_own = halving([grad_down, grad_up_t], "shard", shard_count, shard_steps)
    grad_normed_two = jnp.einsum("tf,if->ti", grad_pre, back_up, preferred_element_type=jnp.float32)
    _, norm_pull_two = jax.vjp(normalize, middle, back_g2.astype(jnp.float32), zero_shift)
    grad_mid_part, grad_g2, grad_s2 = norm_pull_two(grad_normed_two)
    grad_middle = cot_full + grad_mid_part
    grad_branch = grad_middle.astype(jnp.bfloat16)
    grad_bo = jnp.sum(grad_branch.astype(jnp.float32), 0)
    grad_mixed = jnp.einsum(
        "to,io->ti", grad_branch, back_out, preferred_element_type=jnp.float32
    ).astype(jnp.bfloat16)
    grad_out = jnp.einsum(
        "ti,to->io", reorder_cols(mixed, order), grad_branch, preferred_element_type=jnp.float32
    )
    grad_q, grad_k, grad_v = attend_backward(
        queries, key_rows, values, grad_mixed, log_norms, distance, allowed
    )
    grad_proj = jnp.concatenate([grad_q, grad_k, grad_v], 1)
    grad_qb = jnp.sum(grad_q.astype(jnp.float32), 0)
    grad_vb = jnp.sum(grad_v.astype(jnp.float32), 0)
    grad_normed = jnp.einsum("tc,ic->ti", grad_proj, back_qkv, preferred_element_type=jnp.float32)
    _, norm_pull_one = jax.vjp(normalize, inputs, back_g1.astype(jnp.float32), zero_shift)
    grad_in_part, grad_g1, grad_s1 = norm_pull_one(grad_normed)
    grad_inputs = grad_middle + grad_in_part
    grad_qkv_t = jnp.einsum(
        "tc,ti->ci", reorder_cols(grad_proj, order), normed, preferred_element_type=jnp.float32
    )
    smalls = [grad_g1, grad_s1, grad_qb, grad_vb, grad_bo, grad_g2, grad_s2, grad_bu, grad_bd]
    small_rows = jnp.concatenate([g.reshape(shard_count, -1) for g in smalls], 1)
    small_rows = small_rows.reshape(shard_count, -1, model_width)
    small_rows = jnp.pad(small_rows, ((0, 0), (0, 16 - small_rows.shape[1]), (0, 0)))
    small_rows = jnp.concatenate([small_rows[k] for k in order], 0)
    out_own, qkv_own, small_own = halving(
        [grad_out, grad_qkv_t, small_rows], "shard", shard_count, shard_steps
    )
    owned = [down_own, up_own, out_own, qkv_own, small_own]
    total = lax.psum(jnp.concatenate([o.astype(jnp.bfloat16) for o in owned], 0), "rep")
    pieces, offset = [], 0
    for o in owned:
        pieces.append(total[offset : offset + o.shape[0]])
        offset += o.shape[0]
    down_fin, up_fin, out_fin, qkv_fin, small_fin_rows = pieces
    down_fin = down_fin.astype(jnp.float32)
    up_fin = up_fin.astype(jnp.float32).T
    out_fin = out_fin.astype(jnp.float32)
    qkv_fin = qkv_fin.astype(jnp.float32).T
    small_flat = small_fin_rows.reshape(-1).astype(jnp.float32)
    small_fin, offset = [], 0
    for g in smalls:
        width = g.shape[0] // shard_count
        small_fin.append(small_flat[offset : offset + width])
        offset += width
    g1_fin, s1_fin, qb_fin, vb_fin, bo_fin, g2_fin, s2_fin, bu_fin, bd_fin = small_fin
    return (
        outputs.astype(jnp.bfloat16)[None],
        grad_inputs.astype(jnp.bfloat16)[None],
        g1_fin,
        s1_fin,
        qkv_fin,
        qb_fin,
        vb_fin,
        out_fin,
        bo_fin,
        g2_fin,
        s2_fin,
        up_fin,
        bu_fin,
        down_fin,
        bd_fin,
    )


def solution(mesh):
    return jax.shard_map(
        body_inner,
        mesh=mesh,
        in_specs=(
            P(("rep", "shard"), None, None),
            P(("rep", "shard"), None, None),
            P(("rep", "shard"), None, None),
            P("shard"),
            P("shard"),
            P(None, "shard"),
            P("shard"),
            P("shard"),
            P("shard", None),
            P("shard"),
            P("shard"),
            P("shard"),
            P(None, "shard"),
            P("shard"),
            P("shard", None),
            P("shard"),
        ),
        out_specs=(
            P(("rep", "shard"), None, None),
            P(("rep", "shard"), None, None),
            P("shard"),
            P("shard"),
            P(None, "shard"),
            P("shard"),
            P("shard"),
            P("shard", None),
            P("shard"),
            P("shard"),
            P("shard"),
            P(None, "shard"),
            P("shard"),
            P("shard", None),
            P("shard"),
        ),
        check_vma=False,
    )
```

```python
from functools import partial

import jax
import jax.numpy as jnp
from jax import lax
from jax.sharding import PartitionSpec as P


HEADS = 16
HDIM = 64
PROMPT = 256


def normalize(values, gain, shift):
    center = values - jnp.mean(values, -1, keepdims=True)
    spread = jnp.mean(center * center, -1, keepdims=True)
    return center * lax.rsqrt(spread + 1e-05) * gain + shift


def layout(segments):
    micros, row_count = segments.shape
    same_seg = segments[:, :, None] == segments[:, None, :]
    earlier = jnp.arange(row_count)[None, :] < jnp.arange(row_count)[:, None]
    offsets = jnp.sum(jnp.where(same_seg & earlier[None], 1, 0), -1).astype(jnp.int32)
    cont_pos = PROMPT + offsets
    owners = jnp.arange(micros, dtype=jnp.int32)[:, None] * row_count + segments
    positions = jnp.concatenate([jnp.arange(PROMPT, dtype=jnp.int32), cont_pos.reshape(-1)])
    groups = jnp.concatenate([jnp.full((PROMPT,), -1, jnp.int32), owners.reshape(-1)])
    places = jnp.arange(positions.shape[0], dtype=jnp.int32)
    allowed = (places[None, :] <= places[:, None]) & (
        (places[None, :] < PROMPT) | (groups[None, :] == groups[:, None])
    )
    distance = (positions[:, None] - positions[None, :]).astype(jnp.float32)
    return (distance, allowed)


def head_slice(matrix, block):
    block_width = 4 * HDIM
    part = lax.dynamic_slice_in_dim(matrix, block * block_width, block_width, 1)
    return part.reshape(matrix.shape[0], 4, HDIM)


def block_scores(q_part, k_part, block, distance, allowed):
    heads = (block * 4 + jnp.arange(4, dtype=jnp.int32)).astype(jnp.float32)
    slopes = jnp.exp2(-8.0 * (heads + 1.0) / HEADS)
    scores = jnp.einsum(
        "qhd,khd->hqk", q_part, k_part, preferred_element_type=jnp.float32
    ) * HDIM ** (-0.5)
    scores = scores - slopes[:, None, None] * distance[None]
    return jnp.where(allowed[None], scores, -jnp.inf)


def side_by_side(blocks):
    return jnp.transpose(blocks, (1, 0, 2)).reshape(
        blocks.shape[1], blocks.shape[0] * blocks.shape[2]
    )


def attend_forward(queries, key_rows, values, distance, allowed):
    length = queries.shape[0]

    def head_block(block):
        q_part = head_slice(queries, block)
        k_part = head_slice(key_rows, block)
        v_part = head_slice(values, block)
        scores = block_scores(q_part, k_part, block, distance, allowed)
        peak = jnp.max(scores, -1, keepdims=True)
        exps_rel = jnp.exp(scores - peak)
        row_totals = jnp.sum(exps_rel, -1, keepdims=True)
        attn_probs = (exps_rel / row_totals).astype(jnp.bfloat16)
        mixed = jnp.einsum("hqk,khd->qhd", attn_probs, v_part, preferred_element_type=jnp.float32)
        return (mixed.reshape(length, 4 * HDIM), (peak + jnp.log(row_totals))[:, :, 0])

    mixed, log_norms = lax.map(head_block, jnp.arange(HEADS // 4, dtype=jnp.int32))
    return (side_by_side(mixed).astype(jnp.bfloat16), log_norms)


def attend_backward(queries, key_rows, values, grad_mixed, log_norms, distance, allowed):
    length = queries.shape[0]
    scale = HDIM ** (-0.5)

    def head_block(block):
        q_part = head_slice(queries, block)
        k_part = head_slice(key_rows, block)
        v_part = head_slice(values, block)
        g_part = head_slice(grad_mixed, block)
        scores = block_scores(q_part, k_part, block, distance, allowed)
        attn_probs = jnp.exp(scores - log_norms[block][:, :, None])
        grad_probs = jnp.einsum("qhd,khd->hqk", g_part, v_part, preferred_element_type=jnp.float32)
        inner = jnp.sum(attn_probs * grad_probs, -1, keepdims=True)
        grad_scores = (attn_probs * (grad_probs - inner)).astype(jnp.bfloat16)
        grad_q = (
            jnp.einsum("hqk,khd->qhd", grad_scores, k_part, preferred_element_type=jnp.float32)
            * scale
        )
        grad_k = (
            jnp.einsum("hqk,qhd->khd", grad_scores, q_part, preferred_element_type=jnp.float32)
            * scale
        )
        grad_v = jnp.einsum(
            "hqk,qhd->khd",
            attn_probs.astype(jnp.bfloat16),
            g_part,
            preferred_element_type=jnp.float32,
        )
        block_width = 4 * HDIM
        return (
            grad_q.reshape(length, block_width),
            grad_k.reshape(length, block_width),
            grad_v.reshape(length, block_width),
        )

    grad_q, grad_k, grad_v = lax.map(head_block, jnp.arange(HEADS // 4, dtype=jnp.int32))
    return (
        side_by_side(grad_q).astype(jnp.bfloat16),
        side_by_side(grad_k).astype(jnp.bfloat16),
        side_by_side(grad_v).astype(jnp.bfloat16),
    )


def bit_steps(size):
    assert size & (size - 1) == 0
    return [1 << b for b in range(size.bit_length() - 1)]


def chunk_order(size, steps):
    places = []
    for member in range(size):
        place = 0
        for step in steps:
            place = place * 2 + (member // step) % 2
        places.append(place)
    order = [0] * size
    for member, place in enumerate(places):
        order[place] = member
    return order


def reorder_cols(matrix, order):
    pieces = jnp.split(matrix, len(order), 1)
    return jnp.concatenate([pieces[k] for k in order], 1)


def halving(arrays, axis, size, steps):
    index = lax.axis_index(axis)
    for step in steps:
        bit = (index // step) % 2
        keeps, sends = [], []
        for array in arrays:
            pair = array.reshape(2, array.shape[0] // 2, *array.shape[1:])
            keeps.append(lax.dynamic_index_in_dim(pair, bit, 0, keepdims=False))
            sends.append(
                lax.dynamic_index_in_dim(pair, 1 - bit, 0, keepdims=False).astype(jnp.bfloat16)
            )
        got = lax.ppermute(jnp.concatenate(sends, 0), axis, [(a, a ^ step) for a in range(size)])
        arrays, offset = [], 0
        for keep in keeps:
            arrays.append(keep + got[offset : offset + keep.shape[0]].astype(jnp.float32))
            offset += keep.shape[0]
    return arrays


def doubling(buf, axis, size, steps):
    index = lax.axis_index(axis)
    for step in steps:
        low = (index // step) % 2 == 0
        got = lax.ppermute(buf, axis, [(a, a ^ step) for a in range(size)])
        buf = jnp.concatenate([jnp.where(low, buf, got), jnp.where(low, got, buf)], 0)
    return buf


def gather_small(pieces):
    packed = jnp.concatenate(pieces)
    shards = lax.all_gather(packed, "shard", axis=0, tiled=False)
    fulls, offset = [], 0
    for piece in pieces:
        width = piece.shape[0]
        fulls.append(shards[:, offset : offset + width].reshape(-1))
        offset += width
    return fulls


def body_inner(
    tokens,
    cont_segment,
    cotangent,
    ln1_gain,
    ln1_bias,
    w_qkv,
    q_bias,
    v_bias,
    w_out,
    b_out,
    ln2_gain,
    ln2_bias,
    w_up,
    b_up,
    w_down,
    b_down,
):
    shard_count = lax.psum(1, "shard")
    full_g1, full_s1, full_qb, full_vb, full_bo, full_g2, full_s2, full_bu, full_bd = gather_small(
        [ln1_gain, ln1_bias, q_bias, v_bias, b_out, ln2_gain, ln2_bias, b_up, b_down]
    )
    full_qkv = lax.all_gather(w_qkv, "shard", axis=1, tiled=True)
    full_out = lax.all_gather(w_out, "shard", axis=0, tiled=True)
    full_up = lax.all_gather(w_up, "shard", axis=1, tiled=True)
    full_down = lax.all_gather(w_down, "shard", axis=0, tiled=True)
    inputs = tokens[0].astype(jnp.float32)
    _, model_width = inputs.shape
    distance, allowed = layout(cont_segment[0])
    normed = normalize(inputs, full_g1.astype(jnp.float32), full_s1.astype(jnp.float32)).astype(
        jnp.bfloat16
    )
    projected = jnp.dot(normed, full_qkv, preferred_element_type=jnp.float32)
    queries = (projected[:, :model_width] + full_qb.astype(jnp.float32)).astype(jnp.bfloat16)
    key_rows = projected[:, model_width : 2 * model_width].astype(jnp.bfloat16)
    values = (projected[:, 2 * model_width :] + full_vb.astype(jnp.float32)).astype(jnp.bfloat16)
    mixed, log_norms = attend_forward(queries, key_rows, values, distance, allowed)
    branch = jnp.dot(mixed, full_out, preferred_element_type=jnp.float32) + full_bo.astype(
        jnp.float32
    )
    middle = inputs + branch
    normed_two = normalize(middle, full_g2.astype(jnp.float32), full_s2.astype(jnp.float32)).astype(
        jnp.bfloat16
    )
    pre_act = jnp.dot(normed_two, full_up, preferred_element_type=jnp.float32) + full_bu.astype(
        jnp.float32
    )
    activated = jax.nn.gelu(pre_act, approximate=True).astype(jnp.bfloat16)
    outputs = middle + (
        jnp.dot(activated, full_down, preferred_element_type=jnp.float32)
        + full_bd.astype(jnp.float32)
    )
    back_g1, back_qkv, back_out, back_g2, back_up, back_down = (
        full_g1, full_qkv, full_out, full_g2, full_up, full_down
    )
    shard_steps = bit_steps(shard_count)
    order = chunk_order(shard_count, shard_steps)
    cot_low = cotangent[0]
    cot_full = cot_low.astype(jnp.float32)
    zero_shift = jnp.zeros((model_width,), jnp.float32)
    grad_bd = jnp.sum(cot_full, 0)
    grad_act = jnp.einsum("to,fo->tf", cot_low, back_down, preferred_element_type=jnp.float32)
    _, gelu_pull = jax.vjp(partial(jax.nn.gelu, approximate=True), pre_act)
    grad_pre = gelu_pull(grad_act)[0].astype(jnp.bfloat16)
    grad_bu = jnp.sum(grad_pre.astype(jnp.float32), 0)
    grad_down = jnp.einsum(
        "tf,to->fo", reorder_cols(activated, order), cot_low, preferred_element_type=jnp.float32
    )
    grad_up_t = jnp.einsum(
        "tf,ti->fi", reorder_cols(grad_pre, order), normed_two, preferred_element_type=jnp.float32
    )
    grad_normed_two = jnp.einsum("tf,if->ti", grad_pre, back_up, preferred_element_type=jnp.float32)
    _, norm_pull_two = jax.vjp(normalize, middle, back_g2.astype(jnp.float32), zero_shift)
    grad_mid_part, grad_g2, grad_s2 = norm_pull_two(grad_normed_two)
    grad_middle = cot_full + grad_mid_part
    grad_branch = grad_middle.astype(jnp.bfloat16)
    grad_bo = jnp.sum(grad_branch.astype(jnp.float32), 0)
    grad_mixed = jnp.einsum(
        "to,io->ti", grad_branch, back_out, preferred_element_type=jnp.float32
    ).astype(jnp.bfloat16)
    grad_out = jnp.einsum(
        "ti,to->io", reorder_cols(mixed, order), grad_branch, preferred_element_type=jnp.float32
    )
    down_own, up_own, out_own = halving(
        [grad_down, grad_up_t, grad_out], "shard", shard_count, shard_steps
    )
    owned_a = [down_own, up_own, out_own]
    total_a = lax.psum(jnp.concatenate([o.astype(jnp.bfloat16) for o in owned_a], 0), "rep")
    grad_q, grad_k, grad_v = attend_backward(
        queries, key_rows, values, grad_mixed, log_norms, distance, allowed
    )
    grad_proj = jnp.concatenate([grad_q, grad_k, grad_v], 1)
    grad_qb = jnp.sum(grad_q.astype(jnp.float32), 0)
    grad_vb = jnp.sum(grad_v.astype(jnp.float32), 0)
    grad_normed = jnp.einsum("tc,ic->ti", grad_proj, back_qkv, preferred_element_type=jnp.float32)
    _, norm_pull_one = jax.vjp(normalize, inputs, back_g1.astype(jnp.float32), zero_shift)
    grad_in_part, grad_g1, grad_s1 = norm_pull_one(grad_normed)
    grad_inputs = grad_middle + grad_in_part
    grad_qkv_t = jnp.einsum(
        "tc,ti->ci", reorder_cols(grad_proj, order), normed, preferred_element_type=jnp.float32
    )
    smalls = [grad_g1, grad_s1, grad_qb, grad_vb, grad_bo, grad_g2, grad_s2, grad_bu, grad_bd]
    reps = lax.psum(1, "rep")
    rep_steps = bit_steps(reps)
    qkv_rows = grad_qkv_t.shape[0] // shard_count
    small_rows = jnp.concatenate([g.reshape(shard_count, -1) for g in smalls], 1)
    small_rows = small_rows.reshape(shard_count, -1, model_width)
    pad_to = small_rows.shape[1] + (-(qkv_rows + small_rows.shape[1]) % (8 * reps))
    small_rows = jnp.pad(small_rows, ((0, 0), (0, pad_to - small_rows.shape[1]), (0, 0)))
    small_rows = jnp.concatenate([small_rows[k] for k in order], 0)
    qkv_own, small_own = halving([grad_qkv_t, small_rows], "shard", shard_count, shard_steps)
    joined_b = jnp.concatenate([qkv_own, small_own], 0)
    (joined_b,) = halving([joined_b], "rep", reps, rep_steps)
    total_b = doubling(joined_b.astype(jnp.bfloat16), "rep", reps, rep_steps[::-1])
    down_rows = down_own.shape[0]
    up_rows = up_own.shape[0]
    down_fin = total_a[:down_rows].astype(jnp.float32)
    up_fin = total_a[down_rows : down_rows + up_rows].astype(jnp.float32).T
    out_fin = total_a[down_rows + up_rows :].astype(jnp.float32)
    qkv_fin = total_b[:qkv_rows].astype(jnp.float32).T
    small_flat = total_b[qkv_rows:].reshape(-1).astype(jnp.float32)
    small_fin, offset = [], 0
    for g in smalls:
        width = g.shape[0] // shard_count
        small_fin.append(small_flat[offset : offset + width])
        offset += width
    g1_fin, s1_fin, qb_fin, vb_fin, bo_fin, g2_fin, s2_fin, bu_fin, bd_fin = small_fin
    return (
        outputs.astype(jnp.bfloat16)[None],
        grad_inputs.astype(jnp.bfloat16)[None],
        g1_fin,
        s1_fin,
        qkv_fin,
        qb_fin,
        vb_fin,
        out_fin,
        bo_fin,
        g2_fin,
        s2_fin,
        up_fin,
        bu_fin,
        down_fin,
        bd_fin,
    )


def solution(mesh):
    return jax.shard_map(
        body_inner,
        mesh=mesh,
        in_specs=(
            P(("rep", "shard"), None, None),
            P(("rep", "shard"), None, None),
            P(("rep", "shard"), None, None),
            P("shard"),
            P("shard"),
            P(None, "shard"),
            P("shard"),
            P("shard"),
            P("shard", None),
            P("shard"),
            P("shard"),
            P("shard"),
            P(None, "shard"),
            P("shard"),
            P("shard", None),
            P("shard"),
        ),
        out_specs=(
            P(("rep", "shard"), None, None),
            P(("rep", "shard"), None, None),
            P("shard"),
            P("shard"),
            P(None, "shard"),
            P("shard"),
            P("shard"),
            P("shard", None),
            P("shard"),
            P("shard"),
            P("shard"),
            P(None, "shard"),
            P("shard"),
            P("shard", None),
            P("shard"),
        ),
        check_vma=False,
    )
```

```python
from functools import partial

import jax
import jax.numpy as jnp
from jax import lax
from jax.sharding import PartitionSpec as P


HEADS = 16
HDIM = 64
PROMPT = 256


def normalize(values, gain, shift):
    center = values - jnp.mean(values, -1, keepdims=True)
    spread = jnp.mean(center * center, -1, keepdims=True)
    return center * lax.rsqrt(spread + 1e-05) * gain + shift


def layout(segments):
    micros, row_count = segments.shape
    same_seg = segments[:, :, None] == segments[:, None, :]
    earlier = jnp.arange(row_count)[None, :] < jnp.arange(row_count)[:, None]
    offsets = jnp.sum(jnp.where(same_seg & earlier[None], 1, 0), -1).astype(jnp.int32)
    cont_pos = PROMPT + offsets
    owners = jnp.arange(micros, dtype=jnp.int32)[:, None] * row_count + segments
    positions = jnp.concatenate([jnp.arange(PROMPT, dtype=jnp.int32), cont_pos.reshape(-1)])
    groups = jnp.concatenate([jnp.full((PROMPT,), -1, jnp.int32), owners.reshape(-1)])
    places = jnp.arange(positions.shape[0], dtype=jnp.int32)
    allowed = (places[None, :] <= places[:, None]) & (
        (places[None, :] < PROMPT) | (groups[None, :] == groups[:, None])
    )
    distance = (positions[:, None] - positions[None, :]).astype(jnp.float32)
    return (distance, allowed)


def head_slice(matrix, block):
    block_width = 4 * HDIM
    part = lax.dynamic_slice_in_dim(matrix, block * block_width, block_width, 1)
    return part.reshape(matrix.shape[0], 4, HDIM)


def block_scores(q_part, k_part, block, distance, allowed):
    heads = (block * 4 + jnp.arange(4, dtype=jnp.int32)).astype(jnp.float32)
    slopes = jnp.exp2(-8.0 * (heads + 1.0) / HEADS)
    scores = jnp.einsum(
        "qhd,khd->hqk", q_part, k_part, preferred_element_type=jnp.float32
    ) * HDIM ** (-0.5)
    scores = scores - slopes[:, None, None] * distance[None]
    return jnp.where(allowed[None], scores, -jnp.inf)


def side_by_side(blocks):
    return jnp.transpose(blocks, (1, 0, 2)).reshape(
        blocks.shape[1], blocks.shape[0] * blocks.shape[2]
    )


def attend_forward(queries, key_rows, values, distance, allowed):
    length = queries.shape[0]

    def head_block(block):
        q_part = head_slice(queries, block)
        k_part = head_slice(key_rows, block)
        v_part = head_slice(values, block)
        scores = block_scores(q_part, k_part, block, distance, allowed)
        peak = jnp.max(scores, -1, keepdims=True)
        exps_rel = jnp.exp(scores - peak)
        row_totals = jnp.sum(exps_rel, -1, keepdims=True)
        attn_probs = (exps_rel / row_totals).astype(jnp.bfloat16)
        mixed = jnp.einsum("hqk,khd->qhd", attn_probs, v_part, preferred_element_type=jnp.float32)
        return (mixed.reshape(length, 4 * HDIM), (peak + jnp.log(row_totals))[:, :, 0])

    mixed, log_norms = lax.map(head_block, jnp.arange(HEADS // 4, dtype=jnp.int32))
    return (side_by_side(mixed).astype(jnp.bfloat16), log_norms)


def attend_backward(queries, key_rows, values, grad_mixed, log_norms, distance, allowed):
    length = queries.shape[0]
    scale = HDIM ** (-0.5)

    def head_block(block):
        q_part = head_slice(queries, block)
        k_part = head_slice(key_rows, block)
        v_part = head_slice(values, block)
        g_part = head_slice(grad_mixed, block)
        scores = block_scores(q_part, k_part, block, distance, allowed)
        attn_probs = jnp.exp(scores - log_norms[block][:, :, None])
        grad_probs = jnp.einsum("qhd,khd->hqk", g_part, v_part, preferred_element_type=jnp.float32)
        inner = jnp.sum(attn_probs * grad_probs, -1, keepdims=True)
        grad_scores = (attn_probs * (grad_probs - inner)).astype(jnp.bfloat16)
        grad_q = (
            jnp.einsum("hqk,khd->qhd", grad_scores, k_part, preferred_element_type=jnp.float32)
            * scale
        )
        grad_k = (
            jnp.einsum("hqk,qhd->khd", grad_scores, q_part, preferred_element_type=jnp.float32)
            * scale
        )
        grad_v = jnp.einsum(
            "hqk,qhd->khd",
            attn_probs.astype(jnp.bfloat16),
            g_part,
            preferred_element_type=jnp.float32,
        )
        block_width = 4 * HDIM
        return (
            grad_q.reshape(length, block_width),
            grad_k.reshape(length, block_width),
            grad_v.reshape(length, block_width),
        )

    grad_q, grad_k, grad_v = lax.map(head_block, jnp.arange(HEADS // 4, dtype=jnp.int32))
    return (
        side_by_side(grad_q).astype(jnp.bfloat16),
        side_by_side(grad_k).astype(jnp.bfloat16),
        side_by_side(grad_v).astype(jnp.bfloat16),
    )


def bit_steps(size):
    assert size & (size - 1) == 0
    return [1 << b for b in range(size.bit_length() - 1)]


def chunk_order(size, steps):
    places = []
    for member in range(size):
        place = 0
        for step in steps:
            place = place * 2 + (member // step) % 2
        places.append(place)
    order = [0] * size
    for member, place in enumerate(places):
        order[place] = member
    return order


def reorder_cols(matrix, order):
    pieces = jnp.split(matrix, len(order), 1)
    return jnp.concatenate([pieces[k] for k in order], 1)


def halving(arrays, axis, size, steps):
    index = lax.axis_index(axis)
    for step in steps:
        bit = (index // step) % 2
        keeps, sends = [], []
        for array in arrays:
            pair = array.reshape(2, array.shape[0] // 2, *array.shape[1:])
            keeps.append(lax.dynamic_index_in_dim(pair, bit, 0, keepdims=False))
            sends.append(
                lax.dynamic_index_in_dim(pair, 1 - bit, 0, keepdims=False).astype(jnp.bfloat16)
            )
        got = lax.ppermute(jnp.concatenate(sends, 0), axis, [(a, a ^ step) for a in range(size)])
        arrays, offset = [], 0
        for keep in keeps:
            arrays.append(keep + got[offset : offset + keep.shape[0]].astype(jnp.float32))
            offset += keep.shape[0]
    return arrays


def direct_reduce(buf, axis, size):
    index = lax.axis_index(axis)
    chunks = buf.reshape(size, buf.shape[0] // size, *buf.shape[1:])
    total = lax.dynamic_index_in_dim(chunks, index, 0, keepdims=False)
    for shift in range(1, size):
        send = lax.dynamic_index_in_dim(chunks, (index + shift) % size, 0, keepdims=False)
        got = lax.ppermute(
            send.astype(jnp.bfloat16), axis, [(a, (a + shift) % size) for a in range(size)]
        )
        total = total + got.astype(jnp.float32)
    mine = total.astype(jnp.bfloat16)
    result = jnp.zeros((size, *mine.shape), jnp.bfloat16)
    result = lax.dynamic_update_index_in_dim(result, mine, index, 0)
    for shift in range(1, size):
        got = lax.ppermute(mine, axis, [(a, (a + shift) % size) for a in range(size)])
        result = lax.dynamic_update_index_in_dim(result, got, (index - shift) % size, 0)
    return result.reshape(buf.shape)


def gather_small(pieces):
    packed = jnp.concatenate(pieces)
    shards = lax.all_gather(packed, "shard", axis=0, tiled=False)
    fulls, offset = [], 0
    for piece in pieces:
        width = piece.shape[0]
        fulls.append(shards[:, offset : offset + width].reshape(-1))
        offset += width
    return fulls


def body_inner(
    tokens,
    cont_segment,
    cotangent,
    ln1_gain,
    ln1_bias,
    w_qkv,
    q_bias,
    v_bias,
    w_out,
    b_out,
    ln2_gain,
    ln2_bias,
    w_up,
    b_up,
    w_down,
    b_down,
):
    shard_count = lax.psum(1, "shard")
    full_g1, full_s1, full_qb, full_vb, full_bo, full_g2, full_s2, full_bu, full_bd = gather_small(
        [ln1_gain, ln1_bias, q_bias, v_bias, b_out, ln2_gain, ln2_bias, b_up, b_down]
    )
    full_qkv = lax.all_gather(w_qkv, "shard", axis=1, tiled=True)
    full_out = lax.all_gather(w_out, "shard", axis=0, tiled=True)
    full_up = lax.all_gather(w_up, "shard", axis=1, tiled=True)
    full_down = lax.all_gather(w_down, "shard", axis=0, tiled=True)
    inputs = tokens[0].astype(jnp.float32)
    _, model_width = inputs.shape
    distance, allowed = layout(cont_segment[0])
    normed = normalize(inputs, full_g1.astype(jnp.float32), full_s1.astype(jnp.float32)).astype(
        jnp.bfloat16
    )
    projected = jnp.dot(normed, full_qkv, preferred_element_type=jnp.float32)
    queries = (projected[:, :model_width] + full_qb.astype(jnp.float32)).astype(jnp.bfloat16)
    key_rows = projected[:, model_width : 2 * model_width].astype(jnp.bfloat16)
    values = (projected[:, 2 * model_width :] + full_vb.astype(jnp.float32)).astype(jnp.bfloat16)
    mixed, log_norms = attend_forward(queries, key_rows, values, distance, allowed)
    branch = jnp.dot(mixed, full_out, preferred_element_type=jnp.float32) + full_bo.astype(
        jnp.float32
    )
    middle = inputs + branch
    normed_two = normalize(middle, full_g2.astype(jnp.float32), full_s2.astype(jnp.float32)).astype(
        jnp.bfloat16
    )
    pre_act = jnp.dot(normed_two, full_up, preferred_element_type=jnp.float32) + full_bu.astype(
        jnp.float32
    )
    activated = jax.nn.gelu(pre_act, approximate=True).astype(jnp.bfloat16)
    outputs = middle + (
        jnp.dot(activated, full_down, preferred_element_type=jnp.float32)
        + full_bd.astype(jnp.float32)
    )
    back_g1, back_qkv, back_out, back_g2, back_up, back_down = (
        full_g1, full_qkv, full_out, full_g2, full_up, full_down
    )
    shard_steps = bit_steps(shard_count)
    order = chunk_order(shard_count, shard_steps)
    cot_low = cotangent[0]
    cot_full = cot_low.astype(jnp.float32)
    zero_shift = jnp.zeros((model_width,), jnp.float32)
    grad_bd = jnp.sum(cot_full, 0)
    grad_act = jnp.einsum("to,fo->tf", cot_low, back_down, preferred_element_type=jnp.float32)
    _, gelu_pull = jax.vjp(partial(jax.nn.gelu, approximate=True), pre_act)
    grad_pre = gelu_pull(grad_act)[0].astype(jnp.bfloat16)
    grad_bu = jnp.sum(grad_pre.astype(jnp.float32), 0)
    grad_down = jnp.einsum(
        "tf,to->fo", reorder_cols(activated, order), cot_low, preferred_element_type=jnp.float32
    )
    (down_own,) = halving([grad_down], "shard", shard_count, shard_steps)
    total_a1 = lax.psum(down_own.astype(jnp.bfloat16), "rep")
    grad_up_t = jnp.einsum(
        "tf,ti->fi", reorder_cols(grad_pre, order), normed_two, preferred_element_type=jnp.float32
    )
    grad_normed_two = jnp.einsum("tf,if->ti", grad_pre, back_up, preferred_element_type=jnp.float32)
    _, norm_pull_two = jax.vjp(normalize, middle, back_g2.astype(jnp.float32), zero_shift)
    grad_mid_part, grad_g2, grad_s2 = norm_pull_two(grad_normed_two)
    grad_middle = cot_full + grad_mid_part
    grad_branch = grad_middle.astype(jnp.bfloat16)
    grad_bo = jnp.sum(grad_branch.astype(jnp.float32), 0)
    grad_mixed = jnp.einsum(
        "to,io->ti", grad_branch, back_out, preferred_element_type=jnp.float32
    ).astype(jnp.bfloat16)
    grad_out = jnp.einsum(
        "ti,to->io", reorder_cols(mixed, order), grad_branch, preferred_element_type=jnp.float32
    )
    up_own, out_own = halving([grad_up_t, grad_out], "shard", shard_count, shard_steps)
    owned_a = [up_own, out_own]
    joined_a = jnp.concatenate([o.astype(jnp.bfloat16) for o in owned_a], 0)
    total_a1, joined_a = lax.optimization_barrier((total_a1, joined_a))
    total_a = lax.psum(joined_a, "rep")
    grad_q, grad_k, grad_v = attend_backward(
        queries, key_rows, values, grad_mixed, log_norms, distance, allowed
    )
    grad_proj = jnp.concatenate([grad_q, grad_k, grad_v], 1)
    grad_qb = jnp.sum(grad_q.astype(jnp.float32), 0)
    grad_vb = jnp.sum(grad_v.astype(jnp.float32), 0)
    grad_normed = jnp.einsum("tc,ic->ti", grad_proj, back_qkv, preferred_element_type=jnp.float32)
    _, norm_pull_one = jax.vjp(normalize, inputs, back_g1.astype(jnp.float32), zero_shift)
    grad_in_part, grad_g1, grad_s1 = norm_pull_one(grad_normed)
    grad_inputs = grad_middle + grad_in_part
    grad_qkv_t = jnp.einsum(
        "tc,ti->ci", reorder_cols(grad_proj, order), normed, preferred_element_type=jnp.float32
    )
    smalls = [grad_g1, grad_s1, grad_qb, grad_vb, grad_bo, grad_g2, grad_s2, grad_bu, grad_bd]
    reps = lax.psum(1, "rep")
    qkv_rows = grad_qkv_t.shape[0] // shard_count
    small_rows = jnp.concatenate([g.reshape(shard_count, -1) for g in smalls], 1)
    small_rows = small_rows.reshape(shard_count, -1, model_width)
    pad_to = small_rows.shape[1] + (-(qkv_rows + small_rows.shape[1]) % (8 * reps))
    small_rows = jnp.pad(small_rows, ((0, 0), (0, pad_to - small_rows.shape[1]), (0, 0)))
    small_rows = jnp.concatenate([small_rows[k] for k in order], 0)
    qkv_own, small_own = halving([grad_qkv_t, small_rows], "shard", shard_count, shard_steps)
    joined_b = jnp.concatenate([qkv_own, small_own], 0)
    total_b = direct_reduce(joined_b, "rep", reps)
    up_rows = up_own.shape[0]
    down_fin = total_a1.astype(jnp.float32)
    up_fin = total_a[:up_rows].astype(jnp.float32).T
    out_fin = total_a[up_rows:].astype(jnp.float32)
    qkv_fin = total_b[:qkv_rows].astype(jnp.float32).T
    small_flat = total_b[qkv_rows:].reshape(-1).astype(jnp.float32)
    small_fin, offset = [], 0
    for g in smalls:
        width = g.shape[0] // shard_count
        small_fin.append(small_flat[offset : offset + width])
        offset += width
    g1_fin, s1_fin, qb_fin, vb_fin, bo_fin, g2_fin, s2_fin, bu_fin, bd_fin = small_fin
    return (
        outputs.astype(jnp.bfloat16)[None],
        grad_inputs.astype(jnp.bfloat16)[None],
        g1_fin,
        s1_fin,
        qkv_fin,
        qb_fin,
        vb_fin,
        out_fin,
        bo_fin,
        g2_fin,
        s2_fin,
        up_fin,
        bu_fin,
        down_fin,
        bd_fin,
    )


def solution(mesh):
    return jax.shard_map(
        body_inner,
        mesh=mesh,
        in_specs=(
            P(("rep", "shard"), None, None),
            P(("rep", "shard"), None, None),
            P(("rep", "shard"), None, None),
            P("shard"),
            P("shard"),
            P(None, "shard"),
            P("shard"),
            P("shard"),
            P("shard", None),
            P("shard"),
            P("shard"),
            P("shard"),
            P(None, "shard"),
            P("shard"),
            P("shard", None),
            P("shard"),
        ),
        out_specs=(
            P(("rep", "shard"), None, None),
            P(("rep", "shard"), None, None),
            P("shard"),
            P("shard"),
            P(None, "shard"),
            P("shard"),
            P("shard"),
            P("shard", None),
            P("shard"),
            P("shard"),
            P("shard"),
            P(None, "shard"),
            P("shard"),
            P("shard", None),
            P("shard"),
        ),
        check_vma=False,
    )
```

```python
from functools import partial

import jax
import jax.numpy as jnp
from jax import lax
from jax.sharding import PartitionSpec as P


HEADS = 16
HDIM = 64
PROMPT = 256


def normalize(values, gain, shift):
    center = values - jnp.mean(values, -1, keepdims=True)
    spread = jnp.mean(center * center, -1, keepdims=True)
    return center * lax.rsqrt(spread + 1e-05) * gain + shift


def layout(segments):
    micros, row_count = segments.shape
    same_seg = segments[:, :, None] == segments[:, None, :]
    earlier = jnp.arange(row_count)[None, :] < jnp.arange(row_count)[:, None]
    offsets = jnp.sum(jnp.where(same_seg & earlier[None], 1, 0), -1).astype(jnp.int32)
    cont_pos = PROMPT + offsets
    owners = jnp.arange(micros, dtype=jnp.int32)[:, None] * row_count + segments
    positions = jnp.concatenate([jnp.arange(PROMPT, dtype=jnp.int32), cont_pos.reshape(-1)])
    groups = jnp.concatenate([jnp.full((PROMPT,), -1, jnp.int32), owners.reshape(-1)])
    places = jnp.arange(positions.shape[0], dtype=jnp.int32)
    allowed = (places[None, :] <= places[:, None]) & (
        (places[None, :] < PROMPT) | (groups[None, :] == groups[:, None])
    )
    distance = (positions[:, None] - positions[None, :]).astype(jnp.float32)
    return (distance, allowed)


def head_slice(matrix, block):
    block_width = 4 * HDIM
    part = lax.dynamic_slice_in_dim(matrix, block * block_width, block_width, 1)
    return part.reshape(matrix.shape[0], 4, HDIM)


def block_scores(q_part, k_part, block, distance, allowed):
    heads = (block * 4 + jnp.arange(4, dtype=jnp.int32)).astype(jnp.float32)
    slopes = jnp.exp2(-8.0 * (heads + 1.0) / HEADS)
    scores = jnp.einsum(
        "qhd,khd->hqk", q_part, k_part, preferred_element_type=jnp.float32
    ) * HDIM ** (-0.5)
    scores = scores - slopes[:, None, None] * distance[None]
    return jnp.where(allowed[None], scores, -jnp.inf)


def side_by_side(blocks):
    return jnp.transpose(blocks, (1, 0, 2)).reshape(
        blocks.shape[1], blocks.shape[0] * blocks.shape[2]
    )


def attend_forward(queries, key_rows, values, distance, allowed):
    length = queries.shape[0]

    def head_block(block):
        q_part = head_slice(queries, block)
        k_part = head_slice(key_rows, block)
        v_part = head_slice(values, block)
        scores = block_scores(q_part, k_part, block, distance, allowed)
        peak = jnp.max(scores, -1, keepdims=True)
        exps_rel = jnp.exp(scores - peak)
        row_totals = jnp.sum(exps_rel, -1, keepdims=True)
        attn_probs = (exps_rel / row_totals).astype(jnp.bfloat16)
        mixed = jnp.einsum("hqk,khd->qhd", attn_probs, v_part, preferred_element_type=jnp.float32)
        return (mixed.reshape(length, 4 * HDIM), (peak + jnp.log(row_totals))[:, :, 0])

    mixed, log_norms = lax.map(head_block, jnp.arange(HEADS // 4, dtype=jnp.int32))
    return (side_by_side(mixed).astype(jnp.bfloat16), log_norms)


def attend_backward(queries, key_rows, values, grad_mixed, log_norms, distance, allowed):
    length = queries.shape[0]
    scale = HDIM ** (-0.5)

    def head_block(block):
        q_part = head_slice(queries, block)
        k_part = head_slice(key_rows, block)
        v_part = head_slice(values, block)
        g_part = head_slice(grad_mixed, block)
        scores = block_scores(q_part, k_part, block, distance, allowed)
        attn_probs = jnp.exp(scores - log_norms[block][:, :, None])
        grad_probs = jnp.einsum("qhd,khd->hqk", g_part, v_part, preferred_element_type=jnp.float32)
        inner = jnp.sum(attn_probs * grad_probs, -1, keepdims=True)
        grad_scores = (attn_probs * (grad_probs - inner)).astype(jnp.bfloat16)
        grad_q = (
            jnp.einsum("hqk,khd->qhd", grad_scores, k_part, preferred_element_type=jnp.float32)
            * scale
        )
        grad_k = (
            jnp.einsum("hqk,qhd->khd", grad_scores, q_part, preferred_element_type=jnp.float32)
            * scale
        )
        grad_v = jnp.einsum(
            "hqk,qhd->khd",
            attn_probs.astype(jnp.bfloat16),
            g_part,
            preferred_element_type=jnp.float32,
        )
        block_width = 4 * HDIM
        return (
            grad_q.reshape(length, block_width),
            grad_k.reshape(length, block_width),
            grad_v.reshape(length, block_width),
        )

    grad_q, grad_k, grad_v = lax.map(head_block, jnp.arange(HEADS // 4, dtype=jnp.int32))
    return (
        side_by_side(grad_q).astype(jnp.bfloat16),
        side_by_side(grad_k).astype(jnp.bfloat16),
        side_by_side(grad_v).astype(jnp.bfloat16),
    )


def bit_steps(size):
    assert size & (size - 1) == 0
    return [1 << b for b in range(size.bit_length() - 1)]


def chunk_order(size, steps):
    places = []
    for member in range(size):
        place = 0
        for step in steps:
            place = place * 2 + (member // step) % 2
        places.append(place)
    order = [0] * size
    for member, place in enumerate(places):
        order[place] = member
    return order


def reorder_cols(matrix, order):
    pieces = jnp.split(matrix, len(order), 1)
    return jnp.concatenate([pieces[k] for k in order], 1)


def halving(arrays, axis, size, steps):
    index = lax.axis_index(axis)
    for step in steps:
        bit = (index // step) % 2
        keeps, sends = [], []
        for array in arrays:
            pair = array.reshape(2, array.shape[0] // 2, *array.shape[1:])
            keeps.append(lax.dynamic_index_in_dim(pair, bit, 0, keepdims=False))
            sends.append(
                lax.dynamic_index_in_dim(pair, 1 - bit, 0, keepdims=False).astype(jnp.bfloat16)
            )
        got = lax.ppermute(jnp.concatenate(sends, 0), axis, [(a, a ^ step) for a in range(size)])
        arrays, offset = [], 0
        for keep in keeps:
            arrays.append(keep + got[offset : offset + keep.shape[0]].astype(jnp.float32))
            offset += keep.shape[0]
    return arrays


def direct_reduce(buf, axis, size):
    index = lax.axis_index(axis)
    chunks = buf.reshape(size, buf.shape[0] // size, *buf.shape[1:])
    total = lax.dynamic_index_in_dim(chunks, index, 0, keepdims=False)
    for shift in range(1, size):
        send = lax.dynamic_index_in_dim(chunks, (index + shift) % size, 0, keepdims=False)
        got = lax.ppermute(
            send.astype(jnp.bfloat16), axis, [(a, (a + shift) % size) for a in range(size)]
        )
        total = total + got.astype(jnp.float32)
    mine = total.astype(jnp.bfloat16)
    result = jnp.zeros((size, *mine.shape), jnp.bfloat16)
    result = lax.dynamic_update_index_in_dim(result, mine, index, 0)
    for shift in range(1, size):
        got = lax.ppermute(mine, axis, [(a, (a + shift) % size) for a in range(size)])
        result = lax.dynamic_update_index_in_dim(result, got, (index - shift) % size, 0)
    return result.reshape(buf.shape)


def gather_pieces(piece, axis, size, steps, dim):
    index = lax.axis_index(axis)
    results = []
    buf = piece
    for step in steps:
        low = (index // step) % 2 == 0
        got = lax.ppermute(buf, axis, [(a, a ^ step) for a in range(size)])
        results.append(got)
        buf = jnp.concatenate([jnp.where(low, buf, got), jnp.where(low, got, buf)], dim)
    return buf, results[0]


def unpermute(full, order, dim):
    pieces = jnp.split(full, len(order), dim)
    return jnp.concatenate([pieces[order.index(k)] for k in range(len(order))], dim)


def gather_small(pieces):
    packed = jnp.concatenate(pieces)
    shards = lax.all_gather(packed, "shard", axis=0, tiled=False)
    fulls, offset = [], 0
    for piece in pieces:
        width = piece.shape[0]
        fulls.append(shards[:, offset : offset + width].reshape(-1))
        offset += width
    return fulls


def body_inner(
    tokens,
    cont_segment,
    cotangent,
    ln1_gain,
    ln1_bias,
    w_qkv,
    q_bias,
    v_bias,
    w_out,
    b_out,
    ln2_gain,
    ln2_bias,
    w_up,
    b_up,
    w_down,
    b_down,
):
    shard_count = lax.psum(1, "shard")
    full_g1, full_s1, full_qb, full_vb, full_bo, full_g2, full_s2, full_bu, full_bd = gather_small(
        [ln1_gain, ln1_bias, q_bias, v_bias, b_out, ln2_gain, ln2_bias, b_up, b_down]
    )
    shard_steps = bit_steps(shard_count)
    order = chunk_order(shard_count, shard_steps)
    gather_steps = shard_steps[::-1]
    full_qkv, first = gather_pieces(w_qkv, "shard", shard_count, gather_steps, 1)
    first, w_out = lax.optimization_barrier((first, w_out))
    full_out, first = gather_pieces(w_out, "shard", shard_count, gather_steps, 0)
    first, full_qkv, w_up = lax.optimization_barrier((first, full_qkv, w_up))
    full_up, first = gather_pieces(w_up, "shard", shard_count, gather_steps, 1)
    first, full_out, w_down = lax.optimization_barrier((first, full_out, w_down))
    full_down, first = gather_pieces(w_down, "shard", shard_count, gather_steps, 0)
    full_qkv = unpermute(full_qkv, order, 1)
    full_out = unpermute(full_out, order, 0)
    full_bu = reorder_cols(full_bu.reshape(1, -1), order).reshape(-1)
    inputs = tokens[0].astype(jnp.float32)
    _, model_width = inputs.shape
    distance, allowed = layout(cont_segment[0])
    normed = normalize(inputs, full_g1.astype(jnp.float32), full_s1.astype(jnp.float32)).astype(
        jnp.bfloat16
    )
    projected = jnp.dot(normed, full_qkv, preferred_element_type=jnp.float32)
    queries = (projected[:, :model_width] + full_qb.astype(jnp.float32)).astype(jnp.bfloat16)
    key_rows = projected[:, model_width : 2 * model_width].astype(jnp.bfloat16)
    values = (projected[:, 2 * model_width :] + full_vb.astype(jnp.float32)).astype(jnp.bfloat16)
    mixed, log_norms = attend_forward(queries, key_rows, values, distance, allowed)
    branch = jnp.dot(mixed, full_out, preferred_element_type=jnp.float32) + full_bo.astype(
        jnp.float32
    )
    middle = inputs + branch
    normed_two = normalize(middle, full_g2.astype(jnp.float32), full_s2.astype(jnp.float32)).astype(
        jnp.bfloat16
    )
    pre_act = jnp.dot(normed_two, full_up, preferred_element_type=jnp.float32) + full_bu.astype(
        jnp.float32
    )
    activated = jax.nn.gelu(pre_act, approximate=True).astype(jnp.bfloat16)
    outputs = middle + (
        jnp.dot(activated, full_down, preferred_element_type=jnp.float32)
        + full_bd.astype(jnp.float32)
    )
    back_g1, back_qkv, back_out, back_g2, back_up, back_down = (
        full_g1, full_qkv, full_out, full_g2, full_up, full_down
    )
    cot_low = cotangent[0]
    cot_full = cot_low.astype(jnp.float32)
    zero_shift = jnp.zeros((model_width,), jnp.float32)
    grad_bd = jnp.sum(cot_full, 0)
    grad_act = jnp.einsum("to,fo->tf", cot_low, back_down, preferred_element_type=jnp.float32)
    _, gelu_pull = jax.vjp(partial(jax.nn.gelu, approximate=True), pre_act)
    grad_pre = gelu_pull(grad_act)[0].astype(jnp.bfloat16)
    grad_bu = jnp.sum(grad_pre.astype(jnp.float32), 0).reshape(1, -1)
    grad_bu = unpermute(grad_bu, order, 1).reshape(-1)
    grad_down = jnp.einsum(
        "tf,to->fo", activated, cot_low, preferred_element_type=jnp.float32
    )
    (down_own,) = halving([grad_down], "shard", shard_count, shard_steps)
    total_a1 = lax.psum(down_own.astype(jnp.bfloat16), "rep")
    grad_up_t = jnp.einsum(
        "tf,ti->fi", grad_pre, normed_two, preferred_element_type=jnp.float32
    )
    grad_normed_two = jnp.einsum("tf,if->ti", grad_pre, back_up, preferred_element_type=jnp.float32)
    _, norm_pull_two = jax.vjp(normalize, middle, back_g2.astype(jnp.float32), zero_shift)
    grad_mid_part, grad_g2, grad_s2 = norm_pull_two(grad_normed_two)
    grad_middle = cot_full + grad_mid_part
    grad_branch = grad_middle.astype(jnp.bfloat16)
    grad_bo = jnp.sum(grad_branch.astype(jnp.float32), 0)
    grad_mixed = jnp.einsum(
        "to,io->ti", grad_branch, back_out, preferred_element_type=jnp.float32
    ).astype(jnp.bfloat16)
    grad_out = jnp.einsum(
        "ti,to->io", reorder_cols(mixed, order), grad_branch, preferred_element_type=jnp.float32
    )
    up_own, out_own = halving([grad_up_t, grad_out], "shard", shard_count, shard_steps)
    owned_a = [up_own, out_own]
    joined_a = jnp.concatenate([o.astype(jnp.bfloat16) for o in owned_a], 0)
    total_a1, joined_a = lax.optimization_barrier((total_a1, joined_a))
    total_a = lax.psum(joined_a, "rep")
    grad_q, grad_k, grad_v = attend_backward(
        queries, key_rows, values, grad_mixed, log_norms, distance, allowed
    )
    grad_proj = jnp.concatenate([grad_q, grad_k, grad_v], 1)
    grad_qb = jnp.sum(grad_q.astype(jnp.float32), 0)
    grad_vb = jnp.sum(grad_v.astype(jnp.float32), 0)
    grad_normed = jnp.einsum("tc,ic->ti", grad_proj, back_qkv, preferred_element_type=jnp.float32)
    _, norm_pull_one = jax.vjp(normalize, inputs, back_g1.astype(jnp.float32), zero_shift)
    grad_in_part, grad_g1, grad_s1 = norm_pull_one(grad_normed)
    grad_inputs = grad_middle + grad_in_part
    grad_qkv_t = jnp.einsum(
        "tc,ti->ci", reorder_cols(grad_proj, order), normed, preferred_element_type=jnp.float32
    )
    smalls = [grad_g1, grad_s1, grad_qb, grad_vb, grad_bo, grad_g2, grad_s2, grad_bu, grad_bd]
    reps = lax.psum(1, "rep")
    qkv_rows = grad_qkv_t.shape[0] // shard_count
    small_rows = jnp.concatenate([g.reshape(shard_count, -1) for g in smalls], 1)
    small_rows = small_rows.reshape(shard_count, -1, model_width)
    pad_to = small_rows.shape[1] + (-(qkv_rows + small_rows.shape[1]) % (8 * reps))
    small_rows = jnp.pad(small_rows, ((0, 0), (0, pad_to - small_rows.shape[1]), (0, 0)))
    small_rows = jnp.concatenate([small_rows[k] for k in order], 0)
    qkv_own, small_own = halving([grad_qkv_t, small_rows], "shard", shard_count, shard_steps)
    joined_b = jnp.concatenate([qkv_own, small_own], 0)
    total_b = direct_reduce(joined_b, "rep", reps)
    up_rows = up_own.shape[0]
    down_fin = total_a1.astype(jnp.float32)
    up_fin = total_a[:up_rows].astype(jnp.float32).T
    out_fin = total_a[up_rows:].astype(jnp.float32)
    qkv_fin = total_b[:qkv_rows].astype(jnp.float32).T
    small_flat = total_b[qkv_rows:].reshape(-1).astype(jnp.float32)
    small_fin, offset = [], 0
    for g in smalls:
        width = g.shape[0] // shard_count
        small_fin.append(small_flat[offset : offset + width])
        offset += width
    g1_fin, s1_fin, qb_fin, vb_fin, bo_fin, g2_fin, s2_fin, bu_fin, bd_fin = small_fin
    return (
        outputs.astype(jnp.bfloat16)[None],
        grad_inputs.astype(jnp.bfloat16)[None],
        g1_fin,
        s1_fin,
        qkv_fin,
        qb_fin,
        vb_fin,
        out_fin,
        bo_fin,
        g2_fin,
        s2_fin,
        up_fin,
        bu_fin,
        down_fin,
        bd_fin,
    )


def solution(mesh):
    return jax.shard_map(
        body_inner,
        mesh=mesh,
        in_specs=(
            P(("rep", "shard"), None, None),
            P(("rep", "shard"), None, None),
            P(("rep", "shard"), None, None),
            P("shard"),
            P("shard"),
            P(None, "shard"),
            P("shard"),
            P("shard"),
            P("shard", None),
            P("shard"),
            P("shard"),
            P("shard"),
            P(None, "shard"),
            P("shard"),
            P("shard", None),
            P("shard"),
        ),
        out_specs=(
            P(("rep", "shard"), None, None),
            P(("rep", "shard"), None, None),
            P("shard"),
            P("shard"),
            P(None, "shard"),
            P("shard"),
            P("shard"),
            P("shard", None),
            P("shard"),
            P("shard"),
            P("shard"),
            P(None, "shard"),
            P("shard"),
            P("shard", None),
            P("shard"),
        ),
        check_vma=False,
    )
```

```python
from functools import partial

import jax
import jax.numpy as jnp
from jax import lax
from jax.sharding import PartitionSpec as P


HEADS = 16
HDIM = 64
PROMPT = 256


def normalize(values, gain, shift):
    center = values - jnp.mean(values, -1, keepdims=True)
    spread = jnp.mean(center * center, -1, keepdims=True)
    return center * lax.rsqrt(spread + 1e-05) * gain + shift


def layout(segments):
    micros, row_count = segments.shape
    same_seg = segments[:, :, None] == segments[:, None, :]
    earlier = jnp.arange(row_count)[None, :] < jnp.arange(row_count)[:, None]
    offsets = jnp.sum(jnp.where(same_seg & earlier[None], 1, 0), -1).astype(jnp.int32)
    cont_pos = PROMPT + offsets
    owners = jnp.arange(micros, dtype=jnp.int32)[:, None] * row_count + segments
    positions = jnp.concatenate([jnp.arange(PROMPT, dtype=jnp.int32), cont_pos.reshape(-1)])
    groups = jnp.concatenate([jnp.full((PROMPT,), -1, jnp.int32), owners.reshape(-1)])
    places = jnp.arange(positions.shape[0], dtype=jnp.int32)
    allowed = (places[None, :] <= places[:, None]) & (
        (places[None, :] < PROMPT) | (groups[None, :] == groups[:, None])
    )
    distance = (positions[:, None] - positions[None, :]).astype(jnp.float32)
    return (distance, allowed)


def head_slice(matrix, block):
    block_width = 4 * HDIM
    part = lax.dynamic_slice_in_dim(matrix, block * block_width, block_width, 1)
    return part.reshape(matrix.shape[0], 4, HDIM)


def block_scores(q_part, k_part, block, distance, allowed):
    heads = (block * 4 + jnp.arange(4, dtype=jnp.int32)).astype(jnp.float32)
    slopes = jnp.exp2(-8.0 * (heads + 1.0) / HEADS)
    scores = jnp.einsum(
        "qhd,khd->hqk", q_part, k_part, preferred_element_type=jnp.float32
    ) * HDIM ** (-0.5)
    scores = scores - slopes[:, None, None] * distance[None]
    return jnp.where(allowed[None], scores, -jnp.inf)


def side_by_side(blocks):
    return jnp.transpose(blocks, (1, 0, 2)).reshape(
        blocks.shape[1], blocks.shape[0] * blocks.shape[2]
    )


def attend_forward(queries, key_rows, values, distance, allowed):
    length = queries.shape[0]

    def head_block(block):
        q_part = head_slice(queries, block)
        k_part = head_slice(key_rows, block)
        v_part = head_slice(values, block)
        scores = block_scores(q_part, k_part, block, distance, allowed)
        peak = jnp.max(scores, -1, keepdims=True)
        exps_rel = jnp.exp(scores - peak)
        row_totals = jnp.sum(exps_rel, -1, keepdims=True)
        attn_probs = (exps_rel / row_totals).astype(jnp.bfloat16)
        mixed = jnp.einsum("hqk,khd->qhd", attn_probs, v_part, preferred_element_type=jnp.float32)
        return (mixed.reshape(length, 4 * HDIM), (peak + jnp.log(row_totals))[:, :, 0])

    blocks = [head_block(block) for block in range(HEADS // 4)]
    mixed = jnp.stack([b[0] for b in blocks])
    log_norms = jnp.stack([b[1] for b in blocks])
    return (side_by_side(mixed).astype(jnp.bfloat16), log_norms)


def attend_backward(queries, key_rows, values, grad_mixed, log_norms, distance, allowed):
    length = queries.shape[0]
    scale = HDIM ** (-0.5)

    def head_block(block):
        q_part = head_slice(queries, block)
        k_part = head_slice(key_rows, block)
        v_part = head_slice(values, block)
        g_part = head_slice(grad_mixed, block)
        scores = block_scores(q_part, k_part, block, distance, allowed)
        attn_probs = jnp.exp(scores - log_norms[block][:, :, None])
        grad_probs = jnp.einsum("qhd,khd->hqk", g_part, v_part, preferred_element_type=jnp.float32)
        inner = jnp.sum(attn_probs * grad_probs, -1, keepdims=True)
        grad_scores = (attn_probs * (grad_probs - inner)).astype(jnp.bfloat16)
        grad_q = (
            jnp.einsum("hqk,khd->qhd", grad_scores, k_part, preferred_element_type=jnp.float32)
            * scale
        )
        grad_k = (
            jnp.einsum("hqk,qhd->khd", grad_scores, q_part, preferred_element_type=jnp.float32)
            * scale
        )
        grad_v = jnp.einsum(
            "hqk,qhd->khd",
            attn_probs.astype(jnp.bfloat16),
            g_part,
            preferred_element_type=jnp.float32,
        )
        block_width = 4 * HDIM
        return (
            grad_q.reshape(length, block_width),
            grad_k.reshape(length, block_width),
            grad_v.reshape(length, block_width),
        )

    blocks = [head_block(block) for block in range(HEADS // 4)]
    grad_q, grad_k, grad_v = (jnp.stack([b[i] for b in blocks]) for i in range(3))
    return (
        side_by_side(grad_q).astype(jnp.bfloat16),
        side_by_side(grad_k).astype(jnp.bfloat16),
        side_by_side(grad_v).astype(jnp.bfloat16),
    )


def bit_steps(size):
    assert size & (size - 1) == 0
    return [1 << b for b in range(size.bit_length() - 1)]


def chunk_order(size, steps):
    places = []
    for member in range(size):
        place = 0
        for step in steps:
            place = place * 2 + (member // step) % 2
        places.append(place)
    order = [0] * size
    for member, place in enumerate(places):
        order[place] = member
    return order


def reorder_cols(matrix, order):
    pieces = jnp.split(matrix, len(order), 1)
    return jnp.concatenate([pieces[k] for k in order], 1)


def halving(arrays, axis, size, steps):
    index = lax.axis_index(axis)
    for step in steps:
        bit = (index // step) % 2
        keeps, sends = [], []
        for array in arrays:
            pair = array.reshape(2, array.shape[0] // 2, *array.shape[1:])
            keeps.append(lax.dynamic_index_in_dim(pair, bit, 0, keepdims=False))
            sends.append(
                lax.dynamic_index_in_dim(pair, 1 - bit, 0, keepdims=False).astype(jnp.bfloat16)
            )
        got = lax.ppermute(jnp.concatenate(sends, 0), axis, [(a, a ^ step) for a in range(size)])
        arrays, offset = [], 0
        for keep in keeps:
            arrays.append(keep + got[offset : offset + keep.shape[0]].astype(jnp.float32))
            offset += keep.shape[0]
    return arrays


def direct_reduce(buf, axis, size):
    index = lax.axis_index(axis)
    chunks = buf.reshape(size, buf.shape[0] // size, *buf.shape[1:])
    total = lax.dynamic_index_in_dim(chunks, index, 0, keepdims=False)
    for shift in range(1, size):
        send = lax.dynamic_index_in_dim(chunks, (index + shift) % size, 0, keepdims=False)
        got = lax.ppermute(
            send.astype(jnp.bfloat16), axis, [(a, (a + shift) % size) for a in range(size)]
        )
        total = total + got.astype(jnp.float32)
    mine = total.astype(jnp.bfloat16)
    result = jnp.zeros((size, *mine.shape), jnp.bfloat16)
    result = lax.dynamic_update_index_in_dim(result, mine, index, 0)
    for shift in range(1, size):
        got = lax.ppermute(mine, axis, [(a, (a + shift) % size) for a in range(size)])
        result = lax.dynamic_update_index_in_dim(result, got, (index - shift) % size, 0)
    return result.reshape(buf.shape)


def gather_small(pieces):
    packed = jnp.concatenate(pieces)
    shards = lax.all_gather(packed, "shard", axis=0, tiled=False)
    fulls, offset = [], 0
    for piece in pieces:
        width = piece.shape[0]
        fulls.append(shards[:, offset : offset + width].reshape(-1))
        offset += width
    return fulls


def body_inner(
    tokens,
    cont_segment,
    cotangent,
    ln1_gain,
    ln1_bias,
    w_qkv,
    q_bias,
    v_bias,
    w_out,
    b_out,
    ln2_gain,
    ln2_bias,
    w_up,
    b_up,
    w_down,
    b_down,
):
    shard_count = lax.psum(1, "shard")
    full_g1, full_s1, full_qb, full_vb, full_bo, full_g2, full_s2, full_bu, full_bd = gather_small(
        [ln1_gain, ln1_bias, q_bias, v_bias, b_out, ln2_gain, ln2_bias, b_up, b_down]
    )
    full_qkv = lax.all_gather(w_qkv, "shard", axis=1, tiled=True)
    full_out = lax.all_gather(w_out, "shard", axis=0, tiled=True)
    full_up = lax.all_gather(w_up, "shard", axis=1, tiled=True)
    full_down = lax.all_gather(w_down, "shard", axis=0, tiled=True)
    inputs = tokens[0].astype(jnp.float32)
    _, model_width = inputs.shape
    distance, allowed = layout(cont_segment[0])
    normed = normalize(inputs, full_g1.astype(jnp.float32), full_s1.astype(jnp.float32)).astype(
        jnp.bfloat16
    )
    projected = jnp.dot(normed, full_qkv, preferred_element_type=jnp.float32)
    queries = (projected[:, :model_width] + full_qb.astype(jnp.float32)).astype(jnp.bfloat16)
    key_rows = projected[:, model_width : 2 * model_width].astype(jnp.bfloat16)
    values = (projected[:, 2 * model_width :] + full_vb.astype(jnp.float32)).astype(jnp.bfloat16)
    mixed, log_norms = attend_forward(queries, key_rows, values, distance, allowed)
    branch = jnp.dot(mixed, full_out, preferred_element_type=jnp.float32) + full_bo.astype(
        jnp.float32
    )
    middle = inputs + branch
    normed_two = normalize(middle, full_g2.astype(jnp.float32), full_s2.astype(jnp.float32)).astype(
        jnp.bfloat16
    )
    pre_act = jnp.dot(normed_two, full_up, preferred_element_type=jnp.float32) + full_bu.astype(
        jnp.float32
    )
    activated = jax.nn.gelu(pre_act, approximate=True).astype(jnp.bfloat16)
    outputs = middle + (
        jnp.dot(activated, full_down, preferred_element_type=jnp.float32)
        + full_bd.astype(jnp.float32)
    )
    back_g1, back_qkv, back_out, back_g2, back_up, back_down = (
        full_g1, full_qkv, full_out, full_g2, full_up, full_down
    )
    shard_steps = bit_steps(shard_count)
    order = chunk_order(shard_count, shard_steps)
    cot_low = cotangent[0]
    cot_full = cot_low.astype(jnp.float32)
    zero_shift = jnp.zeros((model_width,), jnp.float32)
    grad_bd = jnp.sum(cot_full, 0)
    grad_act = jnp.einsum("to,fo->tf", cot_low, back_down, preferred_element_type=jnp.float32)
    _, gelu_pull = jax.vjp(partial(jax.nn.gelu, approximate=True), pre_act)
    grad_pre = gelu_pull(grad_act)[0].astype(jnp.bfloat16)
    grad_bu = jnp.sum(grad_pre.astype(jnp.float32), 0)
    grad_down = jnp.einsum(
        "tf,to->fo", reorder_cols(activated, order), cot_low, preferred_element_type=jnp.float32
    )
    (down_own,) = halving([grad_down], "shard", shard_count, shard_steps)
    total_a1 = lax.psum(down_own.astype(jnp.bfloat16), "rep")
    grad_up_t = jnp.einsum(
        "tf,ti->fi", reorder_cols(grad_pre, order), normed_two, preferred_element_type=jnp.float32
    )
    grad_normed_two = jnp.einsum("tf,if->ti", grad_pre, back_up, preferred_element_type=jnp.float32)
    _, norm_pull_two = jax.vjp(normalize, middle, back_g2.astype(jnp.float32), zero_shift)
    grad_mid_part, grad_g2, grad_s2 = norm_pull_two(grad_normed_two)
    grad_middle = cot_full + grad_mid_part
    grad_branch = grad_middle.astype(jnp.bfloat16)
    grad_bo = jnp.sum(grad_branch.astype(jnp.float32), 0)
    grad_mixed = jnp.einsum(
        "to,io->ti", grad_branch, back_out, preferred_element_type=jnp.float32
    ).astype(jnp.bfloat16)
    grad_out = jnp.einsum(
        "ti,to->io", reorder_cols(mixed, order), grad_branch, preferred_element_type=jnp.float32
    )
    up_own, out_own = halving([grad_up_t, grad_out], "shard", shard_count, shard_steps)
    owned_a = [up_own, out_own]
    joined_a = jnp.concatenate([o.astype(jnp.bfloat16) for o in owned_a], 0)
    total_a1, joined_a = lax.optimization_barrier((total_a1, joined_a))
    total_a = lax.psum(joined_a, "rep")
    grad_q, grad_k, grad_v = attend_backward(
        queries, key_rows, values, grad_mixed, log_norms, distance, allowed
    )
    grad_proj = jnp.concatenate([grad_q, grad_k, grad_v], 1)
    grad_qb = jnp.sum(grad_q.astype(jnp.float32), 0)
    grad_vb = jnp.sum(grad_v.astype(jnp.float32), 0)
    grad_normed = jnp.einsum("tc,ic->ti", grad_proj, back_qkv, preferred_element_type=jnp.float32)
    _, norm_pull_one = jax.vjp(normalize, inputs, back_g1.astype(jnp.float32), zero_shift)
    grad_in_part, grad_g1, grad_s1 = norm_pull_one(grad_normed)
    grad_inputs = grad_middle + grad_in_part
    grad_qkv_t = jnp.einsum(
        "tc,ti->ci", reorder_cols(grad_proj, order), normed, preferred_element_type=jnp.float32
    )
    smalls = [grad_g1, grad_s1, grad_qb, grad_vb, grad_bo, grad_g2, grad_s2, grad_bu, grad_bd]
    reps = lax.psum(1, "rep")
    qkv_rows = grad_qkv_t.shape[0] // shard_count
    small_rows = jnp.concatenate([g.reshape(shard_count, -1) for g in smalls], 1)
    small_rows = small_rows.reshape(shard_count, -1, model_width)
    pad_to = small_rows.shape[1] + (-(qkv_rows + small_rows.shape[1]) % (8 * reps))
    small_rows = jnp.pad(small_rows, ((0, 0), (0, pad_to - small_rows.shape[1]), (0, 0)))
    small_rows = jnp.concatenate([small_rows[k] for k in order], 0)
    qkv_own, small_own = halving([grad_qkv_t, small_rows], "shard", shard_count, shard_steps)
    joined_b = jnp.concatenate([qkv_own, small_own], 0)
    total_b = direct_reduce(joined_b, "rep", reps)
    up_rows = up_own.shape[0]
    down_fin = total_a1.astype(jnp.float32)
    up_fin = total_a[:up_rows].astype(jnp.float32).T
    out_fin = total_a[up_rows:].astype(jnp.float32)
    qkv_fin = total_b[:qkv_rows].astype(jnp.float32).T
    small_flat = total_b[qkv_rows:].reshape(-1).astype(jnp.float32)
    small_fin, offset = [], 0
    for g in smalls:
        width = g.shape[0] // shard_count
        small_fin.append(small_flat[offset : offset + width])
        offset += width
    g1_fin, s1_fin, qb_fin, vb_fin, bo_fin, g2_fin, s2_fin, bu_fin, bd_fin = small_fin
    return (
        outputs.astype(jnp.bfloat16)[None],
        grad_inputs.astype(jnp.bfloat16)[None],
        g1_fin,
        s1_fin,
        qkv_fin,
        qb_fin,
        vb_fin,
        out_fin,
        bo_fin,
        g2_fin,
        s2_fin,
        up_fin,
        bu_fin,
        down_fin,
        bd_fin,
    )


def solution(mesh):
    return jax.shard_map(
        body_inner,
        mesh=mesh,
        in_specs=(
            P(("rep", "shard"), None, None),
            P(("rep", "shard"), None, None),
            P(("rep", "shard"), None, None),
            P("shard"),
            P("shard"),
            P(None, "shard"),
            P("shard"),
            P("shard"),
            P("shard", None),
            P("shard"),
            P("shard"),
            P("shard"),
            P(None, "shard"),
            P("shard"),
            P("shard", None),
            P("shard"),
        ),
        out_specs=(
            P(("rep", "shard"), None, None),
            P(("rep", "shard"), None, None),
            P("shard"),
            P("shard"),
            P(None, "shard"),
            P("shard"),
            P("shard"),
            P("shard", None),
            P("shard"),
            P("shard"),
            P("shard"),
            P(None, "shard"),
            P("shard"),
            P("shard", None),
            P("shard"),
        ),
        check_vma=False,
    )
```

```python
from functools import partial

import jax
import jax.numpy as jnp
from jax import lax
from jax.sharding import PartitionSpec as P


HEADS = 16
HDIM = 64
PROMPT = 256


def normalize(values, gain, shift):
    center = values - jnp.mean(values, -1, keepdims=True)
    spread = jnp.mean(center * center, -1, keepdims=True)
    return center * lax.rsqrt(spread + 1e-05) * gain + shift


def layout(segments):
    micros, row_count = segments.shape
    same_seg = segments[:, :, None] == segments[:, None, :]
    earlier = jnp.arange(row_count)[None, :] < jnp.arange(row_count)[:, None]
    offsets = jnp.sum(jnp.where(same_seg & earlier[None], 1, 0), -1).astype(jnp.int32)
    cont_pos = PROMPT + offsets
    owners = jnp.arange(micros, dtype=jnp.int32)[:, None] * row_count + segments
    positions = jnp.concatenate([jnp.arange(PROMPT, dtype=jnp.int32), cont_pos.reshape(-1)])
    groups = jnp.concatenate([jnp.full((PROMPT,), -1, jnp.int32), owners.reshape(-1)])
    places = jnp.arange(positions.shape[0], dtype=jnp.int32)
    allowed = (places[None, :] <= places[:, None]) & (
        (places[None, :] < PROMPT) | (groups[None, :] == groups[:, None])
    )
    distance = (positions[:, None] - positions[None, :]).astype(jnp.float32)
    return (distance, allowed)


def head_slice(matrix, block):
    block_width = 4 * HDIM
    part = lax.dynamic_slice_in_dim(matrix, block * block_width, block_width, 1)
    return part.reshape(matrix.shape[0], 4, HDIM)


def block_scores(q_part, k_part, block, distance, allowed):
    heads = (block * 4 + jnp.arange(4, dtype=jnp.int32)).astype(jnp.float32)
    slopes = jnp.exp2(-8.0 * (heads + 1.0) / HEADS)
    scores = jnp.einsum(
        "qhd,khd->hqk", q_part, k_part, preferred_element_type=jnp.float32
    ) * HDIM ** (-0.5)
    scores = scores - slopes[:, None, None] * distance[None]
    return jnp.where(allowed[None], scores, -jnp.inf)


def side_by_side(blocks):
    return jnp.transpose(blocks, (1, 0, 2)).reshape(
        blocks.shape[1], blocks.shape[0] * blocks.shape[2]
    )


def attend_forward(queries, key_rows, values, distance, allowed):
    length = queries.shape[0]

    def head_block(block):
        q_part = head_slice(queries, block)
        k_part = head_slice(key_rows, block)
        v_part = head_slice(values, block)
        scores = block_scores(q_part, k_part, block, distance, allowed)
        peak = jnp.max(scores, -1, keepdims=True)
        exps_rel = jnp.exp(scores - peak)
        row_totals = jnp.sum(exps_rel, -1, keepdims=True)
        attn_probs = (exps_rel / row_totals).astype(jnp.bfloat16)
        mixed = jnp.einsum("hqk,khd->qhd", attn_probs, v_part, preferred_element_type=jnp.float32)
        return (mixed.reshape(length, 4 * HDIM), (peak + jnp.log(row_totals))[:, :, 0])

    mixed, log_norms = lax.map(head_block, jnp.arange(HEADS // 4, dtype=jnp.int32))
    return (side_by_side(mixed).astype(jnp.bfloat16), log_norms)


def attend_backward(queries, key_rows, values, grad_mixed, log_norms, distance, allowed):
    length = queries.shape[0]
    scale = HDIM ** (-0.5)

    def head_block(block):
        q_part = head_slice(queries, block)
        k_part = head_slice(key_rows, block)
        v_part = head_slice(values, block)
        g_part = head_slice(grad_mixed, block)
        scores = block_scores(q_part, k_part, block, distance, allowed)
        attn_probs = jnp.exp(scores - log_norms[block][:, :, None])
        grad_probs = jnp.einsum("qhd,khd->hqk", g_part, v_part, preferred_element_type=jnp.float32)
        inner = jnp.sum(attn_probs * grad_probs, -1, keepdims=True)
        grad_scores = (attn_probs * (grad_probs - inner)).astype(jnp.bfloat16)
        grad_q = (
            jnp.einsum("hqk,khd->qhd", grad_scores, k_part, preferred_element_type=jnp.float32)
            * scale
        )
        grad_k = (
            jnp.einsum("hqk,qhd->khd", grad_scores, q_part, preferred_element_type=jnp.float32)
            * scale
        )
        grad_v = jnp.einsum(
            "hqk,qhd->khd",
            attn_probs.astype(jnp.bfloat16),
            g_part,
            preferred_element_type=jnp.float32,
        )
        block_width = 4 * HDIM
        return (
            grad_q.reshape(length, block_width),
            grad_k.reshape(length, block_width),
            grad_v.reshape(length, block_width),
        )

    grad_q, grad_k, grad_v = lax.map(head_block, jnp.arange(HEADS // 4, dtype=jnp.int32))
    return (
        side_by_side(grad_q).astype(jnp.bfloat16),
        side_by_side(grad_k).astype(jnp.bfloat16),
        side_by_side(grad_v).astype(jnp.bfloat16),
    )


def bit_steps(size):
    assert size & (size - 1) == 0
    return [1 << b for b in range(size.bit_length() - 1)]


def chunk_order(size, steps):
    places = []
    for member in range(size):
        place = 0
        for step in steps:
            place = place * 2 + (member // step) % 2
        places.append(place)
    order = [0] * size
    for member, place in enumerate(places):
        order[place] = member
    return order


def reorder_cols(matrix, order):
    pieces = jnp.split(matrix, len(order), 1)
    return jnp.concatenate([pieces[k] for k in order], 1)


def halving(arrays, axis, size, steps):
    index = lax.axis_index(axis)
    for step in steps:
        bit = (index // step) % 2
        keeps, sends = [], []
        for array in arrays:
            pair = array.reshape(2, array.shape[0] // 2, *array.shape[1:])
            keeps.append(lax.dynamic_index_in_dim(pair, bit, 0, keepdims=False))
            sends.append(
                lax.dynamic_index_in_dim(pair, 1 - bit, 0, keepdims=False).astype(jnp.bfloat16)
            )
        got = lax.ppermute(jnp.concatenate(sends, 0), axis, [(a, a ^ step) for a in range(size)])
        arrays, offset = [], 0
        for keep in keeps:
            arrays.append(keep + got[offset : offset + keep.shape[0]].astype(jnp.float32))
            offset += keep.shape[0]
    return arrays


def direct_reduce(buf, axis, size):
    index = lax.axis_index(axis)
    chunks = buf.reshape(size, buf.shape[0] // size, *buf.shape[1:])
    total = lax.dynamic_index_in_dim(chunks, index, 0, keepdims=False)
    for shift in range(1, size):
        send = lax.dynamic_index_in_dim(chunks, (index + shift) % size, 0, keepdims=False)
        got = lax.ppermute(
            send.astype(jnp.bfloat16), axis, [(a, (a + shift) % size) for a in range(size)]
        )
        total = total + got.astype(jnp.float32)
    mine = total.astype(jnp.bfloat16)
    result = jnp.zeros((size, *mine.shape), jnp.bfloat16)
    result = lax.dynamic_update_index_in_dim(result, mine, index, 0)
    for shift in range(1, size):
        got = lax.ppermute(mine, axis, [(a, (a + shift) % size) for a in range(size)])
        result = lax.dynamic_update_index_in_dim(result, got, (index - shift) % size, 0)
    return result.reshape(buf.shape)


def gather_small(pieces):
    packed = jnp.concatenate(pieces)
    shards = lax.all_gather(packed, "shard", axis=0, tiled=False)
    fulls, offset = [], 0
    for piece in pieces:
        width = piece.shape[0]
        fulls.append(shards[:, offset : offset + width].reshape(-1))
        offset += width
    return fulls


def body_inner(
    tokens,
    cont_segment,
    cotangent,
    ln1_gain,
    ln1_bias,
    w_qkv,
    q_bias,
    v_bias,
    w_out,
    b_out,
    ln2_gain,
    ln2_bias,
    w_up,
    b_up,
    w_down,
    b_down,
):
    shard_count = lax.psum(1, "shard")
    full_g1, full_s1, full_qb, full_vb, full_bo, full_g2, full_s2, full_bu, full_bd = gather_small(
        [ln1_gain, ln1_bias, q_bias, v_bias, b_out, ln2_gain, ln2_bias, b_up, b_down]
    )
    full_qkv = lax.all_gather(w_qkv, "shard", axis=1, tiled=True)
    full_out = lax.all_gather(w_out, "shard", axis=0, tiled=True)
    full_up = lax.all_gather(w_up, "shard", axis=1, tiled=True)
    full_down = lax.all_gather(w_down, "shard", axis=0, tiled=True)
    inputs = tokens[0].astype(jnp.float32)
    _, model_width = inputs.shape
    distance, allowed = layout(cont_segment[0])
    normed = normalize(inputs, full_g1.astype(jnp.float32), full_s1.astype(jnp.float32)).astype(
        jnp.bfloat16
    )
    projected = jnp.dot(normed, full_qkv, preferred_element_type=jnp.float32)
    queries = (projected[:, :model_width] + full_qb.astype(jnp.float32)).astype(jnp.bfloat16)
    key_rows = projected[:, model_width : 2 * model_width].astype(jnp.bfloat16)
    values = (projected[:, 2 * model_width :] + full_vb.astype(jnp.float32)).astype(jnp.bfloat16)
    mixed, log_norms = attend_forward(queries, key_rows, values, distance, allowed)
    branch = jnp.dot(mixed, full_out, preferred_element_type=jnp.float32) + full_bo.astype(
        jnp.float32
    )
    middle = inputs + branch
    normed_two = normalize(middle, full_g2.astype(jnp.float32), full_s2.astype(jnp.float32)).astype(
        jnp.bfloat16
    )
    pre_act = jnp.dot(normed_two, full_up, preferred_element_type=jnp.float32) + full_bu.astype(
        jnp.float32
    )
    activated = jax.nn.gelu(pre_act, approximate=True).astype(jnp.bfloat16)
    outputs = middle + (
        jnp.dot(activated, full_down, preferred_element_type=jnp.float32)
        + full_bd.astype(jnp.float32)
    )
    back_g1, back_qkv, back_out, back_g2, back_up, back_down = (
        full_g1, full_qkv, full_out, full_g2, full_up, full_down
    )
    shard_steps = bit_steps(shard_count)
    order = chunk_order(shard_count, shard_steps)
    cot_low = cotangent[0]
    cot_full = cot_low.astype(jnp.float32)
    zero_shift = jnp.zeros((model_width,), jnp.float32)
    grad_bd = jnp.sum(cot_full, 0)
    grad_act = jnp.einsum("to,fo->tf", cot_low, back_down, preferred_element_type=jnp.float32)
    _, gelu_pull = jax.vjp(partial(jax.nn.gelu, approximate=True), pre_act)
    grad_pre = gelu_pull(grad_act)[0].astype(jnp.bfloat16)
    grad_bu = jnp.sum(grad_pre.astype(jnp.float32), 0)
    grad_down = jnp.einsum(
        "tf,to->fo", reorder_cols(activated, order), cot_low, preferred_element_type=jnp.float32
    )
    (down_own,) = halving([grad_down], "shard", shard_count, shard_steps)
    total_a1 = lax.psum(down_own.astype(jnp.bfloat16), "rep")
    grad_up_t = jnp.einsum(
        "tf,ti->fi", reorder_cols(grad_pre, order), normed_two, preferred_element_type=jnp.float32
    )
    grad_normed_two = jnp.einsum("tf,if->ti", grad_pre, back_up, preferred_element_type=jnp.float32)
    _, norm_pull_two = jax.vjp(normalize, middle, back_g2.astype(jnp.float32), zero_shift)
    grad_mid_part, grad_g2, grad_s2 = norm_pull_two(grad_normed_two)
    grad_middle = cot_full + grad_mid_part
    grad_branch = grad_middle.astype(jnp.bfloat16)
    grad_bo = jnp.sum(grad_branch.astype(jnp.float32), 0)
    grad_mixed = jnp.einsum(
        "to,io->ti", grad_branch, back_out, preferred_element_type=jnp.float32
    ).astype(jnp.bfloat16)
    grad_out = jnp.einsum(
        "ti,to->io", reorder_cols(mixed, order), grad_branch, preferred_element_type=jnp.float32
    )
    up_own, out_own = halving([grad_up_t, grad_out], "shard", shard_count, shard_steps)
    owned_a = [up_own.astype(jnp.bfloat16).T, out_own.astype(jnp.bfloat16)]
    joined_a = jnp.concatenate(owned_a, 0)
    down_fin, joined_a = lax.optimization_barrier((total_a1.astype(jnp.float32), joined_a))
    total_a = lax.psum(joined_a, "rep")
    grad_q, grad_k, grad_v = attend_backward(
        queries, key_rows, values, grad_mixed, log_norms, distance, allowed
    )
    grad_proj = jnp.concatenate([grad_q, grad_k, grad_v], 1)
    grad_qb = jnp.sum(grad_q.astype(jnp.float32), 0)
    grad_vb = jnp.sum(grad_v.astype(jnp.float32), 0)
    grad_normed = jnp.einsum("tc,ic->ti", grad_proj, back_qkv, preferred_element_type=jnp.float32)
    _, norm_pull_one = jax.vjp(normalize, inputs, back_g1.astype(jnp.float32), zero_shift)
    grad_in_part, grad_g1, grad_s1 = norm_pull_one(grad_normed)
    grad_inputs = grad_middle + grad_in_part
    grad_qkv_t = jnp.einsum(
        "tc,ti->ci", reorder_cols(grad_proj, order), normed, preferred_element_type=jnp.float32
    )
    smalls = [grad_g1, grad_s1, grad_qb, grad_vb, grad_bo, grad_g2, grad_s2, grad_bu, grad_bd]
    reps = lax.psum(1, "rep")
    qkv_rows = grad_qkv_t.shape[0] // shard_count
    small_rows = jnp.concatenate([g.reshape(shard_count, -1) for g in smalls], 1)
    small_rows = small_rows.reshape(shard_count, -1, model_width)
    pad_to = small_rows.shape[1] + (-(qkv_rows + small_rows.shape[1]) % (8 * reps))
    small_rows = jnp.pad(small_rows, ((0, 0), (0, pad_to - small_rows.shape[1]), (0, 0)))
    small_rows = jnp.concatenate([small_rows[k] for k in order], 0)
    qkv_own, small_own = halving([grad_qkv_t, small_rows], "shard", shard_count, shard_steps)
    joined_b = jnp.concatenate([qkv_own, small_own], 0)
    total_b = direct_reduce(joined_b, "rep", reps)
    up_rows = up_own.shape[0]
    up_fin = total_a[:up_rows].astype(jnp.float32)
    out_fin = total_a[up_rows:].astype(jnp.float32)
    qkv_fin = total_b[:qkv_rows].astype(jnp.float32).T
    small_flat = total_b[qkv_rows:].reshape(-1).astype(jnp.float32)
    small_fin, offset = [], 0
    for g in smalls:
        width = g.shape[0] // shard_count
        small_fin.append(small_flat[offset : offset + width])
        offset += width
    g1_fin, s1_fin, qb_fin, vb_fin, bo_fin, g2_fin, s2_fin, bu_fin, bd_fin = small_fin
    return (
        outputs.astype(jnp.bfloat16)[None],
        grad_inputs.astype(jnp.bfloat16)[None],
        g1_fin,
        s1_fin,
        qkv_fin,
        qb_fin,
        vb_fin,
        out_fin,
        bo_fin,
        g2_fin,
        s2_fin,
        up_fin,
        bu_fin,
        down_fin,
        bd_fin,
    )


def solution(mesh):
    return jax.shard_map(
        body_inner,
        mesh=mesh,
        in_specs=(
            P(("rep", "shard"), None, None),
            P(("rep", "shard"), None, None),
            P(("rep", "shard"), None, None),
            P("shard"),
            P("shard"),
            P(None, "shard"),
            P("shard"),
            P("shard"),
            P("shard", None),
            P("shard"),
            P("shard"),
            P("shard"),
            P(None, "shard"),
            P("shard"),
            P("shard", None),
            P("shard"),
        ),
        out_specs=(
            P(("rep", "shard"), None, None),
            P(("rep", "shard"), None, None),
            P("shard"),
            P("shard"),
            P(None, "shard"),
            P("shard"),
            P("shard"),
            P("shard", None),
            P("shard"),
            P("shard"),
            P("shard"),
            P(None, "shard"),
            P("shard"),
            P("shard", None),
            P("shard"),
        ),
        check_vma=False,
    )
```

```python
from functools import partial

import jax
import jax.numpy as jnp
from jax import lax
from jax.sharding import PartitionSpec as P


HEADS = 16
HDIM = 64
PROMPT = 256


def normalize(values, gain, shift):
    center = values - jnp.mean(values, -1, keepdims=True)
    spread = jnp.mean(center * center, -1, keepdims=True)
    return center * lax.rsqrt(spread + 1e-05) * gain + shift


def layout(segments):
    micros, row_count = segments.shape
    same_seg = segments[:, :, None] == segments[:, None, :]
    earlier = jnp.arange(row_count)[None, :] < jnp.arange(row_count)[:, None]
    offsets = jnp.sum(jnp.where(same_seg & earlier[None], 1, 0), -1).astype(jnp.int32)
    cont_pos = PROMPT + offsets
    owners = jnp.arange(micros, dtype=jnp.int32)[:, None] * row_count + segments
    positions = jnp.concatenate([jnp.arange(PROMPT, dtype=jnp.int32), cont_pos.reshape(-1)])
    groups = jnp.concatenate([jnp.full((PROMPT,), -1, jnp.int32), owners.reshape(-1)])
    places = jnp.arange(positions.shape[0], dtype=jnp.int32)
    allowed = (places[None, :] <= places[:, None]) & (
        (places[None, :] < PROMPT) | (groups[None, :] == groups[:, None])
    )
    distance = (positions[:, None] - positions[None, :]).astype(jnp.float32)
    return (distance, allowed)


def head_slice(matrix, block):
    block_width = 4 * HDIM
    part = lax.dynamic_slice_in_dim(matrix, block * block_width, block_width, 1)
    return part.reshape(matrix.shape[0], 4, HDIM)


def block_scores(q_part, k_part, block, distance, allowed):
    heads = (block * 4 + jnp.arange(4, dtype=jnp.int32)).astype(jnp.float32)
    slopes = jnp.exp2(-8.0 * (heads + 1.0) / HEADS)
    scores = jnp.einsum(
        "qhd,khd->hqk", q_part, k_part, preferred_element_type=jnp.float32
    ) * HDIM ** (-0.5)
    scores = scores - slopes[:, None, None] * distance[None]
    return jnp.where(allowed[None], scores, -jnp.inf)


def side_by_side(blocks):
    return jnp.transpose(blocks, (1, 0, 2)).reshape(
        blocks.shape[1], blocks.shape[0] * blocks.shape[2]
    )


def attend_forward(queries, key_rows, values, distance, allowed):
    length = queries.shape[0]

    def head_block(block):
        q_part = head_slice(queries, block)
        k_part = head_slice(key_rows, block)
        v_part = head_slice(values, block)
        scores = block_scores(q_part, k_part, block, distance, allowed)
        peak = jnp.max(scores, -1, keepdims=True)
        exps_rel = jnp.exp(scores - peak)
        row_totals = jnp.sum(exps_rel, -1, keepdims=True)
        attn_probs = (exps_rel / row_totals).astype(jnp.bfloat16)
        mixed = jnp.einsum("hqk,khd->qhd", attn_probs, v_part, preferred_element_type=jnp.float32)
        return (mixed.reshape(length, 4 * HDIM), (peak + jnp.log(row_totals))[:, :, 0])

    mixed, log_norms = lax.map(head_block, jnp.arange(HEADS // 4, dtype=jnp.int32))
    return (side_by_side(mixed).astype(jnp.bfloat16), log_norms)


def attend_backward(queries, key_rows, values, grad_mixed, log_norms, distance, allowed):
    length = queries.shape[0]
    scale = HDIM ** (-0.5)

    def head_block(block):
        q_part = head_slice(queries, block)
        k_part = head_slice(key_rows, block)
        v_part = head_slice(values, block)
        g_part = head_slice(grad_mixed, block)
        scores = block_scores(q_part, k_part, block, distance, allowed)
        attn_probs = jnp.exp(scores - log_norms[block][:, :, None])
        grad_probs = jnp.einsum("qhd,khd->hqk", g_part, v_part, preferred_element_type=jnp.float32)
        inner = jnp.sum(attn_probs * grad_probs, -1, keepdims=True)
        grad_scores = (attn_probs * (grad_probs - inner)).astype(jnp.bfloat16)
        grad_q = (
            jnp.einsum("hqk,khd->qhd", grad_scores, k_part, preferred_element_type=jnp.float32)
            * scale
        )
        grad_k = (
            jnp.einsum("hqk,qhd->khd", grad_scores, q_part, preferred_element_type=jnp.float32)
            * scale
        )
        grad_v = jnp.einsum(
            "hqk,qhd->khd",
            attn_probs.astype(jnp.bfloat16),
            g_part,
            preferred_element_type=jnp.float32,
        )
        block_width = 4 * HDIM
        return (
            grad_q.reshape(length, block_width),
            grad_k.reshape(length, block_width),
            grad_v.reshape(length, block_width),
        )

    grad_q, grad_k, grad_v = lax.map(head_block, jnp.arange(HEADS // 4, dtype=jnp.int32))
    return (
        side_by_side(grad_q).astype(jnp.bfloat16),
        side_by_side(grad_k).astype(jnp.bfloat16),
        side_by_side(grad_v).astype(jnp.bfloat16),
    )


def bit_steps(size):
    assert size & (size - 1) == 0
    return [1 << b for b in range(size.bit_length() - 1)]


def chunk_order(size, steps):
    places = []
    for member in range(size):
        place = 0
        for step in steps:
            place = place * 2 + (member // step) % 2
        places.append(place)
    order = [0] * size
    for member, place in enumerate(places):
        order[place] = member
    return order


def reorder_cols(matrix, order):
    pieces = jnp.split(matrix, len(order), 1)
    return jnp.concatenate([pieces[k] for k in order], 1)


def halving(arrays, axis, size, steps):
    index = lax.axis_index(axis)
    for step in steps:
        bit = (index // step) % 2
        keeps, sends = [], []
        for array in arrays:
            pair = array.reshape(2, array.shape[0] // 2, *array.shape[1:])
            keeps.append(lax.dynamic_index_in_dim(pair, bit, 0, keepdims=False))
            sends.append(
                lax.dynamic_index_in_dim(pair, 1 - bit, 0, keepdims=False).astype(jnp.bfloat16)
            )
        got = lax.ppermute(jnp.concatenate(sends, 0), axis, [(a, a ^ step) for a in range(size)])
        arrays, offset = [], 0
        for keep in keeps:
            arrays.append(keep + got[offset : offset + keep.shape[0]].astype(jnp.float32))
            offset += keep.shape[0]
    return arrays


def direct_reduce(buf, axis, size):
    index = lax.axis_index(axis)
    chunks = buf.reshape(size, buf.shape[0] // size, *buf.shape[1:])
    total = lax.dynamic_index_in_dim(chunks, index, 0, keepdims=False)
    for shift in range(1, size):
        send = lax.dynamic_index_in_dim(chunks, (index + shift) % size, 0, keepdims=False)
        got = lax.ppermute(
            send.astype(jnp.bfloat16), axis, [(a, (a + shift) % size) for a in range(size)]
        )
        total = total + got.astype(jnp.float32)
    mine = total.astype(jnp.bfloat16)
    result = jnp.zeros((size, *mine.shape), jnp.bfloat16)
    result = lax.dynamic_update_index_in_dim(result, mine, index, 0)
    for shift in range(1, size):
        got = lax.ppermute(mine, axis, [(a, (a + shift) % size) for a in range(size)])
        result = lax.dynamic_update_index_in_dim(result, got, (index - shift) % size, 0)
    return result.reshape(buf.shape)


def gather_small(pieces):
    packed = jnp.concatenate(pieces)
    shards = lax.all_gather(packed, "shard", axis=0, tiled=False)
    fulls, offset = [], 0
    for piece in pieces:
        width = piece.shape[0]
        fulls.append(shards[:, offset : offset + width].reshape(-1))
        offset += width
    return fulls


def body_inner(
    tokens,
    cont_segment,
    cotangent,
    ln1_gain,
    ln1_bias,
    w_qkv,
    q_bias,
    v_bias,
    w_out,
    b_out,
    ln2_gain,
    ln2_bias,
    w_up,
    b_up,
    w_down,
    b_down,
):
    shard_count = lax.psum(1, "shard")
    full_g1, full_s1, full_qb, full_vb, full_bo, full_g2, full_s2, full_bu, full_bd = gather_small(
        [ln1_gain, ln1_bias, q_bias, v_bias, b_out, ln2_gain, ln2_bias, b_up, b_down]
    )
    full_qkv = lax.all_gather(w_qkv, "shard", axis=1, tiled=True)
    full_out = lax.all_gather(w_out, "shard", axis=0, tiled=True)
    full_up = lax.all_gather(w_up, "shard", axis=1, tiled=True)
    full_down = lax.all_gather(w_down, "shard", axis=0, tiled=True)
    inputs = tokens[0].astype(jnp.float32)
    _, model_width = inputs.shape
    distance, allowed = layout(cont_segment[0])
    normed = normalize(inputs, full_g1.astype(jnp.float32), full_s1.astype(jnp.float32)).astype(
        jnp.bfloat16
    )
    projected = jnp.dot(normed, full_qkv, preferred_element_type=jnp.float32)
    queries = (projected[:, :model_width] + full_qb.astype(jnp.float32)).astype(jnp.bfloat16)
    key_rows = projected[:, model_width : 2 * model_width].astype(jnp.bfloat16)
    values = (projected[:, 2 * model_width :] + full_vb.astype(jnp.float32)).astype(jnp.bfloat16)
    mixed, log_norms = attend_forward(queries, key_rows, values, distance, allowed)
    branch = jnp.dot(mixed, full_out, preferred_element_type=jnp.float32) + full_bo.astype(
        jnp.float32
    )
    middle = inputs + branch
    normed_two = normalize(middle, full_g2.astype(jnp.float32), full_s2.astype(jnp.float32)).astype(
        jnp.bfloat16
    )
    pre_act = jnp.dot(normed_two, full_up, preferred_element_type=jnp.float32) + full_bu.astype(
        jnp.float32
    )
    activated = jax.nn.gelu(pre_act, approximate=True).astype(jnp.bfloat16)
    cot_low = cotangent[0]
    shard_steps = bit_steps(shard_count)
    order = chunk_order(shard_count, shard_steps)
    grad_down = jnp.einsum(
        "tf,to->fo", reorder_cols(activated, order), cot_low, preferred_element_type=jnp.float32
    )
    down_half = halving([grad_down], "shard", shard_count, shard_steps[:1])
    down_half, full_down = lax.optimization_barrier((down_half, full_down))
    outputs = middle + (
        jnp.dot(activated, full_down, preferred_element_type=jnp.float32)
        + full_bd.astype(jnp.float32)
    )
    back_g1, back_qkv, back_out, back_g2, back_up, back_down = (
        full_g1, full_qkv, full_out, full_g2, full_up, full_down
    )
    cot_full = cot_low.astype(jnp.float32)
    zero_shift = jnp.zeros((model_width,), jnp.float32)
    grad_bd = jnp.sum(cot_full, 0)
    grad_act = jnp.einsum("to,fo->tf", cot_low, back_down, preferred_element_type=jnp.float32)
    _, gelu_pull = jax.vjp(partial(jax.nn.gelu, approximate=True), pre_act)
    grad_pre = gelu_pull(grad_act)[0].astype(jnp.bfloat16)
    grad_bu = jnp.sum(grad_pre.astype(jnp.float32), 0)
    (down_own,) = halving(down_half, "shard", shard_count, shard_steps[1:])
    total_a1 = lax.psum(down_own.astype(jnp.bfloat16), "rep")
    grad_up_t = jnp.einsum(
        "tf,ti->fi", reorder_cols(grad_pre, order), normed_two, preferred_element_type=jnp.float32
    )
    grad_normed_two = jnp.einsum("tf,if->ti", grad_pre, back_up, preferred_element_type=jnp.float32)
    _, norm_pull_two = jax.vjp(normalize, middle, back_g2.astype(jnp.float32), zero_shift)
    grad_mid_part, grad_g2, grad_s2 = norm_pull_two(grad_normed_two)
    grad_middle = cot_full + grad_mid_part
    grad_branch = grad_middle.astype(jnp.bfloat16)
    grad_bo = jnp.sum(grad_branch.astype(jnp.float32), 0)
    grad_mixed = jnp.einsum(
        "to,io->ti", grad_branch, back_out, preferred_element_type=jnp.float32
    ).astype(jnp.bfloat16)
    grad_out = jnp.einsum(
        "ti,to->io", reorder_cols(mixed, order), grad_branch, preferred_element_type=jnp.float32
    )
    up_own, out_own = halving([grad_up_t, grad_out], "shard", shard_count, shard_steps)
    owned_a = [up_own.astype(jnp.bfloat16).T, out_own.astype(jnp.bfloat16)]
    joined_a = jnp.concatenate(owned_a, 0)
    down_fin, joined_a = lax.optimization_barrier((total_a1.astype(jnp.float32), joined_a))
    total_a = lax.psum(joined_a, "rep")
    grad_q, grad_k, grad_v = attend_backward(
        queries, key_rows, values, grad_mixed, log_norms, distance, allowed
    )
    grad_proj = jnp.concatenate([grad_q, grad_k, grad_v], 1)
    reps = lax.psum(1, "rep")
    grad_qkv_t = jnp.einsum(
        "tc,ti->ci", reorder_cols(grad_proj, order), normed, preferred_element_type=jnp.float32
    )
    (qkv_own,) = halving([grad_qkv_t], "shard", shard_count, shard_steps)
    total_b = direct_reduce(qkv_own, "rep", reps)
    grad_qkv_t, grad_proj = lax.optimization_barrier((grad_qkv_t, grad_proj))
    grad_qb = jnp.sum(grad_q.astype(jnp.float32), 0)
    grad_vb = jnp.sum(grad_v.astype(jnp.float32), 0)
    grad_normed = jnp.einsum("tc,ic->ti", grad_proj, back_qkv, preferred_element_type=jnp.float32)
    _, norm_pull_one = jax.vjp(normalize, inputs, back_g1.astype(jnp.float32), zero_shift)
    grad_in_part, grad_g1, grad_s1 = norm_pull_one(grad_normed)
    grad_inputs = grad_middle + grad_in_part
    smalls = [grad_g1, grad_s1, grad_qb, grad_vb, grad_bo, grad_g2, grad_s2, grad_bu, grad_bd]
    small_rows = jnp.concatenate([g.reshape(shard_count, -1) for g in smalls], 1)
    small_rows = small_rows.reshape(shard_count, -1, model_width)
    pad_to = small_rows.shape[1] + (-small_rows.shape[1] % reps)
    small_rows = jnp.pad(small_rows, ((0, 0), (0, pad_to - small_rows.shape[1]), (0, 0)))
    small_rows = jnp.concatenate([small_rows[k] for k in order], 0)
    (small_own,) = halving([small_rows], "shard", shard_count, shard_steps)
    total_s = direct_reduce(small_own, "rep", reps)
    up_rows = up_own.shape[0]
    up_fin = total_a[:up_rows].astype(jnp.float32)
    out_fin = total_a[up_rows:].astype(jnp.float32)
    qkv_fin = total_b.astype(jnp.float32).T
    small_flat = total_s.reshape(-1).astype(jnp.float32)
    small_fin, offset = [], 0
    for g in smalls:
        width = g.shape[0] // shard_count
        small_fin.append(small_flat[offset : offset + width])
        offset += width
    g1_fin, s1_fin, qb_fin, vb_fin, bo_fin, g2_fin, s2_fin, bu_fin, bd_fin = small_fin
    return (
        outputs.astype(jnp.bfloat16)[None],
        grad_inputs.astype(jnp.bfloat16)[None],
        g1_fin,
        s1_fin,
        qkv_fin,
        qb_fin,
        vb_fin,
        out_fin,
        bo_fin,
        g2_fin,
        s2_fin,
        up_fin,
        bu_fin,
        down_fin,
        bd_fin,
    )


def solution(mesh):
    return jax.shard_map(
        body_inner,
        mesh=mesh,
        in_specs=(
            P(("rep", "shard"), None, None),
            P(("rep", "shard"), None, None),
            P(("rep", "shard"), None, None),
            P("shard"),
            P("shard"),
            P(None, "shard"),
            P("shard"),
            P("shard"),
            P("shard", None),
            P("shard"),
            P("shard"),
            P("shard"),
            P(None, "shard"),
            P("shard"),
            P("shard", None),
            P("shard"),
        ),
        out_specs=(
            P(("rep", "shard"), None, None),
            P(("rep", "shard"), None, None),
            P("shard"),
            P("shard"),
            P(None, "shard"),
            P("shard"),
            P("shard"),
            P("shard", None),
            P("shard"),
            P("shard"),
            P("shard"),
            P(None, "shard"),
            P("shard"),
            P("shard", None),
            P("shard"),
        ),
        check_vma=False,
    )
```

```python
from functools import partial

import jax
import jax.numpy as jnp
from jax import lax
from jax.sharding import PartitionSpec as P


HEADS = 16
HDIM = 64
PROMPT = 256


def normalize(values, gain, shift):
    center = values - jnp.mean(values, -1, keepdims=True)
    spread = jnp.mean(center * center, -1, keepdims=True)
    return center * lax.rsqrt(spread + 1e-05) * gain + shift


def layout(segments):
    micros, row_count = segments.shape
    same_seg = segments[:, :, None] == segments[:, None, :]
    earlier = jnp.arange(row_count)[None, :] < jnp.arange(row_count)[:, None]
    offsets = jnp.sum(jnp.where(same_seg & earlier[None], 1, 0), -1).astype(jnp.int32)
    cont_pos = PROMPT + offsets
    owners = jnp.arange(micros, dtype=jnp.int32)[:, None] * row_count + segments
    positions = jnp.concatenate([jnp.arange(PROMPT, dtype=jnp.int32), cont_pos.reshape(-1)])
    groups = jnp.concatenate([jnp.full((PROMPT,), -1, jnp.int32), owners.reshape(-1)])
    places = jnp.arange(positions.shape[0], dtype=jnp.int32)
    allowed = (places[None, :] <= places[:, None]) & (
        (places[None, :] < PROMPT) | (groups[None, :] == groups[:, None])
    )
    distance = (positions[:, None] - positions[None, :]).astype(jnp.float32)
    return (distance, allowed)


def head_slice(matrix, block):
    block_width = 4 * HDIM
    part = lax.dynamic_slice_in_dim(matrix, block * block_width, block_width, 1)
    return part.reshape(matrix.shape[0], 4, HDIM)


def block_scores(q_part, k_part, block, distance, allowed):
    heads = (block * 4 + jnp.arange(4, dtype=jnp.int32)).astype(jnp.float32)
    slopes = jnp.exp2(-8.0 * (heads + 1.0) / HEADS)
    scores = jnp.einsum(
        "qhd,khd->hqk", q_part, k_part, preferred_element_type=jnp.float32
    ) * HDIM ** (-0.5)
    scores = scores - slopes[:, None, None] * distance[None]
    return jnp.where(allowed[None], scores, -jnp.inf)


def side_by_side(blocks):
    return jnp.transpose(blocks, (1, 0, 2)).reshape(
        blocks.shape[1], blocks.shape[0] * blocks.shape[2]
    )


def attend_forward(queries, key_rows, values, distance, allowed):
    length = queries.shape[0]

    def head_block(block):
        q_part = head_slice(queries, block)
        k_part = head_slice(key_rows, block)
        v_part = head_slice(values, block)
        scores = block_scores(q_part, k_part, block, distance, allowed)
        peak = jnp.max(scores, -1, keepdims=True)
        exps_rel = jnp.exp(scores - peak)
        row_totals = jnp.sum(exps_rel, -1, keepdims=True)
        attn_probs = (exps_rel / row_totals).astype(jnp.bfloat16)
        mixed = jnp.einsum("hqk,khd->qhd", attn_probs, v_part, preferred_element_type=jnp.float32)
        return (mixed.reshape(length, 4 * HDIM), (peak + jnp.log(row_totals))[:, :, 0])

    mixed, log_norms = lax.map(head_block, jnp.arange(HEADS // 4, dtype=jnp.int32))
    return (side_by_side(mixed).astype(jnp.bfloat16), log_norms)


def attend_backward(queries, key_rows, values, grad_mixed, log_norms, distance, allowed):
    length = queries.shape[0]
    scale = HDIM ** (-0.5)

    def head_block(block):
        q_part = head_slice(queries, block)
        k_part = head_slice(key_rows, block)
        v_part = head_slice(values, block)
        g_part = head_slice(grad_mixed, block)
        scores = block_scores(q_part, k_part, block, distance, allowed)
        attn_probs = jnp.exp(scores - log_norms[block][:, :, None])
        grad_probs = jnp.einsum("qhd,khd->hqk", g_part, v_part, preferred_element_type=jnp.float32)
        inner = jnp.sum(attn_probs * grad_probs, -1, keepdims=True)
        grad_scores = (attn_probs * (grad_probs - inner)).astype(jnp.bfloat16)
        grad_q = (
            jnp.einsum("hqk,khd->qhd", grad_scores, k_part, preferred_element_type=jnp.float32)
            * scale
        )
        grad_k = (
            jnp.einsum("hqk,qhd->khd", grad_scores, q_part, preferred_element_type=jnp.float32)
            * scale
        )
        grad_v = jnp.einsum(
            "hqk,qhd->khd",
            attn_probs.astype(jnp.bfloat16),
            g_part,
            preferred_element_type=jnp.float32,
        )
        block_width = 4 * HDIM
        return (
            grad_q.reshape(length, block_width),
            grad_k.reshape(length, block_width),
            grad_v.reshape(length, block_width),
        )

    grad_q, grad_k, grad_v = lax.map(head_block, jnp.arange(HEADS // 4, dtype=jnp.int32))
    return (
        side_by_side(grad_q).astype(jnp.bfloat16),
        side_by_side(grad_k).astype(jnp.bfloat16),
        side_by_side(grad_v).astype(jnp.bfloat16),
    )


def bit_steps(size):
    assert size & (size - 1) == 0
    return [1 << b for b in range(size.bit_length() - 1)]


def chunk_order(size, steps):
    places = []
    for member in range(size):
        place = 0
        for step in steps:
            place = place * 2 + (member // step) % 2
        places.append(place)
    order = [0] * size
    for member, place in enumerate(places):
        order[place] = member
    return order


def reorder_cols(matrix, order):
    pieces = jnp.split(matrix, len(order), 1)
    return jnp.concatenate([pieces[k] for k in order], 1)


def halving(arrays, axis, size, steps):
    index = lax.axis_index(axis)
    for step in steps:
        bit = (index // step) % 2
        keeps, sends = [], []
        for array in arrays:
            pair = array.reshape(2, array.shape[0] // 2, *array.shape[1:])
            keeps.append(lax.dynamic_index_in_dim(pair, bit, 0, keepdims=False))
            sends.append(
                lax.dynamic_index_in_dim(pair, 1 - bit, 0, keepdims=False).astype(jnp.bfloat16)
            )
        got = lax.ppermute(jnp.concatenate(sends, 0), axis, [(a, a ^ step) for a in range(size)])
        arrays, offset = [], 0
        for keep in keeps:
            arrays.append(keep + got[offset : offset + keep.shape[0]].astype(jnp.float32))
            offset += keep.shape[0]
    return arrays


def direct_reduce(buf, axis, size):
    index = lax.axis_index(axis)
    chunks = buf.reshape(size, buf.shape[0] // size, *buf.shape[1:])
    total = lax.dynamic_index_in_dim(chunks, index, 0, keepdims=False)
    for shift in range(1, size):
        send = lax.dynamic_index_in_dim(chunks, (index + shift) % size, 0, keepdims=False)
        got = lax.ppermute(
            send.astype(jnp.bfloat16), axis, [(a, (a + shift) % size) for a in range(size)]
        )
        total = total + got.astype(jnp.float32)
    mine = total.astype(jnp.bfloat16)
    result = jnp.zeros((size, *mine.shape), jnp.bfloat16)
    result = lax.dynamic_update_index_in_dim(result, mine, index, 0)
    for shift in range(1, size):
        got = lax.ppermute(mine, axis, [(a, (a + shift) % size) for a in range(size)])
        result = lax.dynamic_update_index_in_dim(result, got, (index - shift) % size, 0)
    return result.reshape(buf.shape)


def gather_small(pieces):
    packed = jnp.concatenate(pieces)
    shards = lax.all_gather(packed, "shard", axis=0, tiled=False)
    fulls, offset = [], 0
    for piece in pieces:
        width = piece.shape[0]
        fulls.append(shards[:, offset : offset + width].reshape(-1))
        offset += width
    return fulls


def body_inner(
    tokens,
    cont_segment,
    cotangent,
    ln1_gain,
    ln1_bias,
    w_qkv,
    q_bias,
    v_bias,
    w_out,
    b_out,
    ln2_gain,
    ln2_bias,
    w_up,
    b_up,
    w_down,
    b_down,
):
    shard_count = lax.psum(1, "shard")
    full_g1, full_s1, full_qb, full_vb, full_bo, full_g2, full_s2, full_bu, full_bd = gather_small(
        [ln1_gain, ln1_bias, q_bias, v_bias, b_out, ln2_gain, ln2_bias, b_up, b_down]
    )
    full_qkv = lax.all_gather(w_qkv, "shard", axis=1, tiled=True)
    full_out = lax.all_gather(w_out, "shard", axis=0, tiled=True)
    full_up = lax.all_gather(w_up, "shard", axis=1, tiled=True)
    full_down = lax.all_gather(w_down, "shard", axis=0, tiled=True)
    inputs = tokens[0].astype(jnp.float32)
    _, model_width = inputs.shape
    distance, allowed = layout(cont_segment[0])
    normed = normalize(inputs, full_g1.astype(jnp.float32), full_s1.astype(jnp.float32)).astype(
        jnp.bfloat16
    )
    projected = jnp.dot(normed, full_qkv, preferred_element_type=jnp.float32)
    queries = (projected[:, :model_width] + full_qb.astype(jnp.float32)).astype(jnp.bfloat16)
    key_rows = projected[:, model_width : 2 * model_width].astype(jnp.bfloat16)
    values = (projected[:, 2 * model_width :] + full_vb.astype(jnp.float32)).astype(jnp.bfloat16)
    mixed, log_norms = attend_forward(queries, key_rows, values, distance, allowed)
    branch = jnp.dot(mixed, full_out, preferred_element_type=jnp.float32) + full_bo.astype(
        jnp.float32
    )
    middle = inputs + branch
    normed_two = normalize(middle, full_g2.astype(jnp.float32), full_s2.astype(jnp.float32)).astype(
        jnp.bfloat16
    )
    pre_act = jnp.dot(normed_two, full_up, preferred_element_type=jnp.float32) + full_bu.astype(
        jnp.float32
    )
    activated = jax.nn.gelu(pre_act, approximate=True).astype(jnp.bfloat16)
    cot_low = cotangent[0]
    shard_steps = bit_steps(shard_count)
    order = chunk_order(shard_count, shard_steps)
    grad_down = jnp.einsum(
        "tf,to->fo", reorder_cols(activated, order), cot_low, preferred_element_type=jnp.float32
    )
    down_half = halving([grad_down], "shard", shard_count, shard_steps[:1])
    down_half, full_down = lax.optimization_barrier((down_half, full_down))
    outputs = middle + (
        jnp.dot(activated, full_down, preferred_element_type=jnp.float32)
        + full_bd.astype(jnp.float32)
    )
    back_g1, back_qkv, back_out, back_g2, back_up, back_down = (
        full_g1, full_qkv, full_out, full_g2, full_up, full_down
    )
    cot_full = cot_low.astype(jnp.float32)
    zero_shift = jnp.zeros((model_width,), jnp.float32)
    grad_bd = jnp.sum(cot_full, 0)
    grad_act = jnp.einsum("to,fo->tf", cot_low, back_down, preferred_element_type=jnp.float32)
    _, gelu_pull = jax.vjp(partial(jax.nn.gelu, approximate=True), pre_act)
    grad_pre = gelu_pull(grad_act)[0].astype(jnp.bfloat16)
    grad_bu = jnp.sum(grad_pre.astype(jnp.float32), 0)
    (down_own,) = halving(down_half, "shard", shard_count, shard_steps[1:])
    total_a1 = lax.psum(down_own.astype(jnp.bfloat16), "rep")
    grad_up_t = jnp.einsum(
        "tf,ti->fi", reorder_cols(grad_pre, order), normed_two, preferred_element_type=jnp.float32
    )
    grad_normed_two = jnp.einsum("tf,if->ti", grad_pre, back_up, preferred_element_type=jnp.float32)
    _, norm_pull_two = jax.vjp(normalize, middle, back_g2.astype(jnp.float32), zero_shift)
    grad_mid_part, grad_g2, grad_s2 = norm_pull_two(grad_normed_two)
    grad_middle = cot_full + grad_mid_part
    grad_branch = grad_middle.astype(jnp.bfloat16)
    grad_bo = jnp.sum(grad_branch.astype(jnp.float32), 0)
    grad_mixed = jnp.einsum(
        "to,io->ti", grad_branch, back_out, preferred_element_type=jnp.float32
    ).astype(jnp.bfloat16)
    grad_out = jnp.einsum(
        "ti,to->io", reorder_cols(mixed, order), grad_branch, preferred_element_type=jnp.float32
    )
    up_own, out_own = halving([grad_up_t, grad_out], "shard", shard_count, shard_steps)
    owned_a = [up_own.astype(jnp.bfloat16).T, out_own.astype(jnp.bfloat16)]
    joined_a = jnp.concatenate(owned_a, 0)
    down_fin, joined_a = lax.optimization_barrier((total_a1.astype(jnp.float32), joined_a))
    total_a = lax.psum(joined_a, "rep")
    grad_q, grad_k, grad_v = attend_backward(
        queries, key_rows, values, grad_mixed, log_norms, distance, allowed
    )
    grad_proj = jnp.concatenate([grad_q, grad_k, grad_v], 1)
    reps = lax.psum(1, "rep")
    grad_qkv_t = jnp.einsum(
        "tc,ti->ci", reorder_cols(grad_proj, order), normed, preferred_element_type=jnp.float32
    )
    qkv_half = halving([grad_qkv_t], "shard", shard_count, shard_steps[:1])
    qkv_half, grad_proj = lax.optimization_barrier((qkv_half, grad_proj))
    (qkv_own,) = halving(qkv_half, "shard", shard_count, shard_steps[1:])
    total_b = direct_reduce(qkv_own, "rep", reps)
    grad_qb = jnp.sum(grad_q.astype(jnp.float32), 0)
    grad_vb = jnp.sum(grad_v.astype(jnp.float32), 0)
    grad_normed = jnp.einsum("tc,ic->ti", grad_proj, back_qkv, preferred_element_type=jnp.float32)
    _, norm_pull_one = jax.vjp(normalize, inputs, back_g1.astype(jnp.float32), zero_shift)
    grad_in_part, grad_g1, grad_s1 = norm_pull_one(grad_normed)
    grad_inputs = grad_middle + grad_in_part
    smalls = [grad_g1, grad_s1, grad_qb, grad_vb, grad_bo, grad_g2, grad_s2, grad_bu, grad_bd]
    small_rows = jnp.concatenate([g.reshape(shard_count, -1) for g in smalls], 1)
    small_rows = small_rows.reshape(shard_count, -1, model_width)
    pad_to = small_rows.shape[1] + (-small_rows.shape[1] % reps)
    small_rows = jnp.pad(small_rows, ((0, 0), (0, pad_to - small_rows.shape[1]), (0, 0)))
    small_rows = jnp.concatenate([small_rows[k] for k in order], 0)
    (small_own,) = halving([small_rows], "shard", shard_count, shard_steps)
    total_s = direct_reduce(small_own, "rep", reps)
    up_rows = up_own.shape[0]
    up_fin = total_a[:up_rows].astype(jnp.float32)
    out_fin = total_a[up_rows:].astype(jnp.float32)
    qkv_fin = total_b.astype(jnp.float32).T
    small_flat = total_s.reshape(-1).astype(jnp.float32)
    small_fin, offset = [], 0
    for g in smalls:
        width = g.shape[0] // shard_count
        small_fin.append(small_flat[offset : offset + width])
        offset += width
    g1_fin, s1_fin, qb_fin, vb_fin, bo_fin, g2_fin, s2_fin, bu_fin, bd_fin = small_fin
    return (
        outputs.astype(jnp.bfloat16)[None],
        grad_inputs.astype(jnp.bfloat16)[None],
        g1_fin,
        s1_fin,
        qkv_fin,
        qb_fin,
        vb_fin,
        out_fin,
        bo_fin,
        g2_fin,
        s2_fin,
        up_fin,
        bu_fin,
        down_fin,
        bd_fin,
    )


def solution(mesh):
    return jax.shard_map(
        body_inner,
        mesh=mesh,
        in_specs=(
            P(("rep", "shard"), None, None),
            P(("rep", "shard"), None, None),
            P(("rep", "shard"), None, None),
            P("shard"),
            P("shard"),
            P(None, "shard"),
            P("shard"),
            P("shard"),
            P("shard", None),
            P("shard"),
            P("shard"),
            P("shard"),
            P(None, "shard"),
            P("shard"),
            P("shard", None),
            P("shard"),
        ),
        out_specs=(
            P(("rep", "shard"), None, None),
            P(("rep", "shard"), None, None),
            P("shard"),
            P("shard"),
            P(None, "shard"),
            P("shard"),
            P("shard"),
            P("shard", None),
            P("shard"),
            P("shard"),
            P("shard"),
            P(None, "shard"),
            P("shard"),
            P("shard", None),
            P("shard"),
        ),
        check_vma=False,
    )
```

```python
from functools import partial

import jax
import jax.numpy as jnp
from jax import lax
from jax.sharding import PartitionSpec as P


HEADS = 16
HDIM = 64
PROMPT = 256


def normalize(values, gain, shift):
    center = values - jnp.mean(values, -1, keepdims=True)
    spread = jnp.mean(center * center, -1, keepdims=True)
    return center * lax.rsqrt(spread + 1e-05) * gain + shift


def layout(segments):
    micros, row_count = segments.shape
    same_seg = segments[:, :, None] == segments[:, None, :]
    earlier = jnp.arange(row_count)[None, :] < jnp.arange(row_count)[:, None]
    offsets = jnp.sum(jnp.where(same_seg & earlier[None], 1, 0), -1).astype(jnp.int32)
    cont_pos = PROMPT + offsets
    owners = jnp.arange(micros, dtype=jnp.int32)[:, None] * row_count + segments
    positions = jnp.concatenate([jnp.arange(PROMPT, dtype=jnp.int32), cont_pos.reshape(-1)])
    groups = jnp.concatenate([jnp.full((PROMPT,), -1, jnp.int32), owners.reshape(-1)])
    places = jnp.arange(positions.shape[0], dtype=jnp.int32)
    allowed = (places[None, :] <= places[:, None]) & (
        (places[None, :] < PROMPT) | (groups[None, :] == groups[:, None])
    )
    distance = (positions[:, None] - positions[None, :]).astype(jnp.float32)
    return (distance, allowed)


def head_slice(matrix, block):
    block_width = 4 * HDIM
    part = lax.dynamic_slice_in_dim(matrix, block * block_width, block_width, 1)
    return part.reshape(matrix.shape[0], 4, HDIM)


def block_scores(q_part, k_part, block, distance, allowed):
    heads = (block * 4 + jnp.arange(4, dtype=jnp.int32)).astype(jnp.float32)
    slopes = jnp.exp2(-8.0 * (heads + 1.0) / HEADS)
    scores = jnp.einsum(
        "qhd,khd->hqk", q_part, k_part, preferred_element_type=jnp.float32
    ) * HDIM ** (-0.5)
    scores = scores - slopes[:, None, None] * distance[None]
    return jnp.where(allowed[None], scores, -jnp.inf)


def side_by_side(blocks):
    return jnp.transpose(blocks, (1, 0, 2)).reshape(
        blocks.shape[1], blocks.shape[0] * blocks.shape[2]
    )


def attend_forward(queries, key_rows, values, distance, allowed):
    length = queries.shape[0]

    def head_block(block):
        q_part = head_slice(queries, block)
        k_part = head_slice(key_rows, block)
        v_part = head_slice(values, block)
        scores = block_scores(q_part, k_part, block, distance, allowed)
        peak = jnp.max(scores, -1, keepdims=True)
        exps_rel = jnp.exp(scores - peak)
        row_totals = jnp.sum(exps_rel, -1, keepdims=True)
        attn_probs = (exps_rel / row_totals).astype(jnp.bfloat16)
        mixed = jnp.einsum("hqk,khd->qhd", attn_probs, v_part, preferred_element_type=jnp.float32)
        return (mixed.reshape(length, 4 * HDIM), (peak + jnp.log(row_totals))[:, :, 0])

    mixed, log_norms = lax.map(head_block, jnp.arange(HEADS // 4, dtype=jnp.int32))
    return (side_by_side(mixed).astype(jnp.bfloat16), log_norms)


def attend_backward(queries, key_rows, values, grad_mixed, log_norms, distance, allowed):
    length = queries.shape[0]
    scale = HDIM ** (-0.5)

    def head_block(block):
        q_part = head_slice(queries, block)
        k_part = head_slice(key_rows, block)
        v_part = head_slice(values, block)
        g_part = head_slice(grad_mixed, block)
        scores = block_scores(q_part, k_part, block, distance, allowed)
        attn_probs = jnp.exp(scores - log_norms[block][:, :, None])
        grad_probs = jnp.einsum("qhd,khd->hqk", g_part, v_part, preferred_element_type=jnp.float32)
        inner = jnp.sum(attn_probs * grad_probs, -1, keepdims=True)
        grad_scores = (attn_probs * (grad_probs - inner)).astype(jnp.bfloat16)
        grad_q = (
            jnp.einsum("hqk,khd->qhd", grad_scores, k_part, preferred_element_type=jnp.float32)
            * scale
        )
        grad_k = (
            jnp.einsum("hqk,qhd->khd", grad_scores, q_part, preferred_element_type=jnp.float32)
            * scale
        )
        grad_v = jnp.einsum(
            "hqk,qhd->khd",
            attn_probs.astype(jnp.bfloat16),
            g_part,
            preferred_element_type=jnp.float32,
        )
        block_width = 4 * HDIM
        return (
            grad_q.reshape(length, block_width),
            grad_k.reshape(length, block_width),
            grad_v.reshape(length, block_width),
        )

    grad_q, grad_k, grad_v = lax.map(head_block, jnp.arange(HEADS // 4, dtype=jnp.int32))
    return (
        side_by_side(grad_q).astype(jnp.bfloat16),
        side_by_side(grad_k).astype(jnp.bfloat16),
        side_by_side(grad_v).astype(jnp.bfloat16),
    )


def bit_steps(size):
    assert size & (size - 1) == 0
    return [1 << b for b in range(size.bit_length() - 1)]


def chunk_order(size, steps):
    places = []
    for member in range(size):
        place = 0
        for step in steps:
            place = place * 2 + (member // step) % 2
        places.append(place)
    order = [0] * size
    for member, place in enumerate(places):
        order[place] = member
    return order


def reorder_cols(matrix, order):
    pieces = jnp.split(matrix, len(order), 1)
    return jnp.concatenate([pieces[k] for k in order], 1)


def halving(arrays, axis, size, steps):
    index = lax.axis_index(axis)
    for step in steps:
        bit = (index // step) % 2
        keeps, sends = [], []
        for array in arrays:
            pair = array.reshape(2, array.shape[0] // 2, *array.shape[1:])
            keeps.append(lax.dynamic_index_in_dim(pair, bit, 0, keepdims=False))
            sends.append(
                lax.dynamic_index_in_dim(pair, 1 - bit, 0, keepdims=False).astype(jnp.bfloat16)
            )
        got = lax.ppermute(jnp.concatenate(sends, 0), axis, [(a, a ^ step) for a in range(size)])
        arrays, offset = [], 0
        for keep in keeps:
            arrays.append(keep + got[offset : offset + keep.shape[0]].astype(jnp.float32))
            offset += keep.shape[0]
    return arrays


def direct_reduce(buf, axis, size):
    index = lax.axis_index(axis)
    chunks = buf.reshape(size, buf.shape[0] // size, *buf.shape[1:])
    total = lax.dynamic_index_in_dim(chunks, index, 0, keepdims=False)
    for shift in range(1, size):
        send = lax.dynamic_index_in_dim(chunks, (index + shift) % size, 0, keepdims=False)
        got = lax.ppermute(
            send.astype(jnp.bfloat16), axis, [(a, (a + shift) % size) for a in range(size)]
        )
        total = total + got.astype(jnp.float32)
    mine = total.astype(jnp.bfloat16)
    result = jnp.zeros((size, *mine.shape), jnp.bfloat16)
    result = lax.dynamic_update_index_in_dim(result, mine, index, 0)
    for shift in range(1, size):
        got = lax.ppermute(mine, axis, [(a, (a + shift) % size) for a in range(size)])
        result = lax.dynamic_update_index_in_dim(result, got, (index - shift) % size, 0)
    return result.reshape(buf.shape)


def gather_small(pieces):
    packed = jnp.concatenate(pieces)
    shards = lax.all_gather(packed, "shard", axis=0, tiled=False)
    fulls, offset = [], 0
    for piece in pieces:
        width = piece.shape[0]
        fulls.append(shards[:, offset : offset + width].reshape(-1))
        offset += width
    return fulls


def body_inner(
    tokens,
    cont_segment,
    cotangent,
    ln1_gain,
    ln1_bias,
    w_qkv,
    q_bias,
    v_bias,
    w_out,
    b_out,
    ln2_gain,
    ln2_bias,
    w_up,
    b_up,
    w_down,
    b_down,
):
    shard_count = lax.psum(1, "shard")
    full_g1, full_s1, full_qb, full_vb, full_bo, full_g2, full_s2, full_bu, full_bd = gather_small(
        [ln1_gain, ln1_bias, q_bias, v_bias, b_out, ln2_gain, ln2_bias, b_up, b_down]
    )
    full_qkv = lax.all_gather(w_qkv, "shard", axis=1, tiled=True)
    full_out = lax.all_gather(w_out, "shard", axis=0, tiled=True)
    full_up = lax.all_gather(w_up, "shard", axis=1, tiled=True)
    full_down = lax.all_gather(w_down, "shard", axis=0, tiled=True)
    inputs = tokens[0].astype(jnp.float32)
    _, model_width = inputs.shape
    distance, allowed = layout(cont_segment[0])
    normed = normalize(inputs, full_g1.astype(jnp.float32), full_s1.astype(jnp.float32)).astype(
        jnp.bfloat16
    )
    projected = jnp.dot(normed, full_qkv, preferred_element_type=jnp.float32)
    queries = (projected[:, :model_width] + full_qb.astype(jnp.float32)).astype(jnp.bfloat16)
    key_rows = projected[:, model_width : 2 * model_width].astype(jnp.bfloat16)
    values = (projected[:, 2 * model_width :] + full_vb.astype(jnp.float32)).astype(jnp.bfloat16)
    mixed, log_norms = attend_forward(queries, key_rows, values, distance, allowed)
    branch = jnp.dot(mixed, full_out, preferred_element_type=jnp.float32) + full_bo.astype(
        jnp.float32
    )
    middle = inputs + branch
    normed_two = normalize(middle, full_g2.astype(jnp.float32), full_s2.astype(jnp.float32)).astype(
        jnp.bfloat16
    )
    pre_act = jnp.dot(normed_two, full_up, preferred_element_type=jnp.float32) + full_bu.astype(
        jnp.float32
    )
    activated = jax.nn.gelu(pre_act, approximate=True).astype(jnp.bfloat16)
    cot_low = cotangent[0]
    shard_steps = bit_steps(shard_count)
    order = chunk_order(shard_count, shard_steps)
    grad_down = jnp.einsum(
        "tf,to->fo", reorder_cols(activated, order), cot_low, preferred_element_type=jnp.float32
    )
    down_half = halving([grad_down], "shard", shard_count, shard_steps[:1])
    down_half, full_down = lax.optimization_barrier((down_half, full_down))
    outputs = middle + (
        jnp.dot(activated, full_down, preferred_element_type=jnp.float32)
        + full_bd.astype(jnp.float32)
    )
    back_g1, back_qkv, back_out, back_g2, back_up, back_down = (
        full_g1, full_qkv, full_out, full_g2, full_up, full_down
    )
    cot_full = cot_low.astype(jnp.float32)
    zero_shift = jnp.zeros((model_width,), jnp.float32)
    grad_bd = jnp.sum(cot_full, 0)
    grad_act = jnp.einsum("to,fo->tf", cot_low, back_down, preferred_element_type=jnp.float32)
    _, gelu_pull = jax.vjp(partial(jax.nn.gelu, approximate=True), pre_act)
    grad_pre = gelu_pull(grad_act)[0].astype(jnp.bfloat16)
    grad_bu = jnp.sum(grad_pre.astype(jnp.float32), 0)
    (down_own,) = halving(down_half, "shard", shard_count, shard_steps[1:])
    total_a1 = lax.psum(down_own.astype(jnp.bfloat16), "rep")
    grad_up_t = jnp.einsum(
        "tf,ti->fi", reorder_cols(grad_pre, order), normed_two, preferred_element_type=jnp.float32
    )
    grad_normed_two = jnp.einsum("tf,if->ti", grad_pre, back_up, preferred_element_type=jnp.float32)
    _, norm_pull_two = jax.vjp(normalize, middle, back_g2.astype(jnp.float32), zero_shift)
    grad_mid_part, grad_g2, grad_s2 = norm_pull_two(grad_normed_two)
    grad_middle = cot_full + grad_mid_part
    grad_branch = grad_middle.astype(jnp.bfloat16)
    grad_bo = jnp.sum(grad_branch.astype(jnp.float32), 0)
    grad_mixed = jnp.einsum(
        "to,io->ti", grad_branch, back_out, preferred_element_type=jnp.float32
    ).astype(jnp.bfloat16)
    grad_out = jnp.einsum(
        "ti,to->io", reorder_cols(mixed, order), grad_branch, preferred_element_type=jnp.float32
    )
    up_own, out_own = halving([grad_up_t, grad_out], "shard", shard_count, shard_steps)
    owned_a = [up_own.astype(jnp.bfloat16).T, out_own.astype(jnp.bfloat16)]
    joined_a = jnp.concatenate(owned_a, 0)
    down_fin, joined_a = lax.optimization_barrier((total_a1.astype(jnp.float32), joined_a))
    total_a = lax.psum(joined_a, "rep")
    grad_q, grad_k, grad_v = attend_backward(
        queries, key_rows, values, grad_mixed, log_norms, distance, allowed
    )
    grad_proj = jnp.concatenate([grad_q, grad_k, grad_v], 1)
    reps = lax.psum(1, "rep")
    grad_qkv_t = jnp.einsum(
        "tc,ti->ci", reorder_cols(grad_proj, order), normed, preferred_element_type=jnp.float32
    )
    qkv_rows = grad_qkv_t.shape[0] // shard_count
    qkv_half = halving([grad_qkv_t], "shard", shard_count, shard_steps[:1])
    qkv_half, grad_proj = lax.optimization_barrier((qkv_half, grad_proj))
    (qkv_own,) = halving(qkv_half, "shard", shard_count, shard_steps[1:])
    grad_qb = jnp.sum(grad_q.astype(jnp.float32), 0)
    grad_vb = jnp.sum(grad_v.astype(jnp.float32), 0)
    grad_normed = jnp.einsum("tc,ic->ti", grad_proj, back_qkv, preferred_element_type=jnp.float32)
    _, norm_pull_one = jax.vjp(normalize, inputs, back_g1.astype(jnp.float32), zero_shift)
    grad_in_part, grad_g1, grad_s1 = norm_pull_one(grad_normed)
    grad_inputs = grad_middle + grad_in_part
    smalls = [grad_g1, grad_s1, grad_qb, grad_vb, grad_bo, grad_g2, grad_s2, grad_bu, grad_bd]
    small_rows = jnp.concatenate([g.reshape(shard_count, -1) for g in smalls], 1)
    small_rows = small_rows.reshape(shard_count, -1, model_width)
    pad_to = small_rows.shape[1] + (-small_rows.shape[1] % reps)
    small_rows = jnp.pad(small_rows, ((0, 0), (0, pad_to - small_rows.shape[1]), (0, 0)))
    small_rows = jnp.concatenate([small_rows[k] for k in order], 0)
    (small_own,) = halving([small_rows], "shard", shard_count, shard_steps)
    total_b = direct_reduce(jnp.concatenate([qkv_own, small_own], 0), "rep", reps)
    total_s = total_b[qkv_rows:]
    total_b = total_b[:qkv_rows]
    up_rows = up_own.shape[0]
    up_fin = total_a[:up_rows].astype(jnp.float32)
    out_fin = total_a[up_rows:].astype(jnp.float32)
    qkv_fin = total_b.astype(jnp.float32).T
    small_flat = total_s.reshape(-1).astype(jnp.float32)
    small_fin, offset = [], 0
    for g in smalls:
        width = g.shape[0] // shard_count
        small_fin.append(small_flat[offset : offset + width])
        offset += width
    g1_fin, s1_fin, qb_fin, vb_fin, bo_fin, g2_fin, s2_fin, bu_fin, bd_fin = small_fin
    return (
        outputs.astype(jnp.bfloat16)[None],
        grad_inputs.astype(jnp.bfloat16)[None],
        g1_fin,
        s1_fin,
        qkv_fin,
        qb_fin,
        vb_fin,
        out_fin,
        bo_fin,
        g2_fin,
        s2_fin,
        up_fin,
        bu_fin,
        down_fin,
        bd_fin,
    )


def solution(mesh):
    return jax.shard_map(
        body_inner,
        mesh=mesh,
        in_specs=(
            P(("rep", "shard"), None, None),
            P(("rep", "shard"), None, None),
            P(("rep", "shard"), None, None),
            P("shard"),
            P("shard"),
            P(None, "shard"),
            P("shard"),
            P("shard"),
            P("shard", None),
            P("shard"),
            P("shard"),
            P("shard"),
            P(None, "shard"),
            P("shard"),
            P("shard", None),
            P("shard"),
        ),
        out_specs=(
            P(("rep", "shard"), None, None),
            P(("rep", "shard"), None, None),
            P("shard"),
            P("shard"),
            P(None, "shard"),
            P("shard"),
            P("shard"),
            P("shard", None),
            P("shard"),
            P("shard"),
            P("shard"),
            P(None, "shard"),
            P("shard"),
            P("shard", None),
            P("shard"),
        ),
        check_vma=False,
    )
```

```python
from functools import partial

import jax
import jax.numpy as jnp
from jax import lax
from jax.sharding import PartitionSpec as P


HEADS = 16
HDIM = 64
PROMPT = 256


def normalize(values, gain, shift):
    center = values - jnp.mean(values, -1, keepdims=True)
    spread = jnp.mean(center * center, -1, keepdims=True)
    return center * lax.rsqrt(spread + 1e-05) * gain + shift


def layout(segments):
    micros, row_count = segments.shape
    same_seg = segments[:, :, None] == segments[:, None, :]
    earlier = jnp.arange(row_count)[None, :] < jnp.arange(row_count)[:, None]
    offsets = jnp.sum(jnp.where(same_seg & earlier[None], 1, 0), -1).astype(jnp.int32)
    cont_pos = PROMPT + offsets
    owners = jnp.arange(micros, dtype=jnp.int32)[:, None] * row_count + segments
    positions = jnp.concatenate([jnp.arange(PROMPT, dtype=jnp.int32), cont_pos.reshape(-1)])
    groups = jnp.concatenate([jnp.full((PROMPT,), -1, jnp.int32), owners.reshape(-1)])
    places = jnp.arange(positions.shape[0], dtype=jnp.int32)
    allowed = (places[None, :] <= places[:, None]) & (
        (places[None, :] < PROMPT) | (groups[None, :] == groups[:, None])
    )
    distance = (positions[:, None] - positions[None, :]).astype(jnp.float32)
    return (distance, allowed)


def head_slice(matrix, block):
    block_width = 4 * HDIM
    part = lax.dynamic_slice_in_dim(matrix, block * block_width, block_width, 1)
    return part.reshape(matrix.shape[0], 4, HDIM)


def block_scores(q_part, k_part, block, distance, allowed):
    heads = (block * 4 + jnp.arange(4, dtype=jnp.int32)).astype(jnp.float32)
    slopes = jnp.exp2(-8.0 * (heads + 1.0) / HEADS)
    scores = jnp.einsum(
        "qhd,khd->hqk", q_part, k_part, preferred_element_type=jnp.float32
    ) * HDIM ** (-0.5)
    scores = scores - slopes[:, None, None] * distance[None]
    return jnp.where(allowed[None], scores, -jnp.inf)


def side_by_side(blocks):
    return jnp.transpose(blocks, (1, 0, 2)).reshape(
        blocks.shape[1], blocks.shape[0] * blocks.shape[2]
    )


def attend_forward(queries, key_rows, values, distance, allowed):
    length = queries.shape[0]

    def head_block(block):
        q_part = head_slice(queries, block)
        k_part = head_slice(key_rows, block)
        v_part = head_slice(values, block)
        scores = block_scores(q_part, k_part, block, distance, allowed)
        peak = jnp.max(scores, -1, keepdims=True)
        exps_rel = jnp.exp(scores - peak)
        row_totals = jnp.sum(exps_rel, -1, keepdims=True)
        attn_probs = (exps_rel / row_totals).astype(jnp.bfloat16)
        mixed = jnp.einsum("hqk,khd->qhd", attn_probs, v_part, preferred_element_type=jnp.float32)
        return (mixed.reshape(length, 4 * HDIM), (peak + jnp.log(row_totals))[:, :, 0])

    mixed, log_norms = lax.map(head_block, jnp.arange(HEADS // 4, dtype=jnp.int32))
    return (side_by_side(mixed).astype(jnp.bfloat16), log_norms)


def attend_backward(queries, key_rows, values, grad_mixed, log_norms, distance, allowed):
    length = queries.shape[0]
    scale = HDIM ** (-0.5)

    def head_block(block):
        q_part = head_slice(queries, block)
        k_part = head_slice(key_rows, block)
        v_part = head_slice(values, block)
        g_part = head_slice(grad_mixed, block)
        scores = block_scores(q_part, k_part, block, distance, allowed)
        attn_probs = jnp.exp(scores - log_norms[block][:, :, None])
        grad_probs = jnp.einsum("qhd,khd->hqk", g_part, v_part, preferred_element_type=jnp.float32)
        inner = jnp.sum(attn_probs * grad_probs, -1, keepdims=True)
        grad_scores = (attn_probs * (grad_probs - inner)).astype(jnp.bfloat16)
        grad_q = (
            jnp.einsum("hqk,khd->qhd", grad_scores, k_part, preferred_element_type=jnp.float32)
            * scale
        )
        grad_k = (
            jnp.einsum("hqk,qhd->khd", grad_scores, q_part, preferred_element_type=jnp.float32)
            * scale
        )
        grad_v = jnp.einsum(
            "hqk,qhd->khd",
            attn_probs.astype(jnp.bfloat16),
            g_part,
            preferred_element_type=jnp.float32,
        )
        block_width = 4 * HDIM
        return (
            grad_q.reshape(length, block_width),
            grad_k.reshape(length, block_width),
            grad_v.reshape(length, block_width),
        )

    grad_q, grad_k, grad_v = lax.map(head_block, jnp.arange(HEADS // 4, dtype=jnp.int32))
    return (
        side_by_side(grad_q).astype(jnp.bfloat16),
        side_by_side(grad_k).astype(jnp.bfloat16),
        side_by_side(grad_v).astype(jnp.bfloat16),
    )


def bit_steps(size):
    assert size & (size - 1) == 0
    return [1 << b for b in range(size.bit_length() - 1)]


def chunk_order(size, steps):
    places = []
    for member in range(size):
        place = 0
        for step in steps:
            place = place * 2 + (member // step) % 2
        places.append(place)
    order = [0] * size
    for member, place in enumerate(places):
        order[place] = member
    return order


def reorder_cols(matrix, order):
    pieces = jnp.split(matrix, len(order), 1)
    return jnp.concatenate([pieces[k] for k in order], 1)


def halving(arrays, axis, size, steps):
    index = lax.axis_index(axis)
    for step in steps:
        bit = (index // step) % 2
        keeps, sends = [], []
        for array in arrays:
            pair = array.reshape(2, array.shape[0] // 2, *array.shape[1:])
            keeps.append(lax.dynamic_index_in_dim(pair, bit, 0, keepdims=False))
            sends.append(
                lax.dynamic_index_in_dim(pair, 1 - bit, 0, keepdims=False).astype(jnp.bfloat16)
            )
        got = lax.ppermute(jnp.concatenate(sends, 0), axis, [(a, a ^ step) for a in range(size)])
        arrays, offset = [], 0
        for keep in keeps:
            arrays.append(keep + got[offset : offset + keep.shape[0]].astype(jnp.float32))
            offset += keep.shape[0]
    return arrays


def direct_reduce(buf, axis, size):
    index = lax.axis_index(axis)
    chunks = buf.reshape(size, buf.shape[0] // size, *buf.shape[1:])
    total = lax.dynamic_index_in_dim(chunks, index, 0, keepdims=False)
    for shift in range(1, size):
        send = lax.dynamic_index_in_dim(chunks, (index + shift) % size, 0, keepdims=False)
        got = lax.ppermute(
            send.astype(jnp.bfloat16), axis, [(a, (a + shift) % size) for a in range(size)]
        )
        total = total + got.astype(jnp.float32)
    mine = total.astype(jnp.bfloat16)
    result = jnp.zeros((size, *mine.shape), jnp.bfloat16)
    result = lax.dynamic_update_index_in_dim(result, mine, index, 0)
    for shift in range(1, size):
        got = lax.ppermute(mine, axis, [(a, (a + shift) % size) for a in range(size)])
        result = lax.dynamic_update_index_in_dim(result, got, (index - shift) % size, 0)
    return result.reshape(buf.shape)


def gather_pieces(piece, axis, size, steps, dim):
    index = lax.axis_index(axis)
    buf, first = piece, None
    for step in steps:
        low = (index // step) % 2 == 0
        got = lax.ppermute(buf, axis, [(a, a ^ step) for a in range(size)])
        first = got if first is None else first
        buf = jnp.concatenate([jnp.where(low, buf, got), jnp.where(low, got, buf)], dim)
    return buf, first


def unpermute(full, order, dim):
    pieces = jnp.split(full, len(order), dim)
    return jnp.concatenate([pieces[order.index(k)] for k in range(len(order))], dim)


def gather_small(pieces):
    packed = jnp.concatenate(pieces)
    shards = lax.all_gather(packed, "shard", axis=0, tiled=False)
    fulls, offset = [], 0
    for piece in pieces:
        width = piece.shape[0]
        fulls.append(shards[:, offset : offset + width].reshape(-1))
        offset += width
    return fulls


def body_inner(
    tokens,
    cont_segment,
    cotangent,
    ln1_gain,
    ln1_bias,
    w_qkv,
    q_bias,
    v_bias,
    w_out,
    b_out,
    ln2_gain,
    ln2_bias,
    w_up,
    b_up,
    w_down,
    b_down,
):
    shard_count = lax.psum(1, "shard")
    full_g1, full_s1, full_qb, full_vb, full_bo, full_g2, full_s2, full_bu, full_bd = gather_small(
        [ln1_gain, ln1_bias, q_bias, v_bias, b_out, ln2_gain, ln2_bias, b_up, b_down]
    )
    gather_order = chunk_order(shard_count, bit_steps(shard_count))
    gather_steps = bit_steps(shard_count)[::-1]
    full_qkv, first = gather_pieces(w_qkv, "shard", shard_count, gather_steps, 1)
    first, w_out = lax.optimization_barrier((first, w_out))
    full_out, first = gather_pieces(w_out, "shard", shard_count, gather_steps, 0)
    first, full_qkv, w_up = lax.optimization_barrier((first, full_qkv, w_up))
    full_up, first = gather_pieces(w_up, "shard", shard_count, gather_steps, 1)
    first, full_out, w_down = lax.optimization_barrier((first, full_out, w_down))
    full_down, first = gather_pieces(w_down, "shard", shard_count, gather_steps, 0)
    full_qkv = unpermute(full_qkv, gather_order, 1)
    full_out = unpermute(full_out, gather_order, 0)
    full_up = unpermute(full_up, gather_order, 1)
    full_down = unpermute(full_down, gather_order, 0)
    inputs = tokens[0].astype(jnp.float32)
    _, model_width = inputs.shape
    distance, allowed = layout(cont_segment[0])
    normed = normalize(inputs, full_g1.astype(jnp.float32), full_s1.astype(jnp.float32)).astype(
        jnp.bfloat16
    )
    projected = jnp.dot(normed, full_qkv, preferred_element_type=jnp.float32)
    queries = (projected[:, :model_width] + full_qb.astype(jnp.float32)).astype(jnp.bfloat16)
    key_rows = projected[:, model_width : 2 * model_width].astype(jnp.bfloat16)
    values = (projected[:, 2 * model_width :] + full_vb.astype(jnp.float32)).astype(jnp.bfloat16)
    mixed, log_norms = attend_forward(queries, key_rows, values, distance, allowed)
    branch = jnp.dot(mixed, full_out, preferred_element_type=jnp.float32) + full_bo.astype(
        jnp.float32
    )
    middle = inputs + branch
    normed_two = normalize(middle, full_g2.astype(jnp.float32), full_s2.astype(jnp.float32)).astype(
        jnp.bfloat16
    )
    pre_act = jnp.dot(normed_two, full_up, preferred_element_type=jnp.float32) + full_bu.astype(
        jnp.float32
    )
    activated = jax.nn.gelu(pre_act, approximate=True).astype(jnp.bfloat16)
    cot_low = cotangent[0]
    shard_steps = bit_steps(shard_count)
    order = chunk_order(shard_count, shard_steps)
    grad_down = jnp.einsum(
        "tf,to->fo", reorder_cols(activated, order), cot_low, preferred_element_type=jnp.float32
    )
    down_half = halving([grad_down], "shard", shard_count, shard_steps[:1])
    down_half, full_down = lax.optimization_barrier((down_half, full_down))
    outputs = middle + (
        jnp.dot(activated, full_down, preferred_element_type=jnp.float32)
        + full_bd.astype(jnp.float32)
    )
    back_g1, back_qkv, back_out, back_g2, back_up, back_down = (
        full_g1, full_qkv, full_out, full_g2, full_up, full_down
    )
    cot_full = cot_low.astype(jnp.float32)
    zero_shift = jnp.zeros((model_width,), jnp.float32)
    grad_bd = jnp.sum(cot_full, 0)
    grad_act = jnp.einsum("to,fo->tf", cot_low, back_down, preferred_element_type=jnp.float32)
    _, gelu_pull = jax.vjp(partial(jax.nn.gelu, approximate=True), pre_act)
    grad_pre = gelu_pull(grad_act)[0].astype(jnp.bfloat16)
    grad_bu = jnp.sum(grad_pre.astype(jnp.float32), 0)
    (down_own,) = halving(down_half, "shard", shard_count, shard_steps[1:])
    total_a1 = lax.psum(down_own.astype(jnp.bfloat16), "rep")
    grad_up_t = jnp.einsum(
        "tf,ti->fi", reorder_cols(grad_pre, order), normed_two, preferred_element_type=jnp.float32
    )
    grad_normed_two = jnp.einsum("tf,if->ti", grad_pre, back_up, preferred_element_type=jnp.float32)
    _, norm_pull_two = jax.vjp(normalize, middle, back_g2.astype(jnp.float32), zero_shift)
    grad_mid_part, grad_g2, grad_s2 = norm_pull_two(grad_normed_two)
    grad_middle = cot_full + grad_mid_part
    grad_branch = grad_middle.astype(jnp.bfloat16)
    grad_bo = jnp.sum(grad_branch.astype(jnp.float32), 0)
    grad_mixed = jnp.einsum(
        "to,io->ti", grad_branch, back_out, preferred_element_type=jnp.float32
    ).astype(jnp.bfloat16)
    grad_out = jnp.einsum(
        "ti,to->io", reorder_cols(mixed, order), grad_branch, preferred_element_type=jnp.float32
    )
    up_own, out_own = halving([grad_up_t, grad_out], "shard", shard_count, shard_steps)
    owned_a = [up_own.astype(jnp.bfloat16).T, out_own.astype(jnp.bfloat16)]
    joined_a = jnp.concatenate(owned_a, 0)
    down_fin, joined_a = lax.optimization_barrier((total_a1.astype(jnp.float32), joined_a))
    total_a = lax.psum(joined_a, "rep")
    grad_q, grad_k, grad_v = attend_backward(
        queries, key_rows, values, grad_mixed, log_norms, distance, allowed
    )
    grad_proj = jnp.concatenate([grad_q, grad_k, grad_v], 1)
    reps = lax.psum(1, "rep")
    grad_qkv_t = jnp.einsum(
        "tc,ti->ci", reorder_cols(grad_proj, order), normed, preferred_element_type=jnp.float32
    )
    qkv_rows = grad_qkv_t.shape[0] // shard_count
    qkv_half = halving([grad_qkv_t], "shard", shard_count, shard_steps[:1])
    qkv_half, grad_proj = lax.optimization_barrier((qkv_half, grad_proj))
    (qkv_own,) = halving(qkv_half, "shard", shard_count, shard_steps[1:])
    grad_qb = jnp.sum(grad_q.astype(jnp.float32), 0)
    grad_vb = jnp.sum(grad_v.astype(jnp.float32), 0)
    grad_normed = jnp.einsum("tc,ic->ti", grad_proj, back_qkv, preferred_element_type=jnp.float32)
    _, norm_pull_one = jax.vjp(normalize, inputs, back_g1.astype(jnp.float32), zero_shift)
    grad_in_part, grad_g1, grad_s1 = norm_pull_one(grad_normed)
    grad_inputs = grad_middle + grad_in_part
    smalls = [grad_g1, grad_s1, grad_qb, grad_vb, grad_bo, grad_g2, grad_s2, grad_bu, grad_bd]
    small_rows = jnp.concatenate([g.reshape(shard_count, -1) for g in smalls], 1)
    small_rows = small_rows.reshape(shard_count, -1, model_width)
    pad_to = small_rows.shape[1] + (-small_rows.shape[1] % reps)
    small_rows = jnp.pad(small_rows, ((0, 0), (0, pad_to - small_rows.shape[1]), (0, 0)))
    small_rows = jnp.concatenate([small_rows[k] for k in order], 0)
    (small_own,) = halving([small_rows], "shard", shard_count, shard_steps)
    total_b = direct_reduce(jnp.concatenate([qkv_own, small_own], 0), "rep", reps)
    total_s = total_b[qkv_rows:]
    total_b = total_b[:qkv_rows]
    up_rows = up_own.shape[0]
    up_fin = total_a[:up_rows].astype(jnp.float32)
    out_fin = total_a[up_rows:].astype(jnp.float32)
    qkv_fin = total_b.astype(jnp.float32).T
    small_flat = total_s.reshape(-1).astype(jnp.float32)
    small_fin, offset = [], 0
    for g in smalls:
        width = g.shape[0] // shard_count
        small_fin.append(small_flat[offset : offset + width])
        offset += width
    g1_fin, s1_fin, qb_fin, vb_fin, bo_fin, g2_fin, s2_fin, bu_fin, bd_fin = small_fin
    return (
        outputs.astype(jnp.bfloat16)[None],
        grad_inputs.astype(jnp.bfloat16)[None],
        g1_fin,
        s1_fin,
        qkv_fin,
        qb_fin,
        vb_fin,
        out_fin,
        bo_fin,
        g2_fin,
        s2_fin,
        up_fin,
        bu_fin,
        down_fin,
        bd_fin,
    )


def solution(mesh):
    return jax.shard_map(
        body_inner,
        mesh=mesh,
        in_specs=(
            P(("rep", "shard"), None, None),
            P(("rep", "shard"), None, None),
            P(("rep", "shard"), None, None),
            P("shard"),
            P("shard"),
            P(None, "shard"),
            P("shard"),
            P("shard"),
            P("shard", None),
            P("shard"),
            P("shard"),
            P("shard"),
            P(None, "shard"),
            P("shard"),
            P("shard", None),
            P("shard"),
        ),
        out_specs=(
            P(("rep", "shard"), None, None),
            P(("rep", "shard"), None, None),
            P("shard"),
            P("shard"),
            P(None, "shard"),
            P("shard"),
            P("shard"),
            P("shard", None),
            P("shard"),
            P("shard"),
            P("shard"),
            P(None, "shard"),
            P("shard"),
            P("shard", None),
            P("shard"),
        ),
        check_vma=False,
    )
```

```python
from functools import partial

import jax
import jax.numpy as jnp
from jax import lax
from jax.sharding import PartitionSpec as P


HEADS = 16
HDIM = 64
PROMPT = 256


def normalize(values, gain, shift):
    center = values - jnp.mean(values, -1, keepdims=True)
    spread = jnp.mean(center * center, -1, keepdims=True)
    return center * lax.rsqrt(spread + 1e-05) * gain + shift


def layout(segments):
    micros, row_count = segments.shape
    same_seg = segments[:, :, None] == segments[:, None, :]
    earlier = jnp.arange(row_count)[None, :] < jnp.arange(row_count)[:, None]
    offsets = jnp.sum(jnp.where(same_seg & earlier[None], 1, 0), -1).astype(jnp.int32)
    cont_pos = PROMPT + offsets
    owners = jnp.arange(micros, dtype=jnp.int32)[:, None] * row_count + segments
    positions = jnp.concatenate([jnp.arange(PROMPT, dtype=jnp.int32), cont_pos.reshape(-1)])
    groups = jnp.concatenate([jnp.full((PROMPT,), -1, jnp.int32), owners.reshape(-1)])
    places = jnp.arange(positions.shape[0], dtype=jnp.int32)
    allowed = (places[None, :] <= places[:, None]) & (
        (places[None, :] < PROMPT) | (groups[None, :] == groups[:, None])
    )
    distance = (positions[:, None] - positions[None, :]).astype(jnp.float32)
    return (distance, allowed)


def head_slice(matrix, block):
    block_width = 4 * HDIM
    part = lax.dynamic_slice_in_dim(matrix, block * block_width, block_width, 1)
    return part.reshape(matrix.shape[0], 4, HDIM)


def block_scores(q_part, k_part, block, distance, allowed):
    heads = (block * 4 + jnp.arange(4, dtype=jnp.int32)).astype(jnp.float32)
    slopes = jnp.exp2(-8.0 * (heads + 1.0) / HEADS)
    scores = jnp.einsum(
        "qhd,khd->hqk", q_part, k_part, preferred_element_type=jnp.float32
    ) * HDIM ** (-0.5)
    scores = scores - slopes[:, None, None] * distance[None]
    return jnp.where(allowed[None], scores, -jnp.inf)


def side_by_side(blocks):
    return jnp.transpose(blocks, (1, 0, 2)).reshape(
        blocks.shape[1], blocks.shape[0] * blocks.shape[2]
    )


def attend_forward(queries, key_rows, values, distance, allowed):
    length = queries.shape[0]

    def head_block(block):
        q_part = head_slice(queries, block)
        k_part = head_slice(key_rows, block)
        v_part = head_slice(values, block)
        scores = block_scores(q_part, k_part, block, distance, allowed)
        peak = jnp.max(scores, -1, keepdims=True)
        exps_rel = jnp.exp(scores - peak)
        row_totals = jnp.sum(exps_rel, -1, keepdims=True)
        attn_probs = (exps_rel / row_totals).astype(jnp.bfloat16)
        mixed = jnp.einsum("hqk,khd->qhd", attn_probs, v_part, preferred_element_type=jnp.float32)
        return (mixed.reshape(length, 4 * HDIM), (peak + jnp.log(row_totals))[:, :, 0])

    mixed, log_norms = lax.map(head_block, jnp.arange(HEADS // 4, dtype=jnp.int32))
    return (side_by_side(mixed).astype(jnp.bfloat16), log_norms)


def attend_backward(queries, key_rows, values, grad_mixed, log_norms, distance, allowed):
    length = queries.shape[0]
    scale = HDIM ** (-0.5)

    def head_block(block):
        q_part = head_slice(queries, block)
        k_part = head_slice(key_rows, block)
        v_part = head_slice(values, block)
        g_part = head_slice(grad_mixed, block)
        scores = block_scores(q_part, k_part, block, distance, allowed)
        attn_probs = jnp.exp(scores - log_norms[block][:, :, None])
        grad_probs = jnp.einsum("qhd,khd->hqk", g_part, v_part, preferred_element_type=jnp.float32)
        inner = jnp.sum(attn_probs * grad_probs, -1, keepdims=True)
        grad_scores = (attn_probs * (grad_probs - inner)).astype(jnp.bfloat16)
        grad_q = (
            jnp.einsum("hqk,khd->qhd", grad_scores, k_part, preferred_element_type=jnp.float32)
            * scale
        )
        grad_k = (
            jnp.einsum("hqk,qhd->khd", grad_scores, q_part, preferred_element_type=jnp.float32)
            * scale
        )
        grad_v = jnp.einsum(
            "hqk,qhd->khd",
            attn_probs.astype(jnp.bfloat16),
            g_part,
            preferred_element_type=jnp.float32,
        )
        block_width = 4 * HDIM
        return (
            grad_q.reshape(length, block_width),
            grad_k.reshape(length, block_width),
            grad_v.reshape(length, block_width),
        )

    grad_q, grad_k, grad_v = lax.map(head_block, jnp.arange(HEADS // 4, dtype=jnp.int32))
    return (
        side_by_side(grad_q).astype(jnp.bfloat16),
        side_by_side(grad_k).astype(jnp.bfloat16),
        side_by_side(grad_v).astype(jnp.bfloat16),
    )


def bit_steps(size):
    assert size & (size - 1) == 0
    return [1 << b for b in range(size.bit_length() - 1)]


def chunk_order(size, steps):
    places = []
    for member in range(size):
        place = 0
        for step in steps:
            place = place * 2 + (member // step) % 2
        places.append(place)
    order = [0] * size
    for member, place in enumerate(places):
        order[place] = member
    return order


def reorder_cols(matrix, order):
    pieces = jnp.split(matrix, len(order), 1)
    return jnp.concatenate([pieces[k] for k in order], 1)


def halving(arrays, axis, size, steps):
    index = lax.axis_index(axis)
    for step in steps:
        bit = (index // step) % 2
        keeps, sends = [], []
        for array in arrays:
            pair = array.reshape(2, array.shape[0] // 2, *array.shape[1:])
            keeps.append(lax.dynamic_index_in_dim(pair, bit, 0, keepdims=False))
            sends.append(
                lax.dynamic_index_in_dim(pair, 1 - bit, 0, keepdims=False).astype(jnp.bfloat16)
            )
        got = lax.ppermute(jnp.concatenate(sends, 0), axis, [(a, a ^ step) for a in range(size)])
        arrays, offset = [], 0
        for keep in keeps:
            arrays.append(keep + got[offset : offset + keep.shape[0]].astype(jnp.float32))
            offset += keep.shape[0]
    return arrays


def direct_reduce(buf, axis, size):
    index = lax.axis_index(axis)
    chunks = buf.reshape(size, buf.shape[0] // size, *buf.shape[1:])
    total = lax.dynamic_index_in_dim(chunks, index, 0, keepdims=False)
    low_chunks = chunks.astype(jnp.bfloat16)
    for shift in range(1, size):
        partner = lax.bitwise_xor(index, shift)
        send = lax.dynamic_index_in_dim(low_chunks, partner, 0, keepdims=False)
        got = lax.ppermute(send, axis, [(a, a ^ shift) for a in range(size)])
        total = total + got.astype(jnp.float32)
    mine = total.astype(jnp.bfloat16)
    result = jnp.zeros((size, *mine.shape), jnp.bfloat16)
    result = lax.dynamic_update_index_in_dim(result, mine, index, 0)
    for shift in range(1, size):
        got = lax.ppermute(mine, axis, [(a, a ^ shift) for a in range(size)])
        result = lax.dynamic_update_index_in_dim(result, got, lax.bitwise_xor(index, shift), 0)
    return result.reshape(buf.shape)


def gather_small(pieces):
    packed = jnp.concatenate(pieces)
    shards = lax.all_gather(packed, "shard", axis=0, tiled=False)
    fulls, offset = [], 0
    for piece in pieces:
        width = piece.shape[0]
        fulls.append(shards[:, offset : offset + width].reshape(-1))
        offset += width
    return fulls


def body_inner(
    tokens,
    cont_segment,
    cotangent,
    ln1_gain,
    ln1_bias,
    w_qkv,
    q_bias,
    v_bias,
    w_out,
    b_out,
    ln2_gain,
    ln2_bias,
    w_up,
    b_up,
    w_down,
    b_down,
):
    shard_count = lax.psum(1, "shard")
    full_g1, full_s1, full_qb, full_vb, full_bo, full_g2, full_s2, full_bu, full_bd = gather_small(
        [ln1_gain, ln1_bias, q_bias, v_bias, b_out, ln2_gain, ln2_bias, b_up, b_down]
    )
    full_qkv = lax.all_gather(w_qkv, "shard", axis=1, tiled=True)
    full_out = lax.all_gather(w_out, "shard", axis=0, tiled=True)
    full_up = lax.all_gather(w_up, "shard", axis=1, tiled=True)
    full_down = lax.all_gather(w_down, "shard", axis=0, tiled=True)
    inputs = tokens[0].astype(jnp.float32)
    _, model_width = inputs.shape
    distance, allowed = layout(cont_segment[0])
    normed = normalize(inputs, full_g1.astype(jnp.float32), full_s1.astype(jnp.float32)).astype(
        jnp.bfloat16
    )
    projected = jnp.dot(normed, full_qkv, preferred_element_type=jnp.float32)
    queries = (projected[:, :model_width] + full_qb.astype(jnp.float32)).astype(jnp.bfloat16)
    key_rows = projected[:, model_width : 2 * model_width].astype(jnp.bfloat16)
    values = (projected[:, 2 * model_width :] + full_vb.astype(jnp.float32)).astype(jnp.bfloat16)
    mixed, log_norms = attend_forward(queries, key_rows, values, distance, allowed)
    branch = jnp.dot(mixed, full_out, preferred_element_type=jnp.float32) + full_bo.astype(
        jnp.float32
    )
    middle = inputs + branch
    normed_two = normalize(middle, full_g2.astype(jnp.float32), full_s2.astype(jnp.float32)).astype(
        jnp.bfloat16
    )
    pre_act = jnp.dot(normed_two, full_up, preferred_element_type=jnp.float32) + full_bu.astype(
        jnp.float32
    )
    activated = jax.nn.gelu(pre_act, approximate=True).astype(jnp.bfloat16)
    cot_low = cotangent[0]
    shard_steps = bit_steps(shard_count)
    order = chunk_order(shard_count, shard_steps)
    grad_down = jnp.einsum(
        "tf,to->fo", reorder_cols(activated, order), cot_low, preferred_element_type=jnp.float32
    )
    down_half = halving([grad_down], "shard", shard_count, shard_steps[:1])
    down_half, full_down = lax.optimization_barrier((down_half, full_down))
    outputs = middle + (
        jnp.dot(activated, full_down, preferred_element_type=jnp.float32)
        + full_bd.astype(jnp.float32)
    )
    back_g1, back_qkv, back_out, back_g2, back_up, back_down = (
        full_g1, full_qkv, full_out, full_g2, full_up, full_down
    )
    cot_full = cot_low.astype(jnp.float32)
    zero_shift = jnp.zeros((model_width,), jnp.float32)
    grad_bd = jnp.sum(cot_full, 0)
    grad_act = jnp.einsum("to,fo->tf", cot_low, back_down, preferred_element_type=jnp.float32)
    _, gelu_pull = jax.vjp(partial(jax.nn.gelu, approximate=True), pre_act)
    grad_pre = gelu_pull(grad_act)[0].astype(jnp.bfloat16)
    grad_bu = jnp.sum(grad_pre.astype(jnp.float32), 0)
    (down_own,) = halving(down_half, "shard", shard_count, shard_steps[1:])
    total_a1 = lax.psum(down_own.astype(jnp.bfloat16), "rep")
    grad_up_t = jnp.einsum(
        "tf,ti->fi", reorder_cols(grad_pre, order), normed_two, preferred_element_type=jnp.float32
    )
    grad_normed_two = jnp.einsum("tf,if->ti", grad_pre, back_up, preferred_element_type=jnp.float32)
    _, norm_pull_two = jax.vjp(normalize, middle, back_g2.astype(jnp.float32), zero_shift)
    grad_mid_part, grad_g2, grad_s2 = norm_pull_two(grad_normed_two)
    grad_middle = cot_full + grad_mid_part
    grad_branch = grad_middle.astype(jnp.bfloat16)
    grad_bo = jnp.sum(grad_branch.astype(jnp.float32), 0)
    grad_mixed = jnp.einsum(
        "to,io->ti", grad_branch, back_out, preferred_element_type=jnp.float32
    ).astype(jnp.bfloat16)
    grad_out = jnp.einsum(
        "ti,to->io", reorder_cols(mixed, order), grad_branch, preferred_element_type=jnp.float32
    )
    up_own, out_own = halving([grad_up_t, grad_out], "shard", shard_count, shard_steps)
    owned_a = [up_own.astype(jnp.bfloat16).T, out_own.astype(jnp.bfloat16)]
    joined_a = jnp.concatenate(owned_a, 0)
    down_fin, joined_a = lax.optimization_barrier((total_a1.astype(jnp.float32), joined_a))
    total_a = lax.psum(joined_a, "rep")
    grad_q, grad_k, grad_v = attend_backward(
        queries, key_rows, values, grad_mixed, log_norms, distance, allowed
    )
    grad_proj = jnp.concatenate([grad_q, grad_k, grad_v], 1)
    reps = lax.psum(1, "rep")
    grad_qkv_t = jnp.einsum(
        "tc,ti->ci", reorder_cols(grad_proj, order), normed, preferred_element_type=jnp.float32
    )
    qkv_rows = grad_qkv_t.shape[0] // shard_count
    qkv_half = halving([grad_qkv_t], "shard", shard_count, shard_steps[:1])
    qkv_half, grad_proj = lax.optimization_barrier((qkv_half, grad_proj))
    (qkv_own,) = halving(qkv_half, "shard", shard_count, shard_steps[1:])
    grad_qb = jnp.sum(grad_q.astype(jnp.float32), 0)
    grad_vb = jnp.sum(grad_v.astype(jnp.float32), 0)
    grad_normed = jnp.einsum("tc,ic->ti", grad_proj, back_qkv, preferred_element_type=jnp.float32)
    _, norm_pull_one = jax.vjp(normalize, inputs, back_g1.astype(jnp.float32), zero_shift)
    grad_in_part, grad_g1, grad_s1 = norm_pull_one(grad_normed)
    grad_inputs = grad_middle + grad_in_part
    smalls = [grad_g1, grad_s1, grad_qb, grad_vb, grad_bo, grad_g2, grad_s2, grad_bu, grad_bd]
    small_rows = jnp.concatenate([g.reshape(shard_count, -1) for g in smalls], 1)
    small_rows = small_rows.reshape(shard_count, -1, model_width)
    pad_to = small_rows.shape[1] + (-small_rows.shape[1] % reps)
    small_rows = jnp.pad(small_rows, ((0, 0), (0, pad_to - small_rows.shape[1]), (0, 0)))
    small_rows = jnp.concatenate([small_rows[k] for k in order], 0)
    (small_own,) = halving([small_rows], "shard", shard_count, shard_steps)
    total_b = direct_reduce(jnp.concatenate([qkv_own, small_own], 0), "rep", reps)
    total_s = total_b[qkv_rows:]
    total_b = total_b[:qkv_rows]
    up_rows = up_own.shape[0]
    up_fin = total_a[:up_rows].astype(jnp.float32)
    out_fin = total_a[up_rows:].astype(jnp.float32)
    qkv_fin = total_b.astype(jnp.float32).T
    small_flat = total_s.reshape(-1).astype(jnp.float32)
    small_fin, offset = [], 0
    for g in smalls:
        width = g.shape[0] // shard_count
        small_fin.append(small_flat[offset : offset + width])
        offset += width
    g1_fin, s1_fin, qb_fin, vb_fin, bo_fin, g2_fin, s2_fin, bu_fin, bd_fin = small_fin
    return (
        outputs.astype(jnp.bfloat16)[None],
        grad_inputs.astype(jnp.bfloat16)[None],
        g1_fin,
        s1_fin,
        qkv_fin,
        qb_fin,
        vb_fin,
        out_fin,
        bo_fin,
        g2_fin,
        s2_fin,
        up_fin,
        bu_fin,
        down_fin,
        bd_fin,
    )


def solution(mesh):
    return jax.shard_map(
        body_inner,
        mesh=mesh,
        in_specs=(
            P(("rep", "shard"), None, None),
            P(("rep", "shard"), None, None),
            P(("rep", "shard"), None, None),
            P("shard"),
            P("shard"),
            P(None, "shard"),
            P("shard"),
            P("shard"),
            P("shard", None),
            P("shard"),
            P("shard"),
            P("shard"),
            P(None, "shard"),
            P("shard"),
            P("shard", None),
            P("shard"),
        ),
        out_specs=(
            P(("rep", "shard"), None, None),
            P(("rep", "shard"), None, None),
            P("shard"),
            P("shard"),
            P(None, "shard"),
            P("shard"),
            P("shard"),
            P("shard", None),
            P("shard"),
            P("shard"),
            P("shard"),
            P(None, "shard"),
            P("shard"),
            P("shard", None),
            P("shard"),
        ),
        check_vma=False,
    )
```

```python
from functools import partial

import jax
import jax.numpy as jnp
from jax import lax
from jax.sharding import PartitionSpec as P


HEADS = 16
HDIM = 64
PROMPT = 256


def normalize(values, gain, shift):
    center = values - jnp.mean(values, -1, keepdims=True)
    spread = jnp.mean(center * center, -1, keepdims=True)
    return center * lax.rsqrt(spread + 1e-05) * gain + shift


def layout(segments):
    micros, row_count = segments.shape
    same_seg = segments[:, :, None] == segments[:, None, :]
    earlier = jnp.arange(row_count)[None, :] < jnp.arange(row_count)[:, None]
    offsets = jnp.sum(jnp.where(same_seg & earlier[None], 1, 0), -1).astype(jnp.int32)
    cont_pos = PROMPT + offsets
    owners = jnp.arange(micros, dtype=jnp.int32)[:, None] * row_count + segments
    positions = jnp.concatenate([jnp.arange(PROMPT, dtype=jnp.int32), cont_pos.reshape(-1)])
    groups = jnp.concatenate([jnp.full((PROMPT,), -1, jnp.int32), owners.reshape(-1)])
    places = jnp.arange(positions.shape[0], dtype=jnp.int32)
    allowed = (places[None, :] <= places[:, None]) & (
        (places[None, :] < PROMPT) | (groups[None, :] == groups[:, None])
    )
    distance = (positions[:, None] - positions[None, :]).astype(jnp.float32)
    return (distance, allowed)


def head_slice(matrix, block):
    block_width = 4 * HDIM
    part = lax.dynamic_slice_in_dim(matrix, block * block_width, block_width, 1)
    return part.reshape(matrix.shape[0], 4, HDIM)


def block_scores(q_part, k_part, block, distance, allowed):
    heads = (block * 4 + jnp.arange(4, dtype=jnp.int32)).astype(jnp.float32)
    slopes = jnp.exp2(-8.0 * (heads + 1.0) / HEADS)
    scores = jnp.einsum(
        "qhd,khd->hqk", q_part, k_part, preferred_element_type=jnp.float32
    ) * HDIM ** (-0.5)
    scores = scores - slopes[:, None, None] * distance[None]
    return jnp.where(allowed[None], scores, -jnp.inf)


def side_by_side(blocks):
    return jnp.transpose(blocks, (1, 0, 2)).reshape(
        blocks.shape[1], blocks.shape[0] * blocks.shape[2]
    )


def attend_forward(queries, key_rows, values, distance, allowed):
    length = queries.shape[0]

    def head_block(block):
        q_part = head_slice(queries, block)
        k_part = head_slice(key_rows, block)
        v_part = head_slice(values, block)
        scores = block_scores(q_part, k_part, block, distance, allowed)
        peak = jnp.max(scores, -1, keepdims=True)
        exps_rel = jnp.exp(scores - peak)
        row_totals = jnp.sum(exps_rel, -1, keepdims=True)
        attn_probs = (exps_rel / row_totals).astype(jnp.bfloat16)
        mixed = jnp.einsum("hqk,khd->qhd", attn_probs, v_part, preferred_element_type=jnp.float32)
        return (mixed.reshape(length, 4 * HDIM), (peak + jnp.log(row_totals))[:, :, 0])

    mixed, log_norms = lax.map(head_block, jnp.arange(HEADS // 4, dtype=jnp.int32))
    return (side_by_side(mixed).astype(jnp.bfloat16), log_norms)


def attend_backward(queries, key_rows, values, grad_mixed, log_norms, distance, allowed):
    length = queries.shape[0]
    scale = HDIM ** (-0.5)

    def head_block(block):
        q_part = head_slice(queries, block)
        k_part = head_slice(key_rows, block)
        v_part = head_slice(values, block)
        g_part = head_slice(grad_mixed, block)
        scores = block_scores(q_part, k_part, block, distance, allowed)
        attn_probs = jnp.exp(scores - log_norms[block][:, :, None])
        grad_probs = jnp.einsum("qhd,khd->hqk", g_part, v_part, preferred_element_type=jnp.float32)
        inner = jnp.sum(attn_probs * grad_probs, -1, keepdims=True)
        grad_scores = (attn_probs * (grad_probs - inner)).astype(jnp.bfloat16)
        grad_q = (
            jnp.einsum("hqk,khd->qhd", grad_scores, k_part, preferred_element_type=jnp.float32)
            * scale
        )
        grad_k = (
            jnp.einsum("hqk,qhd->khd", grad_scores, q_part, preferred_element_type=jnp.float32)
            * scale
        )
        grad_v = jnp.einsum(
            "hqk,qhd->khd",
            attn_probs.astype(jnp.bfloat16),
            g_part,
            preferred_element_type=jnp.float32,
        )
        block_width = 4 * HDIM
        return (
            grad_q.reshape(length, block_width),
            grad_k.reshape(length, block_width),
            grad_v.reshape(length, block_width),
        )

    grad_q, grad_k, grad_v = lax.map(head_block, jnp.arange(HEADS // 4, dtype=jnp.int32))
    return (
        side_by_side(grad_q).astype(jnp.bfloat16),
        side_by_side(grad_k).astype(jnp.bfloat16),
        side_by_side(grad_v).astype(jnp.bfloat16),
    )


def bit_steps(size):
    assert size & (size - 1) == 0
    return [1 << b for b in range(size.bit_length() - 1)]


def chunk_order(size, steps):
    places = []
    for member in range(size):
        place = 0
        for step in steps:
            place = place * 2 + (member // step) % 2
        places.append(place)
    order = [0] * size
    for member, place in enumerate(places):
        order[place] = member
    return order


def reorder_cols(matrix, order):
    pieces = jnp.split(matrix, len(order), 1)
    return jnp.concatenate([pieces[k] for k in order], 1)


def halving(arrays, axis, size, steps):
    index = lax.axis_index(axis)
    for step in steps:
        bit = (index // step) % 2
        keeps, sends = [], []
        for array in arrays:
            pair = array.reshape(2, array.shape[0] // 2, *array.shape[1:])
            keeps.append(lax.dynamic_index_in_dim(pair, bit, 0, keepdims=False))
            sends.append(
                lax.dynamic_index_in_dim(pair, 1 - bit, 0, keepdims=False).astype(jnp.bfloat16)
            )
        got = lax.ppermute(jnp.concatenate(sends, 0), axis, [(a, a ^ step) for a in range(size)])
        arrays, offset = [], 0
        for keep in keeps:
            arrays.append(keep + got[offset : offset + keep.shape[0]].astype(jnp.float32))
            offset += keep.shape[0]
    return arrays


def direct_reduce(buf, axis, size):
    index = lax.axis_index(axis)
    chunks = buf.reshape(size, buf.shape[0] // size, *buf.shape[1:])
    total = lax.dynamic_index_in_dim(chunks, index, 0, keepdims=False)
    for shift in range(1, size):
        partner = lax.bitwise_xor(index, shift)
        send = lax.dynamic_index_in_dim(chunks, partner, 0, keepdims=False)
        got = lax.ppermute(send.astype(jnp.bfloat16), axis, [(a, a ^ shift) for a in range(size)])
        total = total + got.astype(jnp.float32)
    mine = total.astype(jnp.bfloat16)
    result = jnp.zeros((size, *mine.shape), jnp.bfloat16)
    result = lax.dynamic_update_index_in_dim(result, mine, index, 0)
    for shift in range(1, size):
        got = lax.ppermute(mine, axis, [(a, a ^ shift) for a in range(size)])
        result = lax.dynamic_update_index_in_dim(result, got, lax.bitwise_xor(index, shift), 0)
    return result.reshape(buf.shape)


def gather_small(pieces):
    packed = jnp.concatenate(pieces)
    shards = lax.all_gather(packed, "shard", axis=0, tiled=False)
    fulls, offset = [], 0
    for piece in pieces:
        width = piece.shape[0]
        fulls.append(shards[:, offset : offset + width].reshape(-1))
        offset += width
    return fulls


def body_inner(
    tokens,
    cont_segment,
    cotangent,
    ln1_gain,
    ln1_bias,
    w_qkv,
    q_bias,
    v_bias,
    w_out,
    b_out,
    ln2_gain,
    ln2_bias,
    w_up,
    b_up,
    w_down,
    b_down,
):
    shard_count = lax.psum(1, "shard")
    full_g1, full_s1, full_qb, full_vb, full_bo, full_g2, full_s2, full_bu, full_bd = gather_small(
        [ln1_gain, ln1_bias, q_bias, v_bias, b_out, ln2_gain, ln2_bias, b_up, b_down]
    )
    full_qkv = lax.all_gather(w_qkv, "shard", axis=1, tiled=True)
    full_out = lax.all_gather(w_out, "shard", axis=0, tiled=True)
    full_up = lax.all_gather(w_up, "shard", axis=1, tiled=True)
    full_down = lax.all_gather(w_down, "shard", axis=0, tiled=True)
    inputs = tokens[0].astype(jnp.float32)
    _, model_width = inputs.shape
    distance, allowed = layout(cont_segment[0])
    normed = normalize(inputs, full_g1.astype(jnp.float32), full_s1.astype(jnp.float32)).astype(
        jnp.bfloat16
    )
    projected = jnp.dot(normed, full_qkv, preferred_element_type=jnp.float32)
    queries = (projected[:, :model_width] + full_qb.astype(jnp.float32)).astype(jnp.bfloat16)
    key_rows = projected[:, model_width : 2 * model_width].astype(jnp.bfloat16)
    values = (projected[:, 2 * model_width :] + full_vb.astype(jnp.float32)).astype(jnp.bfloat16)
    mixed, log_norms = attend_forward(queries, key_rows, values, distance, allowed)
    branch = jnp.dot(mixed, full_out, preferred_element_type=jnp.float32) + full_bo.astype(
        jnp.float32
    )
    middle = inputs + branch
    normed_two = normalize(middle, full_g2.astype(jnp.float32), full_s2.astype(jnp.float32)).astype(
        jnp.bfloat16
    )
    pre_act = jnp.dot(normed_two, full_up, preferred_element_type=jnp.float32) + full_bu.astype(
        jnp.float32
    )
    activated = jax.nn.gelu(pre_act, approximate=True).astype(jnp.bfloat16)
    cot_low = cotangent[0]
    shard_steps = bit_steps(shard_count)
    order = chunk_order(shard_count, shard_steps)
    grad_down = jnp.einsum(
        "tf,to->fo", reorder_cols(activated, order), cot_low, preferred_element_type=jnp.float32
    )
    down_half = halving([grad_down], "shard", shard_count, shard_steps[:1])
    down_half, full_down = lax.optimization_barrier((down_half, full_down))
    outputs = middle + (
        jnp.dot(activated, full_down, preferred_element_type=jnp.float32)
        + full_bd.astype(jnp.float32)
    )
    back_g1, back_qkv, back_out, back_g2, back_up, back_down = (
        full_g1, full_qkv, full_out, full_g2, full_up, full_down
    )
    cot_full = cot_low.astype(jnp.float32)
    zero_shift = jnp.zeros((model_width,), jnp.float32)
    grad_bd = jnp.sum(cot_full, 0)
    grad_act = jnp.einsum("to,fo->tf", cot_low, back_down, preferred_element_type=jnp.float32)
    _, gelu_pull = jax.vjp(partial(jax.nn.gelu, approximate=True), pre_act)
    grad_pre = gelu_pull(grad_act)[0].astype(jnp.bfloat16)
    grad_bu = jnp.sum(grad_pre.astype(jnp.float32), 0)
    (down_own,) = halving(down_half, "shard", shard_count, shard_steps[1:])
    total_a1 = lax.psum(down_own.astype(jnp.bfloat16), "rep")
    grad_up_t = jnp.einsum(
        "tf,ti->fi", reorder_cols(grad_pre, order), normed_two, preferred_element_type=jnp.float32
    )
    grad_normed_two = jnp.einsum("tf,if->ti", grad_pre, back_up, preferred_element_type=jnp.float32)
    _, norm_pull_two = jax.vjp(normalize, middle, back_g2.astype(jnp.float32), zero_shift)
    grad_mid_part, grad_g2, grad_s2 = norm_pull_two(grad_normed_two)
    grad_middle = cot_full + grad_mid_part
    grad_branch = grad_middle.astype(jnp.bfloat16)
    grad_bo = jnp.sum(grad_branch.astype(jnp.float32), 0)
    grad_mixed = jnp.einsum(
        "to,io->ti", grad_branch, back_out, preferred_element_type=jnp.float32
    ).astype(jnp.bfloat16)
    grad_out = jnp.einsum(
        "ti,to->io", reorder_cols(mixed, order), grad_branch, preferred_element_type=jnp.float32
    )
    up_own, out_own = halving([grad_up_t, grad_out], "shard", shard_count, shard_steps)
    owned_a = [up_own.astype(jnp.bfloat16).T, out_own.astype(jnp.bfloat16)]
    joined_a = jnp.concatenate(owned_a, 0)
    down_fin, joined_a = lax.optimization_barrier((total_a1.astype(jnp.float32), joined_a))
    total_a = lax.psum(joined_a, "rep")
    grad_q, grad_k, grad_v = attend_backward(
        queries, key_rows, values, grad_mixed, log_norms, distance, allowed
    )
    grad_proj = jnp.concatenate([grad_q, grad_k, grad_v], 1)
    reps = lax.psum(1, "rep")
    grad_qkv_t = jnp.einsum(
        "tc,ti->ci", reorder_cols(grad_proj, order), normed, preferred_element_type=jnp.float32
    )
    qkv_rows = grad_qkv_t.shape[0] // shard_count
    qkv_half = halving([grad_qkv_t], "shard", shard_count, shard_steps[:1])
    qkv_half, grad_proj = lax.optimization_barrier((qkv_half, grad_proj))
    grad_qb = jnp.sum(grad_q.astype(jnp.float32), 0)
    grad_vb = jnp.sum(grad_v.astype(jnp.float32), 0)
    grad_normed = jnp.einsum("tc,ic->ti", grad_proj, back_qkv, preferred_element_type=jnp.float32)
    _, norm_pull_one = jax.vjp(normalize, inputs, back_g1.astype(jnp.float32), zero_shift)
    grad_in_part, grad_g1, grad_s1 = norm_pull_one(grad_normed)
    grad_inputs = grad_middle + grad_in_part
    smalls = [grad_g1, grad_s1, grad_qb, grad_vb, grad_bo, grad_g2, grad_s2, grad_bu, grad_bd]
    small_rows = jnp.concatenate([g.reshape(shard_count, -1) for g in smalls], 1)
    small_rows = small_rows.reshape(shard_count, -1, model_width)
    pad_to = small_rows.shape[1] + (-small_rows.shape[1] % reps)
    small_rows = jnp.pad(small_rows, ((0, 0), (0, pad_to - small_rows.shape[1]), (0, 0)))
    small_rows = jnp.concatenate([small_rows[k] for k in order], 0)
    small_half = halving([small_rows], "shard", shard_count, shard_steps[:1])
    qkv_own, small_own = halving(qkv_half + small_half, "shard", shard_count, shard_steps[1:])
    total_b = direct_reduce(jnp.concatenate([qkv_own, small_own], 0), "rep", reps)
    total_s = total_b[qkv_rows:]
    total_b = total_b[:qkv_rows]
    up_rows = up_own.shape[0]
    up_fin = total_a[:up_rows].astype(jnp.float32)
    out_fin = total_a[up_rows:].astype(jnp.float32)
    qkv_fin = total_b.astype(jnp.float32).T
    small_flat = total_s.reshape(-1).astype(jnp.float32)
    small_fin, offset = [], 0
    for g in smalls:
        width = g.shape[0] // shard_count
        small_fin.append(small_flat[offset : offset + width])
        offset += width
    g1_fin, s1_fin, qb_fin, vb_fin, bo_fin, g2_fin, s2_fin, bu_fin, bd_fin = small_fin
    return (
        outputs.astype(jnp.bfloat16)[None],
        grad_inputs.astype(jnp.bfloat16)[None],
        g1_fin,
        s1_fin,
        qkv_fin,
        qb_fin,
        vb_fin,
        out_fin,
        bo_fin,
        g2_fin,
        s2_fin,
        up_fin,
        bu_fin,
        down_fin,
        bd_fin,
    )


def solution(mesh):
    return jax.shard_map(
        body_inner,
        mesh=mesh,
        in_specs=(
            P(("rep", "shard"), None, None),
            P(("rep", "shard"), None, None),
            P(("rep", "shard"), None, None),
            P("shard"),
            P("shard"),
            P(None, "shard"),
            P("shard"),
            P("shard"),
            P("shard", None),
            P("shard"),
            P("shard"),
            P("shard"),
            P(None, "shard"),
            P("shard"),
            P("shard", None),
            P("shard"),
        ),
        out_specs=(
            P(("rep", "shard"), None, None),
            P(("rep", "shard"), None, None),
            P("shard"),
            P("shard"),
            P(None, "shard"),
            P("shard"),
            P("shard"),
            P("shard", None),
            P("shard"),
            P("shard"),
            P("shard"),
            P(None, "shard"),
            P("shard"),
            P("shard", None),
            P("shard"),
        ),
        check_vma=False,
    )
```
